32 devices in a mesh: group: 4 (over y, core), tile: 8 (over z, x).
Axes of the slice: x: 2, y: 2, z: 4, core: 2. Of those that a mesh axis runs over, the one named last changes fastest.
Arguments:
- maps: bfloat16 [32, 256, 128, 128], P('group', 'tile'), may hold values from -6 to 6
- first_weight: bfloat16 [3, 3, 128, 256], replicated, may hold values from -0.1875 to 0.1875
- second_weight: bfloat16 [3, 3, 256, 256], replicated, may hold values from -0.125 to 0.125
- out_grad: bfloat16 [32, 128, 64, 256], P(('group', 'tile')), may hold values from -0.0234375 to 0.0234375
Outputs:
- conv_out: bfloat16 [32, 128, 64, 256], P(('group', 'tile'))
- weight_grad: float32 [256, 3, 3, 256], P(('group', 'tile'))
The draws below stay inside these ranges and needn't reach their ends.
All inputs are finite; a program needn't handle non-finite values.
Results may differ from the reference program's by a relative error of at most 0.0051.
Values may be sent and summed in bfloat16 or wider, within the bound.
No kernel may reach another device: no remote copies, remote signals or barrier semaphores. Data moves between devices by JAX's collectives and lax.ppermute only.
A program may use at most 192 MiB of HBM per device.

```python
import jax
import jax.numpy as jnp
from jax import lax

C1 = 128
C2 = 256
H = 256
W = 128
IMAGES = 32


def with_spikes(values, stream_key, source, target, parts, factor):
    def block_of(position):
        return (jnp.arange(values.shape[position]) // (values.shape[position] // parts)).reshape((-1,) + (1,) * (values.ndim - 1 - position))

    first = jax.random.permutation(stream_key, parts)[block_of(target)]
    second = (block_of(target) + parts // 2) % parts
    return jnp.where((block_of(source) == first) | (block_of(source) == second), factor * values, values)


def shard_levels(rng, dims, cuts, least, largest):
    loudness = 1.0
    for position, blocks in cuts:
        steps = jax.random.uniform(jax.random.fold_in(jax.random.fold_in(rng, 6), position), (blocks,), jnp.float32, least / len(cuts), largest / len(cuts))
        loudness = loudness * jnp.repeat(jnp.exp(steps), dims[position] // blocks).reshape((-1,) + (1,) * (len(dims) - 1 - position))
    return loudness


def bell_draw(key, extent, spread, bound, cuts=(), held_as=jnp.bfloat16):
    values = spread * jax.random.normal(key, extent, jnp.float32)
    if cuts:
        values = values * shard_levels(key, extent, cuts, -0.22, 0.18)
    return jnp.clip(values, -bound, bound).astype(held_as)


def gaussian_with(stream_key, dims, scale, most, split, heavy, kind=jnp.bfloat16):
    drawn = scale * jax.random.normal(stream_key, dims, jnp.float32)
    if split:
        drawn = drawn * shard_levels(stream_key, dims, split, -0.22, 0.18)
    return jnp.clip(with_spikes(drawn, jax.random.fold_in(stream_key, 3), *heavy), -most, most).astype(kind)


def setup_inputs(seed: int = 0) -> dict:
    arg_keys = jax.random.split(jax.random.key(seed), 5)
    maps = bell_draw(arg_keys[0], (IMAGES, H, W, C1), 1.0, 6.0, ((0, 4), (1, 8)))
    first_weight = bell_draw(arg_keys[1], (3, 3, C1, C2), (9 * C1) ** -0.5, 0.1875)
    second_weight = bell_draw(arg_keys[2], (3, 3, C2, C2), (9 * C2) ** -0.5, 0.125)
    out_grad = gaussian_with(arg_keys[3], (IMAGES, H // 2, W // 2, C2), (IMAGES * H * W // 4) ** -0.5, 0.0234375, ((0, 32),), (0, 3, 32, 2.75))
    return {"maps": maps, "first_weight": first_weight, "second_weight": second_weight, "out_grad": out_grad}


def stride_patches(padded):
    height = padded.shape[0] - 1
    width = padded.shape[1] - 1
    pieces = [padded[tap_row:tap_row + height - 1:2, tap_col:tap_col + width - 1:2, :] for tap_row in range(3) for tap_col in range(3)]
    return jnp.concatenate(pieces, axis=-1)


def plain_patches(padded):
    height = padded.shape[0] - 2
    width = padded.shape[1] - 2
    pieces = [padded[tap_row:tap_row + height, tap_col:tap_col + width, :] for tap_row in range(3) for tap_col in range(3)]
    return jnp.concatenate(pieces, axis=-1)


def reference(maps, first_weight, second_weight, out_grad):
    kernel_one = first_weight.reshape(9 * C1, C2)
    kernel_two = second_weight.reshape(9 * C2, C2)

    def one_image(total, pair):
        image, gradient = pair
        padded = jnp.pad(image, ((1, 0), (1, 0), (0, 0)))
        pre = jnp.dot(stride_patches(padded).reshape(-1, 9 * C1), kernel_one, preferred_element_type=jnp.float32)
        hidden = jnp.maximum(pre, 0.0).astype(jnp.bfloat16).reshape(H // 2, W // 2, C2)
        columns = plain_patches(jnp.pad(hidden, ((1, 1), (1, 1), (0, 0)))).reshape(-1, 9 * C2)
        result = jnp.dot(columns, kernel_two, preferred_element_type=jnp.float32).astype(jnp.bfloat16)
        term = lax.dot_general(gradient.reshape(-1, C2), columns, (((0,), (0,)), ((), ())), preferred_element_type=jnp.float32)
        return total + term, result.reshape(H // 2, W // 2, C2)

    total, results = lax.scan(one_image, jnp.zeros((C2, 9 * C2), jnp.float32), (maps, out_grad))
    return results, total.reshape(C2, 3, 3, C2)
```

```python
import functools

import jax
import jax.numpy as jnp
from jax import lax
from jax.experimental import pallas as pl
from jax.experimental.pallas import tpu as pltpu
from jax.sharding import PartitionSpec as P


def shifted_2(shard, axis, by):
    length = lax.axis_size(axis)
    pairs = [(i, i + by) for i in range(length) if 0 <= i + by < length]
    return lax.ppermute(shard, axis, pairs)


def shift_cols_right(slab):
    zero_col = jnp.zeros_like(slab[:, :, :1])
    return jnp.concatenate([zero_col, slab[:, :, :-1]], axis=2)


def shift_cols_left(slab):
    zero_col = jnp.zeros_like(slab[:, :, :1])
    return jnp.concatenate([slab[:, :, 1:], zero_col], axis=2)


def first_conv(source, upper_row, first_weight):
    images, rows, width, inputs = source.shape
    outputs = first_weight.shape[3]
    paired = source.reshape(images, rows // 2, 2, width // 2, 2 * inputs)
    even_rows = paired[:, :, 0]
    odd_rows = paired[:, :, 1]
    upper_paired = upper_row.reshape(images, 1, width // 2, 2 * inputs)
    odd_above = jnp.concatenate([upper_paired, odd_rows[:, :-1]], axis=1)
    sources = [odd_above, even_rows, odd_rows]
    total = jnp.zeros((images, rows // 2, width // 2, outputs), jnp.float32)
    for tap_row in range(3):
        wide_kernel = first_weight[tap_row, 1:3].reshape(2 * inputs, outputs)
        total = total + jnp.dot(sources[tap_row], wide_kernel, preferred_element_type=jnp.float32)
    halves = jnp.concatenate([piece[..., inputs:] for piece in sources], axis=-1)
    narrow_kernel = first_weight[:, 0].reshape(3 * inputs, outputs)
    total = total + jnp.dot(
        shift_cols_right(halves), narrow_kernel, preferred_element_type=jnp.float32
    )
    return jnp.maximum(total, 0.0).astype(jnp.bfloat16)


def second_kernel(left_ref, mid_ref, right_ref, weight_ref, grad_ref, out_ref, wgrad_ref, *, rows):
    step = pl.program_id(1)
    _, width, channels = out_ref.shape

    @pl.when(step == 0)
    def _():
        wgrad_ref[...] = jnp.zeros_like(wgrad_ref)

    grad_t = grad_ref[...]
    acc = jnp.zeros((rows * width, channels), jnp.float32)
    for tap_row in range(3):
        for tap_col, src in enumerate((left_ref, mid_ref, right_ref)):
            window = src[pl.ds(step * rows + tap_row, rows)].reshape(rows * width, channels)
            acc = acc + jnp.dot(window, weight_ref[tap_row, tap_col], preferred_element_type=jnp.float32)
            tap = tap_row * 3 + tap_col
            wgrad_ref[:, tap * channels:(tap + 1) * channels] += jnp.dot(
                grad_t, window, preferred_element_type=jnp.float32
            )
    out_ref[...] = acc.astype(out_ref.dtype).reshape(rows, width, channels)


def second_stage(hidden, second_weight, out_grad):
    owned, out_rows, out_cols, channels = hidden.shape
    rows = min(16, out_rows)
    row_padded = jnp.pad(hidden, ((0, 0), (1, 1), (0, 0), (0, 0)))
    shifted = [shift_cols_right(row_padded), row_padded, shift_cols_left(row_padded)]
    grad_t = out_grad.reshape(owned, out_rows * out_cols, channels).transpose(0, 2, 1)
    full = pl.BlockSpec((None, out_rows + 2, out_cols, channels), lambda n, i: (n, 0, 0, 0))
    flops = 4 * owned * out_rows * out_cols * 9 * channels * channels
    conv_out, wgrad = pl.pallas_call(
        functools.partial(second_kernel, rows=rows),
        grid=(owned, out_rows // rows),
        in_specs=[
            full,
            full,
            full,
            pl.BlockSpec((3, 3, channels, channels), lambda n, i: (0, 0, 0, 0)),
            pl.BlockSpec((None, channels, rows * out_cols), lambda n, i: (n, 0, i)),
        ],
        out_specs=[
            pl.BlockSpec((None, rows, out_cols, channels), lambda n, i: (n, i, 0, 0)),
            pl.BlockSpec((None, channels, 9 * channels), lambda n, i: (n, 0, 0)),
        ],
        out_shape=[
            jax.ShapeDtypeStruct(hidden.shape, jnp.bfloat16),
            jax.ShapeDtypeStruct((owned, channels, 9 * channels), jnp.float32),
        ],
        compiler_params=pltpu.CompilerParams(
            dimension_semantics=("arbitrary", "arbitrary"), vmem_limit_bytes=60 * 1024 * 1024
        ),
        cost_estimate=pl.CostEstimate(
            flops=flops, transcendentals=0, bytes_accessed=hidden.size * 2 * 5 + wgrad_bytes(owned, channels)
        ),
    )(*shifted, second_weight, grad_t)
    return conv_out, wgrad.sum(axis=0)


def wgrad_bytes(owned, channels):
    return owned * channels * 9 * channels * 4


def halving_reduce_scatter(partial, axes):
    devices = lax.axis_size(axes)
    tiles = lax.axis_size(axes[-1])
    bits = devices.bit_length() - 1
    me = lax.axis_index(axes)
    order = [tiles.bit_length() - 1] + [b for b in range(bits) if b != tiles.bit_length() - 1]
    rows = partial.shape[0] // devices
    buf = partial.reshape((2,) * bits + (rows,) + partial.shape[1:])
    remaining = list(range(bits - 1, -1, -1))
    for bit in order:
        axis = remaining.index(bit)
        mine = (me >> bit) & 1
        keep = lax.dynamic_index_in_dim(buf, mine, axis=axis, keepdims=False)
        send = lax.dynamic_index_in_dim(buf, 1 - mine, axis=axis, keepdims=False)
        pairs = [(i, i ^ (1 << bit)) for i in range(devices)]
        buf = keep + lax.ppermute(send, axes, pairs)
        remaining.pop(axis)
    return buf


def local(maps, first_weight, second_weight, out_grad):
    tiles = lax.axis_size("tile")
    images, height, width, inputs = maps.shape
    outputs = first_weight.shape[3]
    owned = images // tiles
    upper_row = shifted_2(maps[:, height - 1 : height], "tile", 1)
    local_hidden = first_conv(maps, upper_row, first_weight)
    half_rows = height // 2
    arrived = lax.all_to_all(
        local_hidden.reshape(tiles, owned, half_rows, width // 2, outputs),
        "tile",
        split_axis=0,
        concat_axis=2,
        tiled=True,
    )
    hidden = arrived.reshape(owned, half_rows * tiles, width // 2, outputs)
    conv_out, partial = second_stage(hidden, second_weight, out_grad)
    summed = halving_reduce_scatter(partial, ("group", "tile"))
    weight_grad = summed.reshape(-1, 3, 3, outputs)
    return (conv_out, weight_grad)


def solution(mesh):
    return jax.shard_map(
        local,
        mesh=mesh,
        in_specs=(P("group", "tile", None, None), P(), P(), P(("group", "tile"), None, None, None)),
        out_specs=(P(("group", "tile"), None, None, None), P(("group", "tile"), None, None, None)),
        check_vma=False,
    )
```

```python
import functools

import jax
import jax.numpy as jnp
from jax import lax
from jax.experimental import pallas as pl
from jax.experimental.pallas import tpu as pltpu
from jax.sharding import PartitionSpec as P


def shifted_2(shard, axis, by):
    length = lax.axis_size(axis)
    pairs = [(i, i + by) for i in range(length) if 0 <= i + by < length]
    return lax.ppermute(shard, axis, pairs)


def shift_cols_right(slab):
    zero_col = jnp.zeros_like(slab[:, :, :1])
    return jnp.concatenate([zero_col, slab[:, :, :-1]], axis=2)


def shift_cols_left(slab):
    zero_col = jnp.zeros_like(slab[:, :, :1])
    return jnp.concatenate([slab[:, :, 1:], zero_col], axis=2)


def first_conv(source, upper_row, first_weight):
    images, rows, width, inputs = source.shape
    outputs = first_weight.shape[3]
    paired = source.reshape(images, rows // 2, 2, width // 2, 2 * inputs)
    even_rows = paired[:, :, 0]
    odd_rows = paired[:, :, 1]
    upper_paired = upper_row.reshape(images, 1, width // 2, 2 * inputs)
    odd_above = jnp.concatenate([upper_paired, odd_rows[:, :-1]], axis=1)
    sources = [odd_above, even_rows, odd_rows]
    total = jnp.zeros((images, rows // 2, width // 2, outputs), jnp.float32)
    for tap_row in range(3):
        wide_kernel = first_weight[tap_row, 1:3].reshape(2 * inputs, outputs)
        total = total + jnp.dot(sources[tap_row], wide_kernel, preferred_element_type=jnp.float32)
    halves = jnp.concatenate([piece[..., inputs:] for piece in sources], axis=-1)
    narrow_kernel = first_weight[:, 0].reshape(3 * inputs, outputs)
    total = total + jnp.dot(
        shift_cols_right(halves), narrow_kernel, preferred_element_type=jnp.float32
    )
    return jnp.maximum(total, 0.0).astype(jnp.bfloat16)


def second_kernel(*refs, rows, carry):
    if carry:
        left_ref, mid_ref, right_ref, weight_ref, grad_ref, prev_ref, out_ref, wgrad_ref = refs
    else:
        left_ref, mid_ref, right_ref, weight_ref, grad_ref, out_ref, wgrad_ref = refs
    step = pl.program_id(1)
    _, width, outputs = out_ref.shape
    inputs = mid_ref.shape[-1]
    grad_t = grad_ref[...]
    if carry:
        acc = prev_ref[...].reshape(rows * width, outputs)
    else:
        acc = jnp.zeros((rows * width, outputs), jnp.float32)
    for tap_row in range(3):
        for tap_col, src in enumerate((left_ref, mid_ref, right_ref)):
            window = src[pl.ds(step * rows + tap_row, rows)].reshape(rows * width, inputs)
            acc = acc + jnp.dot(window, weight_ref[tap_row, tap_col], preferred_element_type=jnp.float32)
            term = jnp.dot(grad_t, window, preferred_element_type=jnp.float32)
            tap = tap_row * 3 + tap_col

            @pl.when(step == 0)
            def _():
                wgrad_ref[:, tap * inputs:(tap + 1) * inputs] = term

            @pl.when(step > 0)
            def _():
                wgrad_ref[:, tap * inputs:(tap + 1) * inputs] += term

    out_ref[...] = acc.astype(out_ref.dtype).reshape(rows, width, outputs)


def second_stage(hidden, weight, grad_t, prev, out_dtype):
    owned, out_rows, out_cols, inputs = hidden.shape
    outputs = weight.shape[-1]
    rows = min(16, out_rows)
    row_padded = jnp.pad(hidden, ((0, 0), (1, 1), (0, 0), (0, 0)))
    shifted = [shift_cols_right(row_padded), row_padded, shift_cols_left(row_padded)]
    full = pl.BlockSpec((None, out_rows + 2, out_cols, inputs), lambda n, i: (n, 0, 0, 0))
    block = pl.BlockSpec((None, rows, out_cols, outputs), lambda n, i: (n, i, 0, 0))
    in_specs = [
        full,
        full,
        full,
        pl.BlockSpec((3, 3, inputs, outputs), lambda n, i: (0, 0, 0, 0)),
        pl.BlockSpec((None, outputs, rows * out_cols), lambda n, i: (n, 0, i)),
    ]
    operands = [*shifted, weight, grad_t]
    if prev is not None:
        in_specs.append(block)
        operands.append(prev)
    flops = 4 * owned * out_rows * out_cols * 9 * inputs * outputs
    return pl.pallas_call(
        functools.partial(second_kernel, rows=rows, carry=prev is not None),
        grid=(owned, out_rows // rows),
        in_specs=in_specs,
        out_specs=[block, pl.BlockSpec((None, outputs, 9 * inputs), lambda n, i: (n, 0, 0))],
        out_shape=[
            jax.ShapeDtypeStruct((owned, out_rows, out_cols, outputs), out_dtype),
            jax.ShapeDtypeStruct((owned, outputs, 9 * inputs), jnp.float32),
        ],
        compiler_params=pltpu.CompilerParams(
            dimension_semantics=("arbitrary", "arbitrary"), vmem_limit_bytes=60 * 1024 * 1024
        ),
        cost_estimate=pl.CostEstimate(
            flops=flops,
            transcendentals=0,
            bytes_accessed=hidden.size * 2 * 4 + owned * out_rows * out_cols * outputs * 8
            + owned * outputs * 9 * inputs * 4,
        ),
    )(*operands)


def halving_reduce_scatter(partial, axes):
    devices = lax.axis_size(axes)
    tiles = lax.axis_size(axes[-1])
    bits = devices.bit_length() - 1
    me = lax.axis_index(axes)
    core = tiles.bit_length() - 1
    order = [core] + [b for b in range(bits) if b > core] + [b for b in range(core)]
    rows = partial.shape[0] // devices
    buf = partial.reshape((2,) * bits + (rows,) + partial.shape[1:])
    remaining = list(range(bits - 1, -1, -1))
    for bit in order:
        axis = remaining.index(bit)
        mine = (me >> bit) & 1
        keep = lax.dynamic_index_in_dim(buf, mine, axis=axis, keepdims=False)
        send = lax.dynamic_index_in_dim(buf, 1 - mine, axis=axis, keepdims=False)
        pairs = [(i, i ^ (1 << bit)) for i in range(devices)]
        buf = keep + lax.ppermute(send, axes, pairs)
        remaining.pop(axis)
    return buf


def local(maps, first_weight, second_weight, out_grad):
    tiles = lax.axis_size("tile")
    images, height, width, inputs = maps.shape
    outputs = first_weight.shape[3]
    owned = images // tiles
    half_rows = height // 2
    chunks = 2 if outputs % 256 == 0 else 1
    part = outputs // chunks
    upper_row = shifted_2(maps[:, height - 1 : height], "tile", 1)
    grad_t = out_grad.reshape(owned, -1, outputs).transpose(0, 2, 1)
    conv = None
    pieces = []
    for chunk in range(chunks):
        channels = slice(chunk * part, (chunk + 1) * part)
        local_hidden = first_conv(maps, upper_row, first_weight[..., channels])
        arrived = lax.all_to_all(
            local_hidden.reshape(tiles, owned, half_rows, width // 2, part),
            "tile",
            split_axis=0,
            concat_axis=2,
            tiled=True,
        )
        if conv is not None:
            arrived, conv = lax.optimization_barrier((arrived, conv))
        hidden = arrived.reshape(owned, half_rows * tiles, width // 2, part)
        last = chunk == chunks - 1
        conv, partial = second_stage(
            hidden, second_weight[:, :, channels], grad_t, conv, jnp.bfloat16 if last else jnp.float32
        )
        summed = halving_reduce_scatter(partial.sum(axis=0).reshape(outputs, 9 * part), ("group", "tile"))
        pieces.append(summed.reshape(-1, 9, part))
    weight_grad = jnp.concatenate(pieces, axis=-1).reshape(-1, 3, 3, outputs)
    return (conv, weight_grad)


def solution(mesh):
    return jax.shard_map(
        local,
        mesh=mesh,
        in_specs=(P("group", "tile", None, None), P(), P(), P(("group", "tile"), None, None, None)),
        out_specs=(P(("group", "tile"), None, None, None), P(("group", "tile"), None, None, None)),
        check_vma=False,
    )
```

```python
import functools

import jax
import jax.numpy as jnp
from jax import lax
from jax.experimental import pallas as pl
from jax.experimental.pallas import tpu as pltpu
from jax.sharding import PartitionSpec as P


def shifted_2(shard, axis, by):
    length = lax.axis_size(axis)
    pairs = [(i, i + by) for i in range(length) if 0 <= i + by < length]
    return lax.ppermute(shard, axis, pairs)


def shift_cols_right(slab):
    zero_col = jnp.zeros_like(slab[:, :, :1])
    return jnp.concatenate([zero_col, slab[:, :, :-1]], axis=2)


def shift_cols_left(slab):
    zero_col = jnp.zeros_like(slab[:, :, :1])
    return jnp.concatenate([slab[:, :, 1:], zero_col], axis=2)


def first_conv(source, upper_row, first_weight):
    images, rows, width, inputs = source.shape
    outputs = first_weight.shape[3]
    paired = source.reshape(images, rows // 2, 2, width // 2, 2 * inputs)
    even_rows = paired[:, :, 0]
    odd_rows = paired[:, :, 1]
    upper_paired = upper_row.reshape(images, 1, width // 2, 2 * inputs)
    odd_above = jnp.concatenate([upper_paired, odd_rows[:, :-1]], axis=1)
    sources = [odd_above, even_rows, odd_rows]
    total = jnp.zeros((images, rows // 2, width // 2, outputs), jnp.float32)
    for tap_row in range(3):
        wide_kernel = first_weight[tap_row, 1:3].reshape(2 * inputs, outputs)
        total = total + jnp.dot(sources[tap_row], wide_kernel, preferred_element_type=jnp.float32)
    halves = jnp.concatenate([piece[..., inputs:] for piece in sources], axis=-1)
    narrow_kernel = first_weight[:, 0].reshape(3 * inputs, outputs)
    total = total + jnp.dot(
        shift_cols_right(halves), narrow_kernel, preferred_element_type=jnp.float32
    )
    return jnp.maximum(total, 0.0).astype(jnp.bfloat16)


def second_kernel(*refs, rows, carry, group):
    if carry:
        left_ref, mid_ref, right_ref, weight_ref, grad_ref, prev_ref, out_ref, wgrad_ref = refs
    else:
        left_ref, mid_ref, right_ref, weight_ref, grad_ref, out_ref, wgrad_ref = refs
    step = pl.program_id(1)
    _, width, outputs = out_ref.shape
    inputs = mid_ref.shape[-1]
    sources = (left_ref, mid_ref, right_ref)
    grad_t = grad_ref[...]
    if carry:
        acc = prev_ref[...].reshape(rows * width, outputs)
    else:
        acc = jnp.zeros((rows * width, outputs), jnp.float32)
    for first in range(0, 9, group):
        taps = range(first, min(first + group, 9))
        windows = [
            sources[tap % 3][pl.ds(step * rows + tap // 3, rows)].reshape(rows * width, inputs)
            for tap in taps
        ]
        window = windows[0] if len(windows) == 1 else jnp.concatenate(windows, axis=-1)
        lanes = slice(first * inputs, (first + len(windows)) * inputs)
        acc = acc + jnp.dot(window, weight_ref[lanes, :], preferred_element_type=jnp.float32)
        term = jnp.dot(grad_t, window, preferred_element_type=jnp.float32)

        @pl.when(step == 0)
        def _():
            wgrad_ref[:, lanes] = term

        @pl.when(step > 0)
        def _():
            wgrad_ref[:, lanes] += term

    out_ref[...] = acc.astype(out_ref.dtype).reshape(rows, width, outputs)


def second_stage(hidden, weight, grad_t, prev, out_dtype):
    owned, out_rows, out_cols, inputs = hidden.shape
    outputs = weight.shape[-1]
    rows = min(16, out_rows)
    row_padded = jnp.pad(hidden, ((0, 0), (1, 1), (0, 0), (0, 0)))
    shifted = [shift_cols_right(row_padded), row_padded, shift_cols_left(row_padded)]
    full = pl.BlockSpec((None, out_rows + 2, out_cols, inputs), lambda n, i: (n, 0, 0, 0))
    block = pl.BlockSpec((None, rows, out_cols, outputs), lambda n, i: (n, i, 0, 0))
    in_specs = [
        full,
        full,
        full,
        pl.BlockSpec((9 * inputs, outputs), lambda n, i: (0, 0)),
        pl.BlockSpec((None, outputs, rows * out_cols), lambda n, i: (n, 0, i)),
    ]
    operands = [*shifted, weight.reshape(9 * inputs, outputs), grad_t]
    if prev is not None:
        in_specs.append(block)
        operands.append(prev)
    flops = 4 * owned * out_rows * out_cols * 9 * inputs * outputs
    return pl.pallas_call(
        functools.partial(second_kernel, rows=rows, carry=prev is not None, group=max(1, 256 // inputs)),
        grid=(owned, out_rows // rows),
        in_specs=in_specs,
        out_specs=[block, pl.BlockSpec((None, outputs, 9 * inputs), lambda n, i: (n, 0, 0))],
        out_shape=[
            jax.ShapeDtypeStruct((owned, out_rows, out_cols, outputs), out_dtype),
            jax.ShapeDtypeStruct((owned, outputs, 9 * inputs), jnp.float32),
        ],
        compiler_params=pltpu.CompilerParams(
            dimension_semantics=("arbitrary", "arbitrary"), vmem_limit_bytes=60 * 1024 * 1024
        ),
        cost_estimate=pl.CostEstimate(
            flops=flops,
            transcendentals=0,
            bytes_accessed=hidden.size * 2 * 4 + owned * out_rows * out_cols * outputs * 8
            + owned * outputs * 9 * inputs * 4,
        ),
    )(*operands)


def halving_reduce_scatter(partial, axes):
    devices = lax.axis_size(axes)
    tiles = lax.axis_size(axes[-1])
    bits = devices.bit_length() - 1
    me = lax.axis_index(axes)
    core = tiles.bit_length() - 1
    order = [core] + [b for b in range(bits) if b > core] + [b for b in range(core)]
    rows = partial.shape[0] // devices
    buf = partial.reshape((2,) * bits + (rows,) + partial.shape[1:])
    remaining = list(range(bits - 1, -1, -1))
    for bit in order:
        axis = remaining.index(bit)
        mine = (me >> bit) & 1
        keep = lax.dynamic_index_in_dim(buf, mine, axis=axis, keepdims=False)
        send = lax.dynamic_index_in_dim(buf, 1 - mine, axis=axis, keepdims=False)
        pairs = [(i, i ^ (1 << bit)) for i in range(devices)]
        buf = keep + lax.ppermute(send, axes, pairs)
        remaining.pop(axis)
    return buf


def local(maps, first_weight, second_weight, out_grad):
    tiles = lax.axis_size("tile")
    images, height, width, inputs = maps.shape
    outputs = first_weight.shape[3]
    owned = images // tiles
    half_rows = height // 2
    chunks = 2 if outputs % 256 == 0 else 1
    part = outputs // chunks
    upper_row = shifted_2(maps[:, height - 1 : height], "tile", 1)
    grad_t = out_grad.reshape(owned, -1, outputs).transpose(0, 2, 1)
    conv = None
    pieces = []
    for chunk in range(chunks):
        channels = slice(chunk * part, (chunk + 1) * part)
        local_hidden = first_conv(maps, upper_row, first_weight[..., channels])
        arrived = lax.all_to_all(
            local_hidden.reshape(tiles, owned, half_rows, width // 2, part),
            "tile",
            split_axis=0,
            concat_axis=2,
            tiled=True,
        )
        if conv is not None:
            arrived, conv = lax.optimization_barrier((arrived, conv))
        hidden = arrived.reshape(owned, half_rows * tiles, width // 2, part)
        last = chunk == chunks - 1
        conv, partial = second_stage(
            hidden, second_weight[:, :, channels], grad_t, conv, jnp.bfloat16 if last else jnp.float32
        )
        summed = halving_reduce_scatter(partial.sum(axis=0).reshape(outputs, 9 * part), ("group", "tile"))
        pieces.append(summed.reshape(-1, 9, part))
    weight_grad = jnp.concatenate(pieces, axis=-1).reshape(-1, 3, 3, outputs)
    return (conv, weight_grad)


def solution(mesh):
    return jax.shard_map(
        local,
        mesh=mesh,
        in_specs=(P("group", "tile", None, None), P(), P(), P(("group", "tile"), None, None, None)),
        out_specs=(P(("group", "tile"), None, None, None), P(("group", "tile"), None, None, None)),
        check_vma=False,
    )
```

```python
import functools

import jax
import jax.numpy as jnp
from jax import lax
from jax.experimental import pallas as pl
from jax.experimental.pallas import tpu as pltpu
from jax.sharding import PartitionSpec as P


def shifted_2(shard, axis, by):
    length = lax.axis_size(axis)
    pairs = [(i, i + by) for i in range(length) if 0 <= i + by < length]
    return lax.ppermute(shard, axis, pairs)


def shift_cols_right(slab):
    zero_col = jnp.zeros_like(slab[:, :, :1])
    return jnp.concatenate([zero_col, slab[:, :, :-1]], axis=2)


def shift_cols_left(slab):
    zero_col = jnp.zeros_like(slab[:, :, :1])
    return jnp.concatenate([slab[:, :, 1:], zero_col], axis=2)


def first_conv(source, upper_row, first_weight):
    images, rows, width, inputs = source.shape
    outputs = first_weight.shape[3]
    paired = source.reshape(images, rows // 2, 2, width // 2, 2 * inputs)
    even_rows = paired[:, :, 0]
    odd_rows = paired[:, :, 1]
    upper_paired = upper_row.reshape(images, 1, width // 2, 2 * inputs)
    odd_above = jnp.concatenate([upper_paired, odd_rows[:, :-1]], axis=1)
    sources = [odd_above, even_rows, odd_rows]
    total = jnp.zeros((images, rows // 2, width // 2, outputs), jnp.float32)
    for tap_row in range(3):
        wide_kernel = first_weight[tap_row, 1:3].reshape(2 * inputs, outputs)
        total = total + jnp.dot(sources[tap_row], wide_kernel, preferred_element_type=jnp.float32)
    halves = jnp.concatenate([piece[..., inputs:] for piece in sources], axis=-1)
    narrow_kernel = first_weight[:, 0].reshape(3 * inputs, outputs)
    total = total + jnp.dot(
        shift_cols_right(halves), narrow_kernel, preferred_element_type=jnp.float32
    )
    return jnp.maximum(total, 0.0).astype(jnp.bfloat16)


def first_kernel(x_ref, up_ref, w_ref, low_ref, high_ref, scratch):
    rows, width, inputs = x_ref.shape
    out_rows, out_cols = rows // 2, width // 2
    scratch[0] = up_ref[0].astype(jnp.float32)
    scratch[1:] = x_ref[...].astype(jnp.float32)
    first_col = lax.broadcasted_iota(jnp.int32, (out_rows, out_cols, inputs), 1) == 0
    pieces = []
    for tap_row in range(3):
        even = scratch[pl.ds(tap_row, out_rows, stride=2), pl.ds(0, out_cols, stride=2), :]
        odd = scratch[pl.ds(tap_row, out_rows, stride=2), pl.ds(1, out_cols, stride=2), :]
        left = jnp.where(first_col, 0.0, pltpu.roll(odd, 1, 1))
        pieces += [even, odd, left]
    patches = jnp.concatenate(
        [p.astype(jnp.bfloat16).reshape(out_rows * out_cols, inputs) for p in pieces], axis=-1
    )
    total = jnp.dot(patches, w_ref[...], preferred_element_type=jnp.float32)
    hidden = jnp.maximum(total, 0.0).astype(jnp.bfloat16).reshape(out_rows, out_cols, -1)
    half = low_ref.shape[-1]
    low_ref[...] = hidden[..., :half]
    high_ref[...] = hidden[..., half:]


def first_stage(maps, upper_row, first_weight, part):
    images, rows, width, inputs = maps.shape
    outputs = first_weight.shape[3]
    weight = first_weight[:, jnp.array([1, 2, 0])].reshape(9 * inputs, outputs)
    out_block = pl.BlockSpec((None, rows // 2, width // 2, part), lambda n: (n, 0, 0, 0))
    shape = jax.ShapeDtypeStruct((images, rows // 2, width // 2, part), jnp.bfloat16)
    return pl.pallas_call(
        first_kernel,
        grid=(images,),
        in_specs=[
            pl.BlockSpec((None, rows, width, inputs), lambda n: (n, 0, 0, 0)),
            pl.BlockSpec((None, 1, width, inputs), lambda n: (n, 0, 0, 0)),
            pl.BlockSpec((9 * inputs, outputs), lambda n: (0, 0)),
        ],
        out_specs=[out_block, out_block],
        out_shape=[shape, shape],
        scratch_shapes=[pltpu.VMEM((rows + 1, width, inputs), jnp.float32)],
        compiler_params=pltpu.CompilerParams(
            dimension_semantics=("arbitrary",), vmem_limit_bytes=60 * 1024 * 1024
        ),
        cost_estimate=pl.CostEstimate(
            flops=2 * images * (rows // 2) * (width // 2) * 9 * inputs * outputs,
            transcendentals=0,
            bytes_accessed=maps.size * 2 + images * (rows // 2) * (width // 2) * outputs * 2,
        ),
    )(maps, upper_row, weight)


def second_kernel(*refs, rows, carry, group):
    if carry:
        left_ref, mid_ref, right_ref, weight_ref, grad_ref, prev_ref, out_ref, wgrad_ref = refs
    else:
        left_ref, mid_ref, right_ref, weight_ref, grad_ref, out_ref, wgrad_ref = refs
    step = pl.program_id(1)
    _, width, outputs = out_ref.shape
    inputs = mid_ref.shape[-1]
    sources = (left_ref, mid_ref, right_ref)
    grad_t = grad_ref[...]
    if carry:
        acc = prev_ref[...].reshape(rows * width, outputs)
    else:
        acc = jnp.zeros((rows * width, outputs), jnp.float32)
    for first in range(0, 9, group):
        taps = range(first, min(first + group, 9))
        windows = [
            sources[tap % 3][pl.ds(step * rows + tap // 3, rows)].reshape(rows * width, inputs)
            for tap in taps
        ]
        window = windows[0] if len(windows) == 1 else jnp.concatenate(windows, axis=-1)
        lanes = slice(first * inputs, (first + len(windows)) * inputs)
        acc = acc + jnp.dot(window, weight_ref[lanes, :], preferred_element_type=jnp.float32)
        term = jnp.dot(grad_t, window, preferred_element_type=jnp.float32)

        @pl.when(step == 0)
        def _():
            wgrad_ref[:, lanes] = term

        @pl.when(step > 0)
        def _():
            wgrad_ref[:, lanes] += term

    out_ref[...] = acc.astype(out_ref.dtype).reshape(rows, width, outputs)


def second_stage(hidden, weight, grad_t, prev, out_dtype):
    owned, out_rows, out_cols, inputs = hidden.shape
    outputs = weight.shape[-1]
    rows = min(16, out_rows)
    row_padded = jnp.pad(hidden, ((0, 0), (1, 1), (0, 0), (0, 0)))
    shifted = [shift_cols_right(row_padded), row_padded, shift_cols_left(row_padded)]
    full = pl.BlockSpec((None, out_rows + 2, out_cols, inputs), lambda n, i: (n, 0, 0, 0))
    block = pl.BlockSpec((None, rows, out_cols, outputs), lambda n, i: (n, i, 0, 0))
    in_specs = [
        full,
        full,
        full,
        pl.BlockSpec((9 * inputs, outputs), lambda n, i: (0, 0)),
        pl.BlockSpec((None, outputs, rows * out_cols), lambda n, i: (n, 0, i)),
    ]
    operands = [*shifted, weight.reshape(9 * inputs, outputs), grad_t]
    if prev is not None:
        in_specs.append(block)
        operands.append(prev)
    flops = 4 * owned * out_rows * out_cols * 9 * inputs * outputs
    return pl.pallas_call(
        functools.partial(second_kernel, rows=rows, carry=prev is not None, group=max(1, 256 // inputs)),
        grid=(owned, out_rows // rows),
        in_specs=in_specs,
        out_specs=[block, pl.BlockSpec((None, outputs, 9 * inputs), lambda n, i: (n, 0, 0))],
        out_shape=[
            jax.ShapeDtypeStruct((owned, out_rows, out_cols, outputs), out_dtype),
            jax.ShapeDtypeStruct((owned, outputs, 9 * inputs), jnp.float32),
        ],
        compiler_params=pltpu.CompilerParams(
            dimension_semantics=("arbitrary", "arbitrary"), vmem_limit_bytes=60 * 1024 * 1024
        ),
        cost_estimate=pl.CostEstimate(
            flops=flops,
            transcendentals=0,
            bytes_accessed=hidden.size * 2 * 4 + owned * out_rows * out_cols * outputs * 8
            + owned * outputs * 9 * inputs * 4,
        ),
    )(*operands)


def halving_reduce_scatter(partial, axes):
    devices = lax.axis_size(axes)
    tiles = lax.axis_size(axes[-1])
    bits = devices.bit_length() - 1
    me = lax.axis_index(axes)
    core = tiles.bit_length() - 1
    order = [core] + [b for b in range(bits) if b > core] + [b for b in range(core)]
    rows = partial.shape[0] // devices
    buf = partial.reshape((2,) * bits + (rows,) + partial.shape[1:])
    remaining = list(range(bits - 1, -1, -1))
    for bit in order:
        axis = remaining.index(bit)
        mine = (me >> bit) & 1
        keep = lax.dynamic_index_in_dim(buf, mine, axis=axis, keepdims=False)
        send = lax.dynamic_index_in_dim(buf, 1 - mine, axis=axis, keepdims=False)
        pairs = [(i, i ^ (1 << bit)) for i in range(devices)]
        buf = keep + lax.ppermute(send, axes, pairs)
        remaining.pop(axis)
    return buf


def local(maps, first_weight, second_weight, out_grad):
    tiles = lax.axis_size("tile")
    images, height, width, inputs = maps.shape
    outputs = first_weight.shape[3]
    owned = images // tiles
    half_rows = height // 2
    chunks = 2
    part = outputs // chunks
    upper_row = shifted_2(maps[:, height - 1 : height], "tile", 1)
    grad_t = out_grad.reshape(owned, -1, outputs).transpose(0, 2, 1)
    conv = None
    pieces = []
    halves = first_stage(maps, upper_row, first_weight, part)
    for chunk in range(chunks):
        channels = slice(chunk * part, (chunk + 1) * part)
        local_hidden = halves[chunk]
        arrived = lax.all_to_all(
            local_hidden.reshape(tiles, owned, half_rows, width // 2, part),
            "tile",
            split_axis=0,
            concat_axis=2,
            tiled=True,
        )
        if conv is not None:
            arrived, conv = lax.optimization_barrier((arrived, conv))
        hidden = arrived.reshape(owned, half_rows * tiles, width // 2, part)
        last = chunk == chunks - 1
        conv, partial = second_stage(
            hidden, second_weight[:, :, channels], grad_t, conv, jnp.bfloat16 if last else jnp.float32
        )
        summed = halving_reduce_scatter(partial.sum(axis=0).reshape(outputs, 9 * part), ("group", "tile"))
        pieces.append(summed.reshape(-1, 9, part))
    weight_grad = jnp.concatenate(pieces, axis=-1).reshape(-1, 3, 3, outputs)
    return (conv, weight_grad)


def solution(mesh):
    return jax.shard_map(
        local,
        mesh=mesh,
        in_specs=(P("group", "tile", None, None), P(), P(), P(("group", "tile"), None, None, None)),
        out_specs=(P(("group", "tile"), None, None, None), P(("group", "tile"), None, None, None)),
        check_vma=False,
    )
```

```python
import functools

import jax
import jax.numpy as jnp
from jax import lax
from jax.experimental import pallas as pl
from jax.experimental.pallas import tpu as pltpu
from jax.sharding import PartitionSpec as P


def shifted_2(shard, axis, by):
    length = lax.axis_size(axis)
    pairs = [(i, i + by) for i in range(length) if 0 <= i + by < length]
    return lax.ppermute(shard, axis, pairs)


def shift_cols_right(slab):
    zero_col = jnp.zeros_like(slab[:, :, :1])
    return jnp.concatenate([zero_col, slab[:, :, :-1]], axis=2)


def shift_cols_left(slab):
    zero_col = jnp.zeros_like(slab[:, :, :1])
    return jnp.concatenate([slab[:, :, 1:], zero_col], axis=2)


def first_conv(source, upper_row, first_weight):
    images, rows, width, inputs = source.shape
    outputs = first_weight.shape[3]
    paired = source.reshape(images, rows // 2, 2, width // 2, 2 * inputs)
    even_rows = paired[:, :, 0]
    odd_rows = paired[:, :, 1]
    upper_paired = upper_row.reshape(images, 1, width // 2, 2 * inputs)
    odd_above = jnp.concatenate([upper_paired, odd_rows[:, :-1]], axis=1)
    sources = [odd_above, even_rows, odd_rows]
    total = jnp.zeros((images, rows // 2, width // 2, outputs), jnp.float32)
    for tap_row in range(3):
        wide_kernel = first_weight[tap_row, 1:3].reshape(2 * inputs, outputs)
        total = total + jnp.dot(sources[tap_row], wide_kernel, preferred_element_type=jnp.float32)
    halves = jnp.concatenate([piece[..., inputs:] for piece in sources], axis=-1)
    narrow_kernel = first_weight[:, 0].reshape(3 * inputs, outputs)
    total = total + jnp.dot(
        shift_cols_right(halves), narrow_kernel, preferred_element_type=jnp.float32
    )
    return jnp.maximum(total, 0.0).astype(jnp.bfloat16)


def first_kernel(*refs, with_up):
    if with_up:
        x_ref, up_ref, w_ref, _, _, low_ref, high_ref, scratch = refs
    else:
        x_ref, w_ref, low_ref, high_ref, scratch = refs
    rows, width, inputs = x_ref.shape
    out_rows, out_cols = rows // 2, width // 2
    if with_up:
        scratch[0] = up_ref[0].astype(jnp.float32)
    else:
        scratch[0] = jnp.zeros(scratch.shape[1:], jnp.float32)
    scratch[1:] = x_ref[...].astype(jnp.float32)
    first_col = lax.broadcasted_iota(jnp.int32, (out_rows, out_cols, inputs), 1) == 0
    pieces = []
    for tap_row in range(3):
        even = scratch[pl.ds(tap_row, out_rows, stride=2), pl.ds(0, out_cols, stride=2), :]
        odd = scratch[pl.ds(tap_row, out_rows, stride=2), pl.ds(1, out_cols, stride=2), :]
        left = jnp.where(first_col, 0.0, pltpu.roll(odd, 1, 1))
        pieces += [even, odd, left]
    patches = jnp.concatenate(
        [p.astype(jnp.bfloat16).reshape(out_rows * out_cols, inputs) for p in pieces], axis=-1
    )
    total = jnp.dot(patches, w_ref[...], preferred_element_type=jnp.float32)
    hidden = jnp.maximum(total, 0.0).astype(jnp.bfloat16).reshape(out_rows, out_cols, -1)
    half = low_ref.shape[-1]
    low_ref[...] = hidden[..., :half]
    high_ref[...] = hidden[..., half:]


def first_stage(maps, upper_row, first_weight, part):
    images, rows, width, inputs = maps.shape
    outputs = first_weight.shape[3]
    weight = first_weight[:, jnp.array([1, 2, 0])].reshape(9 * inputs, outputs)
    shape = jax.ShapeDtypeStruct((images, rows // 2, width // 2, part), jnp.bfloat16)
    params = pltpu.CompilerParams(dimension_semantics=("arbitrary",), vmem_limit_bytes=60 * 1024 * 1024)
    weight_spec = pl.BlockSpec((9 * inputs, outputs), lambda n: (0, 0))

    def cost(out_rows):
        return pl.CostEstimate(
            flops=2 * images * out_rows * (width // 2) * 9 * inputs * outputs,
            transcendentals=0,
            bytes_accessed=images * out_rows * 2 * width * inputs * 2 + images * out_rows * (width // 2) * outputs * 2,
        )

    out_block = pl.BlockSpec((None, rows // 2, width // 2, part), lambda n: (n, 0, 0, 0))
    low, high = pl.pallas_call(
        functools.partial(first_kernel, with_up=False),
        grid=(images,),
        in_specs=[pl.BlockSpec((None, rows, width, inputs), lambda n: (n, 0, 0, 0)), weight_spec],
        out_specs=[out_block, out_block],
        out_shape=[shape, shape],
        scratch_shapes=[pltpu.VMEM((rows + 1, width, inputs), jnp.float32)],
        compiler_params=params,
        cost_estimate=cost(rows // 2),
    )(maps, weight)
    row_block = pl.BlockSpec((None, 1, width // 2, part), lambda n: (n, 0, 0, 0))
    anywhere = pl.BlockSpec(memory_space=pl.ANY)
    return pl.pallas_call(
        functools.partial(first_kernel, with_up=True),
        grid=(images,),
        in_specs=[
            pl.BlockSpec((None, 2, width, inputs), lambda n: (n, 0, 0, 0)),
            pl.BlockSpec((None, 1, width, inputs), lambda n: (n, 0, 0, 0)),
            weight_spec,
            anywhere,
            anywhere,
        ],
        out_specs=[row_block, row_block],
        out_shape=[shape, shape],
        scratch_shapes=[pltpu.VMEM((3, width, inputs), jnp.float32)],
        input_output_aliases={3: 0, 4: 1},
        compiler_params=params,
        cost_estimate=cost(1),
    )(maps, upper_row, weight, low, high)


def second_kernel(*refs, rows, carry, group):
    if carry:
        left_ref, mid_ref, right_ref, weight_ref, grad_ref, prev_ref, out_ref, wgrad_ref = refs
    else:
        left_ref, mid_ref, right_ref, weight_ref, grad_ref, out_ref, wgrad_ref = refs
    step = pl.program_id(1)
    _, width, outputs = out_ref.shape
    inputs = mid_ref.shape[-1]
    sources = (left_ref, mid_ref, right_ref)
    grad_t = grad_ref[...]
    if carry:
        acc = prev_ref[...].reshape(rows * width, outputs)
    else:
        acc = jnp.zeros((rows * width, outputs), jnp.float32)
    for first in range(0, 9, group):
        taps = range(first, min(first + group, 9))
        windows = [
            sources[tap % 3][pl.ds(step * rows + tap // 3, rows)].reshape(rows * width, inputs)
            for tap in taps
        ]
        window = windows[0] if len(windows) == 1 else jnp.concatenate(windows, axis=-1)
        lanes = slice(first * inputs, (first + len(windows)) * inputs)
        acc = acc + jnp.dot(window, weight_ref[lanes, :], preferred_element_type=jnp.float32)
        term = jnp.dot(grad_t, window, preferred_element_type=jnp.float32)

        @pl.when(step == 0)
        def _():
            wgrad_ref[:, lanes] = term

        @pl.when(step > 0)
        def _():
            wgrad_ref[:, lanes] += term

    out_ref[...] = acc.astype(out_ref.dtype).reshape(rows, width, outputs)


def second_stage(hidden, weight, grad_t, prev, out_dtype):
    owned, out_rows, out_cols, inputs = hidden.shape
    outputs = weight.shape[-1]
    rows = min(16, out_rows)
    row_padded = jnp.pad(hidden, ((0, 0), (1, 1), (0, 0), (0, 0)))
    shifted = [shift_cols_right(row_padded), row_padded, shift_cols_left(row_padded)]
    full = pl.BlockSpec((None, out_rows + 2, out_cols, inputs), lambda n, i: (n, 0, 0, 0))
    block = pl.BlockSpec((None, rows, out_cols, outputs), lambda n, i: (n, i, 0, 0))
    in_specs = [
        full,
        full,
        full,
        pl.BlockSpec((9 * inputs, outputs), lambda n, i: (0, 0)),
        pl.BlockSpec((None, outputs, rows * out_cols), lambda n, i: (n, 0, i)),
    ]
    operands = [*shifted, weight.reshape(9 * inputs, outputs), grad_t]
    if prev is not None:
        in_specs.append(block)
        operands.append(prev)
    flops = 4 * owned * out_rows * out_cols * 9 * inputs * outputs
    return pl.pallas_call(
        functools.partial(second_kernel, rows=rows, carry=prev is not None, group=max(1, 256 // inputs)),
        grid=(owned, out_rows // rows),
        in_specs=in_specs,
        out_specs=[block, pl.BlockSpec((None, outputs, 9 * inputs), lambda n, i: (n, 0, 0))],
        out_shape=[
            jax.ShapeDtypeStruct((owned, out_rows, out_cols, outputs), out_dtype),
            jax.ShapeDtypeStruct((owned, outputs, 9 * inputs), jnp.float32),
        ],
        compiler_params=pltpu.CompilerParams(
            dimension_semantics=("arbitrary", "arbitrary"), vmem_limit_bytes=60 * 1024 * 1024
        ),
        cost_estimate=pl.CostEstimate(
            flops=flops,
            transcendentals=0,
            bytes_accessed=hidden.size * 2 * 4 + owned * out_rows * out_cols * outputs * 8
            + owned * outputs * 9 * inputs * 4,
        ),
    )(*operands)


def halving_reduce_scatter(partial, axes):
    devices = lax.axis_size(axes)
    tiles = lax.axis_size(axes[-1])
    bits = devices.bit_length() - 1
    me = lax.axis_index(axes)
    core = tiles.bit_length() - 1
    order = [core] + [b for b in range(bits) if b > core] + [b for b in range(core)]
    rows = partial.shape[0] // devices
    buf = partial.reshape((2,) * bits + (rows,) + partial.shape[1:])
    remaining = list(range(bits - 1, -1, -1))
    for bit in order:
        axis = remaining.index(bit)
        mine = (me >> bit) & 1
        keep = lax.dynamic_index_in_dim(buf, mine, axis=axis, keepdims=False)
        send = lax.dynamic_index_in_dim(buf, 1 - mine, axis=axis, keepdims=False)
        pairs = [(i, i ^ (1 << bit)) for i in range(devices)]
        buf = keep + lax.ppermute(send, axes, pairs)
        remaining.pop(axis)
    return buf


def local(maps, first_weight, second_weight, out_grad):
    tiles = lax.axis_size("tile")
    images, height, width, inputs = maps.shape
    outputs = first_weight.shape[3]
    owned = images // tiles
    half_rows = height // 2
    chunks = 2
    part = outputs // chunks
    upper_row = shifted_2(maps[:, height - 1 : height], "tile", 1)
    grad_t = out_grad.reshape(owned, -1, outputs).transpose(0, 2, 1)
    conv = None
    pieces = []
    halves = first_stage(maps, upper_row, first_weight, part)
    for chunk in range(chunks):
        channels = slice(chunk * part, (chunk + 1) * part)
        local_hidden = halves[chunk]
        arrived = lax.all_to_all(
            local_hidden.reshape(tiles, owned, half_rows, width // 2, part),
            "tile",
            split_axis=0,
            concat_axis=2,
            tiled=True,
        )
        if conv is not None:
            arrived, conv = lax.optimization_barrier((arrived, conv))
        hidden = arrived.reshape(owned, half_rows * tiles, width // 2, part)
        last = chunk == chunks - 1
        conv, partial = second_stage(
            hidden, second_weight[:, :, channels], grad_t, conv, jnp.bfloat16 if last else jnp.float32
        )
        summed = halving_reduce_scatter(partial.sum(axis=0).reshape(outputs, 9 * part), ("group", "tile"))
        pieces.append(summed.reshape(-1, 9, part))
    weight_grad = jnp.concatenate(pieces, axis=-1).reshape(-1, 3, 3, outputs)
    return (conv, weight_grad)


def solution(mesh):
    return jax.shard_map(
        local,
        mesh=mesh,
        in_specs=(P("group", "tile", None, None), P(), P(), P(("group", "tile"), None, None, None)),
        out_specs=(P(("group", "tile"), None, None, None), P(("group", "tile"), None, None, None)),
        check_vma=False,
    )
```

```python
import functools

import jax
import jax.numpy as jnp
from jax import lax
from jax.experimental import pallas as pl
from jax.experimental.pallas import tpu as pltpu
from jax.sharding import PartitionSpec as P


def shifted_2(shard, axis, by):
    length = lax.axis_size(axis)
    pairs = [(i, i + by) for i in range(length) if 0 <= i + by < length]
    return lax.ppermute(shard, axis, pairs)


def shift_cols_right(slab):
    zero_col = jnp.zeros_like(slab[:, :, :1])
    return jnp.concatenate([zero_col, slab[:, :, :-1]], axis=2)


def shift_cols_left(slab):
    zero_col = jnp.zeros_like(slab[:, :, :1])
    return jnp.concatenate([slab[:, :, 1:], zero_col], axis=2)


def first_conv(source, upper_row, first_weight):
    images, rows, width, inputs = source.shape
    outputs = first_weight.shape[3]
    paired = source.reshape(images, rows // 2, 2, width // 2, 2 * inputs)
    even_rows = paired[:, :, 0]
    odd_rows = paired[:, :, 1]
    upper_paired = upper_row.reshape(images, 1, width // 2, 2 * inputs)
    odd_above = jnp.concatenate([upper_paired, odd_rows[:, :-1]], axis=1)
    sources = [odd_above, even_rows, odd_rows]
    total = jnp.zeros((images, rows // 2, width // 2, outputs), jnp.float32)
    for tap_row in range(3):
        wide_kernel = first_weight[tap_row, 1:3].reshape(2 * inputs, outputs)
        total = total + jnp.dot(sources[tap_row], wide_kernel, preferred_element_type=jnp.float32)
    halves = jnp.concatenate([piece[..., inputs:] for piece in sources], axis=-1)
    narrow_kernel = first_weight[:, 0].reshape(3 * inputs, outputs)
    total = total + jnp.dot(
        shift_cols_right(halves), narrow_kernel, preferred_element_type=jnp.float32
    )
    return jnp.maximum(total, 0.0).astype(jnp.bfloat16)


def first_kernel(x_ref, up_ref, w_ref, low_ref, high_ref, scratch):
    rows, width, inputs = x_ref.shape
    out_rows, out_cols = rows // 2, width // 2
    scratch[0] = up_ref[0].astype(jnp.float32)
    scratch[1:] = x_ref[...].astype(jnp.float32)
    first_col = lax.broadcasted_iota(jnp.int32, (out_rows, out_cols, inputs), 1) == 0
    pieces = []
    for tap_row in range(3):
        even = scratch[pl.ds(tap_row, out_rows, stride=2), pl.ds(0, out_cols, stride=2), :]
        odd = scratch[pl.ds(tap_row, out_rows, stride=2), pl.ds(1, out_cols, stride=2), :]
        left = jnp.where(first_col, 0.0, pltpu.roll(odd, 1, 1))
        pieces += [even, odd, left]
    patches = jnp.concatenate(
        [p.astype(jnp.bfloat16).reshape(out_rows * out_cols, inputs) for p in pieces], axis=-1
    )
    total = jnp.dot(patches, w_ref[...], preferred_element_type=jnp.float32)
    hidden = jnp.maximum(total, 0.0).astype(jnp.bfloat16).reshape(out_rows, out_cols, -1)
    half = low_ref.shape[-1]
    low_ref[...] = hidden[..., :half]
    high_ref[...] = hidden[..., half:]


def first_stage(maps, upper_row, first_weight, part):
    images, rows, width, inputs = maps.shape
    outputs = first_weight.shape[3]
    weight = first_weight[:, jnp.array([1, 2, 0])].reshape(9 * inputs, outputs)
    out_block = pl.BlockSpec((None, rows // 2, width // 2, part), lambda n: (n, 0, 0, 0))
    shape = jax.ShapeDtypeStruct((images, rows // 2, width // 2, part), jnp.bfloat16)
    return pl.pallas_call(
        first_kernel,
        grid=(images,),
        in_specs=[
            pl.BlockSpec((None, rows, width, inputs), lambda n: (n, 0, 0, 0)),
            pl.BlockSpec((None, 1, width, inputs), lambda n: (n, 0, 0, 0)),
            pl.BlockSpec((9 * inputs, outputs), lambda n: (0, 0)),
        ],
        out_specs=[out_block, out_block],
        out_shape=[shape, shape],
        scratch_shapes=[pltpu.VMEM((rows + 1, width, inputs), jnp.float32)],
        compiler_params=pltpu.CompilerParams(
            dimension_semantics=("arbitrary",), vmem_limit_bytes=60 * 1024 * 1024
        ),
        cost_estimate=pl.CostEstimate(
            flops=2 * images * (rows // 2) * (width // 2) * 9 * inputs * outputs,
            transcendentals=0,
            bytes_accessed=maps.size * 2 + images * (rows // 2) * (width // 2) * outputs * 2,
        ),
    )(maps, upper_row, weight)


def second_kernel(*refs, rows, carry, group, base, conv, wgrad, alias):
    refs = list(refs)
    left_ref, mid_ref, right_ref, weight_ref, grad_ref = refs[:5]
    rest = refs[5:]
    prev_ref = rest.pop(0) if carry else None
    if alias:
        rest.pop(0)
    out_ref = rest.pop(0) if conv else None
    wgrad_ref = rest.pop(0) if wgrad else None
    step = pl.program_id(1)
    block = base + step
    width = mid_ref.shape[1]
    inputs = mid_ref.shape[-1]
    outputs = weight_ref.shape[-1]
    sources = (left_ref, mid_ref, right_ref)
    if wgrad:
        grad_t = grad_ref[...]
    if conv:
        if carry:
            acc = prev_ref[...].reshape(rows * width, outputs)
        else:
            acc = jnp.zeros((rows * width, outputs), jnp.float32)
    for first in range(0, 9, group):
        taps = range(first, min(first + group, 9))
        windows = [
            sources[tap % 3][pl.ds(block * rows + tap // 3, rows)].reshape(rows * width, inputs)
            for tap in taps
        ]
        window = windows[0] if len(windows) == 1 else jnp.concatenate(windows, axis=-1)
        lanes = slice(first * inputs, (first + len(windows)) * inputs)
        if conv:
            acc = acc + jnp.dot(window, weight_ref[lanes, :], preferred_element_type=jnp.float32)
        if wgrad:
            term = jnp.dot(grad_t, window, preferred_element_type=jnp.float32)

            @pl.when(step == 0)
            def _():
                wgrad_ref[:, lanes] = term

            @pl.when(step > 0)
            def _():
                wgrad_ref[:, lanes] += term

    if conv:
        out_ref[...] = acc.astype(out_ref.dtype).reshape(rows, width, outputs)


def second_stage(shifted, weight, grad_t, prev, out_dtype, conv=True, wgrad=True, span=None, into=None):
    owned, padded_rows, out_cols, inputs = shifted[0].shape
    out_rows = padded_rows - 2
    outputs = weight.shape[-1]
    rows = min(16, out_rows)
    first_row, last_row = span if span is not None else (0, out_rows)
    base = first_row // rows
    full = pl.BlockSpec((None, out_rows + 2, out_cols, inputs), lambda n, i: (n, 0, 0, 0))
    block = pl.BlockSpec((None, rows, out_cols, outputs), lambda n, i: (n, base + i, 0, 0))
    in_specs = [
        full,
        full,
        full,
        pl.BlockSpec((9 * inputs, outputs), lambda n, i: (0, 0)),
        pl.BlockSpec((None, outputs, rows * out_cols), lambda n, i: (n, 0, base + i)),
    ]
    operands = [*shifted, weight.reshape(9 * inputs, outputs), grad_t]
    if prev is not None:
        in_specs.append(block)
        operands.append(prev)
    aliases = {}
    if into is not None:
        aliases = {len(operands): 0}
        in_specs.append(pl.BlockSpec(memory_space=pl.ANY))
        operands.append(into)
    out_specs, out_shape = [], []
    if conv:
        out_specs.append(block)
        out_shape.append(jax.ShapeDtypeStruct((owned, out_rows, out_cols, outputs), out_dtype))
    if wgrad:
        out_specs.append(pl.BlockSpec((None, outputs, 9 * inputs), lambda n, i: (n, 0, 0)))
        out_shape.append(jax.ShapeDtypeStruct((owned, outputs, 9 * inputs), jnp.float32))
    span_rows = last_row - first_row
    flops = 2 * owned * span_rows * out_cols * 9 * inputs * outputs * (int(conv) + int(wgrad))
    return pl.pallas_call(
        functools.partial(
            second_kernel, rows=rows, carry=prev is not None, group=max(1, 256 // inputs),
            base=base, conv=conv, wgrad=wgrad, alias=into is not None,
        ),
        grid=(owned, span_rows // rows),
        in_specs=in_specs,
        out_specs=out_specs,
        out_shape=out_shape,
        input_output_aliases=aliases,
        compiler_params=pltpu.CompilerParams(
            dimension_semantics=("arbitrary", "arbitrary"), vmem_limit_bytes=60 * 1024 * 1024
        ),
        cost_estimate=pl.CostEstimate(
            flops=flops,
            transcendentals=0,
            bytes_accessed=owned * (out_rows + 2) * out_cols * inputs * 6
            + owned * span_rows * out_cols * outputs * 8,
        ),
    )(*operands)


def shift_copies(hidden):
    row_padded = jnp.pad(hidden, ((0, 0), (1, 1), (0, 0), (0, 0)))
    return [shift_cols_right(row_padded), row_padded, shift_cols_left(row_padded)]


def halving_plan(partial, axes):
    devices = lax.axis_size(axes)
    tiles = lax.axis_size(axes[-1])
    bits = devices.bit_length() - 1
    me = lax.axis_index(axes)
    core = tiles.bit_length() - 1
    order = [core] + [b for b in range(bits) if b > core] + [b for b in range(core)]
    rows = partial.shape[0] // devices
    buf = partial.reshape((2,) * bits + (rows,) + partial.shape[1:])

    def make(bit, axis):
        def step(buf):
            mine = (me >> bit) & 1
            keep = lax.dynamic_index_in_dim(buf, mine, axis=axis, keepdims=False)
            send = lax.dynamic_index_in_dim(buf, 1 - mine, axis=axis, keepdims=False)
            pairs = [(i, i ^ (1 << bit)) for i in range(devices)]
            return keep + lax.ppermute(send, axes, pairs)

        return step

    remaining = list(range(bits - 1, -1, -1))
    steps = []
    for bit in order:
        axis = remaining.index(bit)
        steps.append(make(bit, axis))
        remaining.pop(axis)
    return buf, steps


def local(maps, first_weight, second_weight, out_grad):
    tiles = lax.axis_size("tile")
    images, height, width, inputs = maps.shape
    outputs = first_weight.shape[3]
    owned = images // tiles
    half_rows = height // 2
    chunks = 2
    part = outputs // chunks
    upper_row = shifted_2(maps[:, height - 1 : height], "tile", 1)
    grad_t = out_grad.reshape(owned, -1, outputs).transpose(0, 2, 1)
    conv = None
    plans = []
    halves = first_stage(maps, upper_row, first_weight, part)
    for chunk in range(chunks):
        channels = slice(chunk * part, (chunk + 1) * part)
        local_hidden = halves[chunk]
        arrived = lax.all_to_all(
            local_hidden.reshape(tiles, owned, half_rows, width // 2, part),
            "tile",
            split_axis=0,
            concat_axis=2,
            tiled=True,
        )
        if conv is not None:
            arrived, conv = lax.optimization_barrier((arrived, conv))
        hidden = arrived.reshape(owned, half_rows * tiles, width // 2, part)
        shifted = shift_copies(hidden)
        weight = second_weight[:, :, channels]
        if chunk < chunks - 1:
            conv, partial = second_stage(shifted, weight, grad_t, conv, jnp.float32)
        else:
            (partial,) = second_stage(shifted, weight, grad_t, None, jnp.float32, conv=False)
        plans.append(halving_plan(partial.sum(axis=0).reshape(outputs, 9 * part), ("group", "tile")))
    out_rows = half_rows * tiles
    spans = 4 if out_rows % 64 == 0 else 1
    span = out_rows // spans
    bufs = [buf for buf, _ in plans]
    result = None
    for index in range(len(plans[0][1])):
        bufs = [steps[index](buf) for buf, (_, steps) in zip(bufs, plans)]
        if index < spans:
            (result,) = second_stage(
                shifted, weight, grad_t, conv, jnp.bfloat16, wgrad=False,
                span=(index * span, (index + 1) * span), into=result,
            )
            result, bufs = lax.optimization_barrier((result, bufs))
    pieces = [buf.reshape(-1, 9, part) for buf in bufs]
    conv = result
    weight_grad = jnp.concatenate(pieces, axis=-1).reshape(-1, 3, 3, outputs)
    return (conv, weight_grad)


def solution(mesh):
    return jax.shard_map(
        local,
        mesh=mesh,
        in_specs=(P("group", "tile", None, None), P(), P(), P(("group", "tile"), None, None, None)),
        out_specs=(P(("group", "tile"), None, None, None), P(("group", "tile"), None, None, None)),
        check_vma=False,
    )
```

```python
import functools

import jax
import jax.numpy as jnp
from jax import lax
from jax.experimental import pallas as pl
from jax.experimental.pallas import tpu as pltpu
from jax.sharding import PartitionSpec as P


def shifted_2(shard, axis, by):
    length = lax.axis_size(axis)
    pairs = [(i, i + by) for i in range(length) if 0 <= i + by < length]
    return lax.ppermute(shard, axis, pairs)


def shift_cols_right(slab):
    zero_col = jnp.zeros_like(slab[:, :, :1])
    return jnp.concatenate([zero_col, slab[:, :, :-1]], axis=2)


def shift_cols_left(slab):
    zero_col = jnp.zeros_like(slab[:, :, :1])
    return jnp.concatenate([slab[:, :, 1:], zero_col], axis=2)


def first_conv(source, upper_row, first_weight):
    images, rows, width, inputs = source.shape
    outputs = first_weight.shape[3]
    paired = source.reshape(images, rows // 2, 2, width // 2, 2 * inputs)
    even_rows = paired[:, :, 0]
    odd_rows = paired[:, :, 1]
    upper_paired = upper_row.reshape(images, 1, width // 2, 2 * inputs)
    odd_above = jnp.concatenate([upper_paired, odd_rows[:, :-1]], axis=1)
    sources = [odd_above, even_rows, odd_rows]
    total = jnp.zeros((images, rows // 2, width // 2, outputs), jnp.float32)
    for tap_row in range(3):
        wide_kernel = first_weight[tap_row, 1:3].reshape(2 * inputs, outputs)
        total = total + jnp.dot(sources[tap_row], wide_kernel, preferred_element_type=jnp.float32)
    halves = jnp.concatenate([piece[..., inputs:] for piece in sources], axis=-1)
    narrow_kernel = first_weight[:, 0].reshape(3 * inputs, outputs)
    total = total + jnp.dot(
        shift_cols_right(halves), narrow_kernel, preferred_element_type=jnp.float32
    )
    return jnp.maximum(total, 0.0).astype(jnp.bfloat16)


def first_kernel(x_ref, up_ref, w_ref, low_ref, high_ref, scratch):
    rows, width, inputs = x_ref.shape
    out_rows, out_cols = rows // 2, width // 2
    scratch[0] = up_ref[0].astype(jnp.float32)
    scratch[1:] = x_ref[...].astype(jnp.float32)
    first_col = lax.broadcasted_iota(jnp.int32, (out_rows, out_cols, inputs), 1) == 0
    pieces = []
    for tap_row in range(3):
        even = scratch[pl.ds(tap_row, out_rows, stride=2), pl.ds(0, out_cols, stride=2), :]
        odd = scratch[pl.ds(tap_row, out_rows, stride=2), pl.ds(1, out_cols, stride=2), :]
        left = jnp.where(first_col, 0.0, pltpu.roll(odd, 1, 1))
        pieces += [even, odd, left]
    patches = jnp.concatenate(
        [p.astype(jnp.bfloat16).reshape(out_rows * out_cols, inputs) for p in pieces], axis=-1
    )
    total = jnp.dot(patches, w_ref[...], preferred_element_type=jnp.float32)
    hidden = jnp.maximum(total, 0.0).astype(jnp.bfloat16).reshape(out_rows, out_cols, -1)
    half = low_ref.shape[-1]
    low_ref[...] = hidden[..., :half]
    high_ref[...] = hidden[..., half:]


def first_stage(maps, upper_row, first_weight, part):
    images, rows, width, inputs = maps.shape
    outputs = first_weight.shape[3]
    weight = first_weight[:, jnp.array([1, 2, 0])].reshape(9 * inputs, outputs)
    out_block = pl.BlockSpec((None, rows // 2, width // 2, part), lambda n: (n, 0, 0, 0))
    shape = jax.ShapeDtypeStruct((images, rows // 2, width // 2, part), jnp.bfloat16)
    return pl.pallas_call(
        first_kernel,
        grid=(images,),
        in_specs=[
            pl.BlockSpec((None, rows, width, inputs), lambda n: (n, 0, 0, 0)),
            pl.BlockSpec((None, 1, width, inputs), lambda n: (n, 0, 0, 0)),
            pl.BlockSpec((9 * inputs, outputs), lambda n: (0, 0)),
        ],
        out_specs=[out_block, out_block],
        out_shape=[shape, shape],
        scratch_shapes=[pltpu.VMEM((rows + 1, width, inputs), jnp.float32)],
        compiler_params=pltpu.CompilerParams(
            dimension_semantics=("arbitrary",), vmem_limit_bytes=60 * 1024 * 1024
        ),
        cost_estimate=pl.CostEstimate(
            flops=2 * images * (rows // 2) * (width // 2) * 9 * inputs * outputs,
            transcendentals=0,
            bytes_accessed=maps.size * 2 + images * (rows // 2) * (width // 2) * outputs * 2,
        ),
    )(maps, upper_row, weight)


def second_kernel(*refs, rows, carry):
    if carry:
        left_ref, mid_ref, right_ref, weight_ref, grad_ref, prev_ref, out_ref, wgrad_ref = refs
    else:
        left_ref, mid_ref, right_ref, weight_ref, grad_ref, out_ref, wgrad_ref = refs
    step = pl.program_id(1)
    _, width, outputs = out_ref.shape
    inputs = mid_ref.shape[-1]
    sources = (left_ref, mid_ref, right_ref)
    patches = jnp.concatenate(
        [
            sources[tap % 3][pl.ds(step * rows + tap // 3, rows)].reshape(rows * width, inputs)
            for tap in range(9)
        ],
        axis=-1,
    )
    total = jnp.dot(patches, weight_ref[...], preferred_element_type=jnp.float32)
    if carry:
        total = total + prev_ref[...].reshape(rows * width, outputs)
    out_ref[...] = total.astype(out_ref.dtype).reshape(rows, width, outputs)
    term = lax.dot_general(
        patches, grad_ref[...], (((0,), (0,)), ((), ())), preferred_element_type=jnp.float32
    )

    @pl.when(step == 0)
    def _():
        wgrad_ref[...] = term

    @pl.when(step > 0)
    def _():
        wgrad_ref[...] += term


def second_stage(hidden, weight, grad, prev, out_dtype):
    owned, out_rows, out_cols, inputs = hidden.shape
    outputs = weight.shape[-1]
    rows = min(16, out_rows)
    row_padded = jnp.pad(hidden, ((0, 0), (1, 1), (0, 0), (0, 0)))
    shifted = [shift_cols_right(row_padded), row_padded, shift_cols_left(row_padded)]
    full = pl.BlockSpec((None, out_rows + 2, out_cols, inputs), lambda n, i: (n, 0, 0, 0))
    block = pl.BlockSpec((None, rows, out_cols, outputs), lambda n, i: (n, i, 0, 0))
    in_specs = [
        full,
        full,
        full,
        pl.BlockSpec((9 * inputs, outputs), lambda n, i: (0, 0)),
        pl.BlockSpec((None, rows * out_cols, outputs), lambda n, i: (n, i, 0)),
    ]
    operands = [*shifted, weight.reshape(9 * inputs, outputs), grad]
    if prev is not None:
        in_specs.append(block)
        operands.append(prev)
    flops = 4 * owned * out_rows * out_cols * 9 * inputs * outputs
    conv, wgrad_t = pl.pallas_call(
        functools.partial(second_kernel, rows=rows, carry=prev is not None),
        grid=(owned, out_rows // rows),
        in_specs=in_specs,
        out_specs=[block, pl.BlockSpec((None, 9 * inputs, outputs), lambda n, i: (n, 0, 0))],
        out_shape=[
            jax.ShapeDtypeStruct((owned, out_rows, out_cols, outputs), out_dtype),
            jax.ShapeDtypeStruct((owned, 9 * inputs, outputs), jnp.float32),
        ],
        compiler_params=pltpu.CompilerParams(
            dimension_semantics=("arbitrary", "arbitrary"), vmem_limit_bytes=60 * 1024 * 1024
        ),
        cost_estimate=pl.CostEstimate(
            flops=flops,
            transcendentals=0,
            bytes_accessed=hidden.size * 2 * 4 + owned * out_rows * out_cols * outputs * 8
            + owned * outputs * 9 * inputs * 4,
        ),
    )(*operands)
    return conv, wgrad_t.sum(axis=0).T


def halving_reduce_scatter(partial, axes):
    devices = lax.axis_size(axes)
    tiles = lax.axis_size(axes[-1])
    bits = devices.bit_length() - 1
    me = lax.axis_index(axes)
    core = tiles.bit_length() - 1
    order = [core] + [b for b in range(bits) if b > core] + [b for b in range(core)]
    rows = partial.shape[0] // devices
    buf = partial.reshape((2,) * bits + (rows,) + partial.shape[1:])
    remaining = list(range(bits - 1, -1, -1))
    for bit in order:
        axis = remaining.index(bit)
        mine = (me >> bit) & 1
        keep = lax.dynamic_index_in_dim(buf, mine, axis=axis, keepdims=False)
        send = lax.dynamic_index_in_dim(buf, 1 - mine, axis=axis, keepdims=False)
        pairs = [(i, i ^ (1 << bit)) for i in range(devices)]
        buf = keep + lax.ppermute(send, axes, pairs)
        remaining.pop(axis)
    return buf


def local(maps, first_weight, second_weight, out_grad):
    tiles = lax.axis_size("tile")
    images, height, width, inputs = maps.shape
    outputs = first_weight.shape[3]
    owned = images // tiles
    half_rows = height // 2
    chunks = 2
    part = outputs // chunks
    upper_row = shifted_2(maps[:, height - 1 : height], "tile", 1)
    grad = out_grad.reshape(owned, -1, outputs)
    conv = None
    pieces = []
    halves = first_stage(maps, upper_row, first_weight, part)
    for chunk in range(chunks):
        channels = slice(chunk * part, (chunk + 1) * part)
        local_hidden = halves[chunk]
        arrived = lax.all_to_all(
            local_hidden.reshape(tiles, owned, half_rows, width // 2, part),
            "tile",
            split_axis=0,
            concat_axis=2,
            tiled=True,
        )
        if conv is not None:
            arrived, conv = lax.optimization_barrier((arrived, conv))
        hidden = arrived.reshape(owned, half_rows * tiles, width // 2, part)
        last = chunk == chunks - 1
        conv, partial = second_stage(
            hidden, second_weight[:, :, channels], grad, conv, jnp.bfloat16 if last else jnp.float32
        )
        summed = halving_reduce_scatter(partial.reshape(outputs, 9 * part), ("group", "tile"))
        pieces.append(summed.reshape(-1, 9, part))
    weight_grad = jnp.concatenate(pieces, axis=-1).reshape(-1, 3, 3, outputs)
    return (conv, weight_grad)


def solution(mesh):
    return jax.shard_map(
        local,
        mesh=mesh,
        in_specs=(P("group", "tile", None, None), P(), P(), P(("group", "tile"), None, None, None)),
        out_specs=(P(("group", "tile"), None, None, None), P(("group", "tile"), None, None, None)),
        check_vma=False,
    )
```

```python
import functools

import jax
import jax.numpy as jnp
from jax import lax
from jax.experimental import pallas as pl
from jax.experimental.pallas import tpu as pltpu
from jax.sharding import PartitionSpec as P


def shifted_2(shard, axis, by):
    length = lax.axis_size(axis)
    pairs = [(i, i + by) for i in range(length) if 0 <= i + by < length]
    return lax.ppermute(shard, axis, pairs)


def shift_cols_right(slab):
    zero_col = jnp.zeros_like(slab[:, :, :1])
    return jnp.concatenate([zero_col, slab[:, :, :-1]], axis=2)


def shift_cols_left(slab):
    zero_col = jnp.zeros_like(slab[:, :, :1])
    return jnp.concatenate([slab[:, :, 1:], zero_col], axis=2)


def first_conv(source, upper_row, first_weight):
    images, rows, width, inputs = source.shape
    outputs = first_weight.shape[3]
    paired = source.reshape(images, rows // 2, 2, width // 2, 2 * inputs)
    even_rows = paired[:, :, 0]
    odd_rows = paired[:, :, 1]
    upper_paired = upper_row.reshape(images, 1, width // 2, 2 * inputs)
    odd_above = jnp.concatenate([upper_paired, odd_rows[:, :-1]], axis=1)
    sources = [odd_above, even_rows, odd_rows]
    total = jnp.zeros((images, rows // 2, width // 2, outputs), jnp.float32)
    for tap_row in range(3):
        wide_kernel = first_weight[tap_row, 1:3].reshape(2 * inputs, outputs)
        total = total + jnp.dot(sources[tap_row], wide_kernel, preferred_element_type=jnp.float32)
    halves = jnp.concatenate([piece[..., inputs:] for piece in sources], axis=-1)
    narrow_kernel = first_weight[:, 0].reshape(3 * inputs, outputs)
    total = total + jnp.dot(
        shift_cols_right(halves), narrow_kernel, preferred_element_type=jnp.float32
    )
    return jnp.maximum(total, 0.0).astype(jnp.bfloat16)


def first_kernel(x_ref, up_ref, w_ref, low_ref, high_ref, scratch):
    rows, width, inputs = x_ref.shape
    out_rows, out_cols = rows // 2, width // 2
    scratch[0] = up_ref[0].astype(jnp.float32)
    scratch[1:] = x_ref[...].astype(jnp.float32)
    first_col = lax.broadcasted_iota(jnp.int32, (out_rows, out_cols, inputs), 1) == 0
    pieces = []
    for tap_row in range(3):
        even = scratch[pl.ds(tap_row, out_rows, stride=2), pl.ds(0, out_cols, stride=2), :]
        odd = scratch[pl.ds(tap_row, out_rows, stride=2), pl.ds(1, out_cols, stride=2), :]
        left = jnp.where(first_col, 0.0, pltpu.roll(odd, 1, 1))
        pieces += [even, odd, left]
    patches = jnp.concatenate(
        [p.astype(jnp.bfloat16).reshape(out_rows * out_cols, inputs) for p in pieces], axis=-1
    )
    total = jnp.dot(patches, w_ref[...], preferred_element_type=jnp.float32)
    hidden = jnp.maximum(total, 0.0).astype(jnp.bfloat16).reshape(out_rows, out_cols, -1)
    half = low_ref.shape[-1]
    low_ref[...] = hidden[..., :half]
    high_ref[...] = hidden[..., half:]


def first_stage(maps, upper_row, first_weight, part):
    images, rows, width, inputs = maps.shape
    outputs = first_weight.shape[3]
    weight = first_weight[:, jnp.array([1, 2, 0])].reshape(9 * inputs, outputs)
    out_block = pl.BlockSpec((None, rows // 2, width // 2, part), lambda n: (n, 0, 0, 0))
    shape = jax.ShapeDtypeStruct((images, rows // 2, width // 2, part), jnp.bfloat16)
    return pl.pallas_call(
        first_kernel,
        grid=(images,),
        in_specs=[
            pl.BlockSpec((None, rows, width, inputs), lambda n: (n, 0, 0, 0)),
            pl.BlockSpec((None, 1, width, inputs), lambda n: (n, 0, 0, 0)),
            pl.BlockSpec((9 * inputs, outputs), lambda n: (0, 0)),
        ],
        out_specs=[out_block, out_block],
        out_shape=[shape, shape],
        scratch_shapes=[pltpu.VMEM((rows + 1, width, inputs), jnp.float32)],
        compiler_params=pltpu.CompilerParams(
            dimension_semantics=("arbitrary",), vmem_limit_bytes=60 * 1024 * 1024
        ),
        cost_estimate=pl.CostEstimate(
            flops=2 * images * (rows // 2) * (width // 2) * 9 * inputs * outputs,
            transcendentals=0,
            bytes_accessed=maps.size * 2 + images * (rows // 2) * (width // 2) * outputs * 2,
        ),
    )(maps, upper_row, weight)


def second_kernel(*refs, rows, carry, group):
    if carry:
        left_ref, mid_ref, right_ref, weight_ref, grad_ref, prev_ref, out_ref, wgrad_ref = refs
    else:
        left_ref, mid_ref, right_ref, weight_ref, grad_ref, out_ref, wgrad_ref = refs
    step = pl.program_id(1)
    _, width, outputs = out_ref.shape
    inputs = mid_ref.shape[-1]
    sources = (left_ref, mid_ref, right_ref)
    grad_t = grad_ref[...]
    if carry:
        acc = prev_ref[...].reshape(rows * width, outputs)
    else:
        acc = jnp.zeros((rows * width, outputs), jnp.float32)
    for first in range(0, 9, group):
        taps = range(first, min(first + group, 9))
        windows = [
            sources[tap % 3][pl.ds(step * rows + tap // 3, rows)].reshape(rows * width, inputs)
            for tap in taps
        ]
        window = windows[0] if len(windows) == 1 else jnp.concatenate(windows, axis=-1)
        lanes = slice(first * inputs, (first + len(windows)) * inputs)
        acc = acc + jnp.dot(window, weight_ref[lanes, :], preferred_element_type=jnp.float32)
        term = jnp.dot(grad_t, window, preferred_element_type=jnp.float32)

        @pl.when(step == 0)
        def _():
            wgrad_ref[:, lanes] = term

        @pl.when(step > 0)
        def _():
            wgrad_ref[:, lanes] += term

    out_ref[...] = acc.astype(out_ref.dtype).reshape(rows, width, outputs)


def second_stage(hidden, weight, grad_t, prev, out_dtype):
    owned, out_rows, out_cols, inputs = hidden.shape
    outputs = weight.shape[-1]
    rows = min(16, out_rows)
    row_padded = jnp.pad(hidden, ((0, 0), (1, 1), (0, 0), (0, 0)))
    shifted = [shift_cols_right(row_padded), row_padded, shift_cols_left(row_padded)]
    full = pl.BlockSpec((None, out_rows + 2, out_cols, inputs), lambda n, i: (n, 0, 0, 0))
    block = pl.BlockSpec((None, rows, out_cols, outputs), lambda n, i: (n, i, 0, 0))
    in_specs = [
        full,
        full,
        full,
        pl.BlockSpec((9 * inputs, outputs), lambda n, i: (0, 0)),
        pl.BlockSpec((None, outputs, rows * out_cols), lambda n, i: (n, 0, i)),
    ]
    operands = [*shifted, weight.reshape(9 * inputs, outputs), grad_t]
    if prev is not None:
        in_specs.append(block)
        operands.append(prev)
    flops = 4 * owned * out_rows * out_cols * 9 * inputs * outputs
    return pl.pallas_call(
        functools.partial(second_kernel, rows=rows, carry=prev is not None, group=max(1, 256 // inputs)),
        grid=(owned, out_rows // rows),
        in_specs=in_specs,
        out_specs=[block, pl.BlockSpec((None, outputs, 9 * inputs), lambda n, i: (n, 0, 0))],
        out_shape=[
            jax.ShapeDtypeStruct((owned, out_rows, out_cols, outputs), out_dtype),
            jax.ShapeDtypeStruct((owned, outputs, 9 * inputs), jnp.float32),
        ],
        compiler_params=pltpu.CompilerParams(
            dimension_semantics=("arbitrary", "arbitrary"), vmem_limit_bytes=60 * 1024 * 1024
        ),
        cost_estimate=pl.CostEstimate(
            flops=flops,
            transcendentals=0,
            bytes_accessed=hidden.size * 2 * 4 + owned * out_rows * out_cols * outputs * 8
            + owned * outputs * 9 * inputs * 4,
        ),
    )(*operands)


def halving_reduce_scatter(partial, axes, swap=False):
    devices = lax.axis_size(axes)
    tiles = lax.axis_size(axes[-1])
    bits = devices.bit_length() - 1
    me = lax.axis_index(axes)
    core = tiles.bit_length() - 1
    high = [b for b in range(bits) if b > core]
    low = [b for b in range(core)]
    order = [core] + (low[:1] + high + low[1:] if swap else high + low)
    rows = partial.shape[0] // devices
    buf = partial.reshape((2,) * bits + (rows,) + partial.shape[1:])
    remaining = list(range(bits - 1, -1, -1))
    for bit in order:
        axis = remaining.index(bit)
        mine = (me >> bit) & 1
        keep = lax.dynamic_index_in_dim(buf, mine, axis=axis, keepdims=False)
        send = lax.dynamic_index_in_dim(buf, 1 - mine, axis=axis, keepdims=False)
        pairs = [(i, i ^ (1 << bit)) for i in range(devices)]
        buf = keep + lax.ppermute(send, axes, pairs)
        remaining.pop(axis)
    return buf


def local(maps, first_weight, second_weight, out_grad):
    tiles = lax.axis_size("tile")
    images, height, width, inputs = maps.shape
    outputs = first_weight.shape[3]
    owned = images // tiles
    half_rows = height // 2
    chunks = 2
    part = outputs // chunks
    upper_row = shifted_2(maps[:, height - 1 : height], "tile", 1)
    grad_t = out_grad.reshape(owned, -1, outputs).transpose(0, 2, 1)
    conv = None
    pieces = []
    halves = first_stage(maps, upper_row, first_weight, part)
    for chunk in range(chunks):
        channels = slice(chunk * part, (chunk + 1) * part)
        local_hidden = halves[chunk]
        arrived = lax.all_to_all(
            local_hidden.reshape(tiles, owned, half_rows, width // 2, part),
            "tile",
            split_axis=0,
            concat_axis=2,
            tiled=True,
        )
        if conv is not None:
            arrived, conv = lax.optimization_barrier((arrived, conv))
        hidden = arrived.reshape(owned, half_rows * tiles, width // 2, part)
        last = chunk == chunks - 1
        conv, partial = second_stage(
            hidden, second_weight[:, :, channels], grad_t, conv, jnp.bfloat16 if last else jnp.float32
        )
        summed = halving_reduce_scatter(
            partial.sum(axis=0).reshape(outputs, 9 * part), ("group", "tile"), swap=chunk % 2 == 1
        )
        pieces.append(summed.reshape(-1, 9, part))
    weight_grad = jnp.concatenate(pieces, axis=-1).reshape(-1, 3, 3, outputs)
    return (conv, weight_grad)


def solution(mesh):
    return jax.shard_map(
        local,
        mesh=mesh,
        in_specs=(P("group", "tile", None, None), P(), P(), P(("group", "tile"), None, None, None)),
        out_specs=(P(("group", "tile"), None, None, None), P(("group", "tile"), None, None, None)),
        check_vma=False,
    )
```

```python
import functools

import jax
import jax.numpy as jnp
from jax import lax
from jax.experimental import pallas as pl
from jax.experimental.pallas import tpu as pltpu
from jax.sharding import PartitionSpec as P


def shifted_2(shard, axis, by):
    length = lax.axis_size(axis)
    pairs = [(i, i + by) for i in range(length) if 0 <= i + by < length]
    return lax.ppermute(shard, axis, pairs)


def shift_cols_right(slab):
    zero_col = jnp.zeros_like(slab[:, :, :1])
    return jnp.concatenate([zero_col, slab[:, :, :-1]], axis=2)


def shift_cols_left(slab):
    zero_col = jnp.zeros_like(slab[:, :, :1])
    return jnp.concatenate([slab[:, :, 1:], zero_col], axis=2)


def first_conv(source, upper_row, first_weight):
    images, rows, width, inputs = source.shape
    outputs = first_weight.shape[3]
    paired = source.reshape(images, rows // 2, 2, width // 2, 2 * inputs)
    even_rows = paired[:, :, 0]
    odd_rows = paired[:, :, 1]
    upper_paired = upper_row.reshape(images, 1, width // 2, 2 * inputs)
    odd_above = jnp.concatenate([upper_paired, odd_rows[:, :-1]], axis=1)
    sources = [odd_above, even_rows, odd_rows]
    total = jnp.zeros((images, rows // 2, width // 2, outputs), jnp.float32)
    for tap_row in range(3):
        wide_kernel = first_weight[tap_row, 1:3].reshape(2 * inputs, outputs)
        total = total + jnp.dot(sources[tap_row], wide_kernel, preferred_element_type=jnp.float32)
    halves = jnp.concatenate([piece[..., inputs:] for piece in sources], axis=-1)
    narrow_kernel = first_weight[:, 0].reshape(3 * inputs, outputs)
    total = total + jnp.dot(
        shift_cols_right(halves), narrow_kernel, preferred_element_type=jnp.float32
    )
    return jnp.maximum(total, 0.0).astype(jnp.bfloat16)


def first_kernel(x_ref, up_ref, w_ref, low_ref, high_ref, scratch):
    rows, width, inputs = x_ref.shape
    out_rows, out_cols = rows // 2, width // 2
    scratch[0] = up_ref[0].astype(jnp.float32)
    scratch[1:] = x_ref[...].astype(jnp.float32)
    first_col = lax.broadcasted_iota(jnp.int32, (out_rows, out_cols, inputs), 1) == 0
    pieces = []
    for tap_row in range(3):
        even = scratch[pl.ds(tap_row, out_rows, stride=2), pl.ds(0, out_cols, stride=2), :]
        odd = scratch[pl.ds(tap_row, out_rows, stride=2), pl.ds(1, out_cols, stride=2), :]
        left = jnp.where(first_col, 0.0, pltpu.roll(odd, 1, 1))
        pieces += [even, odd, left]
    patches = jnp.concatenate(
        [p.astype(jnp.bfloat16).reshape(out_rows * out_cols, inputs) for p in pieces], axis=-1
    )
    total = jnp.dot(patches, w_ref[...], preferred_element_type=jnp.float32)
    hidden = jnp.maximum(total, 0.0).astype(jnp.bfloat16).reshape(out_rows, out_cols, -1)
    half = low_ref.shape[-1]
    low_ref[...] = hidden[..., :half]
    high_ref[...] = hidden[..., half:]


def first_stage(maps, upper_row, first_weight, part):
    images, rows, width, inputs = maps.shape
    outputs = first_weight.shape[3]
    weight = first_weight[:, jnp.array([1, 2, 0])].reshape(9 * inputs, outputs)
    out_block = pl.BlockSpec((None, rows // 2, width // 2, part), lambda n: (n, 0, 0, 0))
    shape = jax.ShapeDtypeStruct((images, rows // 2, width // 2, part), jnp.bfloat16)
    return pl.pallas_call(
        first_kernel,
        grid=(images,),
        in_specs=[
            pl.BlockSpec((None, rows, width, inputs), lambda n: (n, 0, 0, 0)),
            pl.BlockSpec((None, 1, width, inputs), lambda n: (n, 0, 0, 0)),
            pl.BlockSpec((9 * inputs, outputs), lambda n: (0, 0)),
        ],
        out_specs=[out_block, out_block],
        out_shape=[shape, shape],
        scratch_shapes=[pltpu.VMEM((rows + 1, width, inputs), jnp.float32)],
        compiler_params=pltpu.CompilerParams(
            dimension_semantics=("arbitrary",), vmem_limit_bytes=60 * 1024 * 1024
        ),
        cost_estimate=pl.CostEstimate(
            flops=2 * images * (rows // 2) * (width // 2) * 9 * inputs * outputs,
            transcendentals=0,
            bytes_accessed=maps.size * 2 + images * (rows // 2) * (width // 2) * outputs * 2,
        ),
    )(maps, upper_row, weight)


def second_kernel(*refs, rows, carry):
    if carry:
        left_ref, mid_ref, right_ref, weight_ref, grad_ref, prev_ref, out_ref, wgrad_ref, acc_ref = refs
    else:
        left_ref, mid_ref, right_ref, weight_ref, grad_ref, out_ref, wgrad_ref, acc_ref = refs
    step = pl.program_id(1)
    _, width, outputs = out_ref.shape
    inputs = mid_ref.shape[-1]
    sources = (left_ref, mid_ref, right_ref)
    patches = jnp.concatenate(
        [
            sources[tap % 3][pl.ds(step * rows + tap // 3, rows)].reshape(rows * width, inputs)
            for tap in range(9)
        ],
        axis=-1,
    )
    total = jnp.dot(patches, weight_ref[...], preferred_element_type=jnp.float32)
    if carry:
        total = total + prev_ref[...].reshape(rows * width, outputs)
    out_ref[...] = total.astype(out_ref.dtype).reshape(rows, width, outputs)
    term = lax.dot_general(
        patches, grad_ref[...], (((0,), (0,)), ((), ())), preferred_element_type=jnp.float32
    )

    @pl.when(step == 0)
    def _():
        acc_ref[...] = term

    @pl.when(step > 0)
    def _():
        acc_ref[...] += term

    @pl.when(step == pl.num_programs(1) - 1)
    def _():
        wgrad_ref[...] = acc_ref[...].T


def second_stage(hidden, weight, grad, prev, out_dtype):
    owned, out_rows, out_cols, inputs = hidden.shape
    outputs = weight.shape[-1]
    rows = min(16, out_rows)
    row_padded = jnp.pad(hidden, ((0, 0), (1, 1), (0, 0), (0, 0)))
    shifted = [shift_cols_right(row_padded), row_padded, shift_cols_left(row_padded)]
    full = pl.BlockSpec((None, out_rows + 2, out_cols, inputs), lambda n, i: (n, 0, 0, 0))
    block = pl.BlockSpec((None, rows, out_cols, outputs), lambda n, i: (n, i, 0, 0))
    in_specs = [
        full,
        full,
        full,
        pl.BlockSpec((9 * inputs, outputs), lambda n, i: (0, 0)),
        pl.BlockSpec((None, rows * out_cols, outputs), lambda n, i: (n, i, 0)),
    ]
    operands = [*shifted, weight.reshape(9 * inputs, outputs), grad]
    if prev is not None:
        in_specs.append(block)
        operands.append(prev)
    flops = 4 * owned * out_rows * out_cols * 9 * inputs * outputs
    return pl.pallas_call(
        functools.partial(second_kernel, rows=rows, carry=prev is not None),
        grid=(owned, out_rows // rows),
        in_specs=in_specs,
        out_specs=[block, pl.BlockSpec((None, outputs, 9 * inputs), lambda n, i: (n, 0, 0))],
        out_shape=[
            jax.ShapeDtypeStruct((owned, out_rows, out_cols, outputs), out_dtype),
            jax.ShapeDtypeStruct((owned, outputs, 9 * inputs), jnp.float32),
        ],
        scratch_shapes=[pltpu.VMEM((9 * inputs, outputs), jnp.float32)],
        compiler_params=pltpu.CompilerParams(
            dimension_semantics=("arbitrary", "arbitrary"), vmem_limit_bytes=60 * 1024 * 1024
        ),
        cost_estimate=pl.CostEstimate(
            flops=flops,
            transcendentals=0,
            bytes_accessed=hidden.size * 2 * 4 + owned * out_rows * out_cols * outputs * 8
            + owned * outputs * 9 * inputs * 4,
        ),
    )(*operands)


def halving_reduce_scatter(partial, axes, swap=False):
    devices = lax.axis_size(axes)
    tiles = lax.axis_size(axes[-1])
    bits = devices.bit_length() - 1
    me = lax.axis_index(axes)
    core = tiles.bit_length() - 1
    high = [b for b in range(bits) if b > core]
    low = [b for b in range(core)]
    order = [core] + (low[:1] + high + low[1:] if swap else high + low)
    rows = partial.shape[0] // devices
    buf = partial.reshape((2,) * bits + (rows,) + partial.shape[1:])
    remaining = list(range(bits - 1, -1, -1))
    for bit in order:
        axis = remaining.index(bit)
        mine = (me >> bit) & 1
        keep = lax.dynamic_index_in_dim(buf, mine, axis=axis, keepdims=False)
        send = lax.dynamic_index_in_dim(buf, 1 - mine, axis=axis, keepdims=False)
        pairs = [(i, i ^ (1 << bit)) for i in range(devices)]
        buf = keep + lax.ppermute(send, axes, pairs)
        remaining.pop(axis)
    return buf


def local(maps, first_weight, second_weight, out_grad):
    tiles = lax.axis_size("tile")
    images, height, width, inputs = maps.shape
    outputs = first_weight.shape[3]
    owned = images // tiles
    half_rows = height // 2
    chunks = 2
    part = outputs // chunks
    upper_row = shifted_2(maps[:, height - 1 : height], "tile", 1)
    grad = out_grad.reshape(owned, -1, outputs)
    conv = None
    pieces = []
    halves = first_stage(maps, upper_row, first_weight, part)
    for chunk in range(chunks):
        channels = slice(chunk * part, (chunk + 1) * part)
        local_hidden = halves[chunk]
        arrived = lax.all_to_all(
            local_hidden.reshape(tiles, owned, half_rows, width // 2, part),
            "tile",
            split_axis=0,
            concat_axis=2,
            tiled=True,
        )
        if conv is not None:
            arrived, conv = lax.optimization_barrier((arrived, conv))
        hidden = arrived.reshape(owned, half_rows * tiles, width // 2, part)
        last = chunk == chunks - 1
        conv, partial = second_stage(
            hidden, second_weight[:, :, channels], grad, conv, jnp.bfloat16 if last else jnp.float32
        )
        summed = halving_reduce_scatter(
            partial.sum(axis=0).reshape(outputs, 9 * part), ("group", "tile"), swap=chunk % 2 == 1
        )
        pieces.append(summed.reshape(-1, 9, part))
    weight_grad = jnp.concatenate(pieces, axis=-1).reshape(-1, 3, 3, outputs)
    return (conv, weight_grad)


def solution(mesh):
    return jax.shard_map(
        local,
        mesh=mesh,
        in_specs=(P("group", "tile", None, None), P(), P(), P(("group", "tile"), None, None, None)),
        out_specs=(P(("group", "tile"), None, None, None), P(("group", "tile"), None, None, None)),
        check_vma=False,
    )
```

```python
import functools

import jax
import jax.numpy as jnp
from jax import lax
from jax.experimental import pallas as pl
from jax.experimental.pallas import tpu as pltpu
from jax.sharding import PartitionSpec as P


def shifted_2(shard, axis, by):
    length = lax.axis_size(axis)
    pairs = [(i, i + by) for i in range(length) if 0 <= i + by < length]
    return lax.ppermute(shard, axis, pairs)


def shift_cols_right(slab):
    zero_col = jnp.zeros_like(slab[:, :, :1])
    return jnp.concatenate([zero_col, slab[:, :, :-1]], axis=2)


def shift_cols_left(slab):
    zero_col = jnp.zeros_like(slab[:, :, :1])
    return jnp.concatenate([slab[:, :, 1:], zero_col], axis=2)


def first_conv(source, upper_row, first_weight):
    images, rows, width, inputs = source.shape
    outputs = first_weight.shape[3]
    paired = source.reshape(images, rows // 2, 2, width // 2, 2 * inputs)
    even_rows = paired[:, :, 0]
    odd_rows = paired[:, :, 1]
    upper_paired = upper_row.reshape(images, 1, width // 2, 2 * inputs)
    odd_above = jnp.concatenate([upper_paired, odd_rows[:, :-1]], axis=1)
    sources = [odd_above, even_rows, odd_rows]
    total = jnp.zeros((images, rows // 2, width // 2, outputs), jnp.float32)
    for tap_row in range(3):
        wide_kernel = first_weight[tap_row, 1:3].reshape(2 * inputs, outputs)
        total = total + jnp.dot(sources[tap_row], wide_kernel, preferred_element_type=jnp.float32)
    halves = jnp.concatenate([piece[..., inputs:] for piece in sources], axis=-1)
    narrow_kernel = first_weight[:, 0].reshape(3 * inputs, outputs)
    total = total + jnp.dot(
        shift_cols_right(halves), narrow_kernel, preferred_element_type=jnp.float32
    )
    return jnp.maximum(total, 0.0).astype(jnp.bfloat16)


def first_kernel(x_ref, up_ref, w_ref, low_ref, high_ref, scratch):
    rows, width, inputs = x_ref.shape
    out_rows, out_cols = rows // 2, width // 2
    scratch[0] = up_ref[0].astype(jnp.float32)
    scratch[1:] = x_ref[...].astype(jnp.float32)
    first_col = lax.broadcasted_iota(jnp.int32, (out_rows, out_cols, inputs), 1) == 0
    pieces = []
    for tap_row in range(3):
        even = scratch[pl.ds(tap_row, out_rows, stride=2), pl.ds(0, out_cols, stride=2), :]
        odd = scratch[pl.ds(tap_row, out_rows, stride=2), pl.ds(1, out_cols, stride=2), :]
        left = jnp.where(first_col, 0.0, pltpu.roll(odd, 1, 1))
        pieces += [even, odd, left]
    patches = jnp.concatenate(
        [p.astype(jnp.bfloat16).reshape(out_rows * out_cols, inputs) for p in pieces], axis=-1
    )
    total = jnp.dot(patches, w_ref[...], preferred_element_type=jnp.float32)
    hidden = jnp.maximum(total, 0.0).astype(jnp.bfloat16).reshape(out_rows, out_cols, -1)
    half = low_ref.shape[-1]
    low_ref[...] = hidden[..., :half]
    high_ref[...] = hidden[..., half:]


def first_stage(maps, upper_row, first_weight, part):
    images, rows, width, inputs = maps.shape
    outputs = first_weight.shape[3]
    weight = first_weight[:, jnp.array([1, 2, 0])].reshape(9 * inputs, outputs)
    out_block = pl.BlockSpec((None, rows // 2, width // 2, part), lambda n: (n, 0, 0, 0))
    shape = jax.ShapeDtypeStruct((images, rows // 2, width // 2, part), jnp.bfloat16)
    return pl.pallas_call(
        first_kernel,
        grid=(images,),
        in_specs=[
            pl.BlockSpec((None, rows, width, inputs), lambda n: (n, 0, 0, 0)),
            pl.BlockSpec((None, 1, width, inputs), lambda n: (n, 0, 0, 0)),
            pl.BlockSpec((9 * inputs, outputs), lambda n: (0, 0)),
        ],
        out_specs=[out_block, out_block],
        out_shape=[shape, shape],
        scratch_shapes=[pltpu.VMEM((rows + 1, width, inputs), jnp.float32)],
        compiler_params=pltpu.CompilerParams(
            dimension_semantics=("arbitrary",), vmem_limit_bytes=60 * 1024 * 1024
        ),
        cost_estimate=pl.CostEstimate(
            flops=2 * images * (rows // 2) * (width // 2) * 9 * inputs * outputs,
            transcendentals=0,
            bytes_accessed=maps.size * 2 + images * (rows // 2) * (width // 2) * outputs * 2,
        ),
    )(maps, upper_row, weight)


def second_kernel(*refs, rows, carry):
    if carry:
        left_ref, mid_ref, right_ref, weight_ref, grad_ref, prev_ref, out_ref, wgrad_ref, acc_ref = refs
    else:
        left_ref, mid_ref, right_ref, weight_ref, grad_ref, out_ref, wgrad_ref, acc_ref = refs
    step = pl.program_id(1)
    _, width, outputs = out_ref.shape
    inputs = mid_ref.shape[-1]
    sources = (left_ref, mid_ref, right_ref)
    patches = jnp.concatenate(
        [
            sources[tap % 3][pl.ds(step * rows + tap // 3, rows)].reshape(rows * width, inputs)
            for tap in range(9)
        ],
        axis=-1,
    )
    total = jnp.dot(patches, weight_ref[...], preferred_element_type=jnp.float32)
    if carry:
        total = total + prev_ref[...].reshape(rows * width, outputs)
    out_ref[...] = total.astype(out_ref.dtype).reshape(rows, width, outputs)
    term = lax.dot_general(
        patches, grad_ref[...], (((0,), (0,)), ((), ())), preferred_element_type=jnp.float32
    )

    @pl.when(step == 0)
    def _():
        acc_ref[...] = term

    @pl.when(step > 0)
    def _():
        acc_ref[...] += term

    @pl.when(step == pl.num_programs(1) - 1)
    def _():
        wgrad_ref[...] = acc_ref[...].T


def second_stage(hidden, weight, grad, prev, out_dtype):
    owned, out_rows, out_cols, inputs = hidden.shape
    outputs = weight.shape[-1]
    rows = min(16, out_rows)
    row_padded = jnp.pad(hidden, ((0, 0), (1, 1), (0, 0), (0, 0)))
    shifted = [shift_cols_right(row_padded), row_padded, shift_cols_left(row_padded)]
    full = pl.BlockSpec((None, out_rows + 2, out_cols, inputs), lambda n, i: (n, 0, 0, 0))
    block = pl.BlockSpec((None, rows, out_cols, outputs), lambda n, i: (n, i, 0, 0))
    in_specs = [
        full,
        full,
        full,
        pl.BlockSpec((9 * inputs, outputs), lambda n, i: (0, 0)),
        pl.BlockSpec((None, rows * out_cols, outputs), lambda n, i: (n, i, 0)),
    ]
    operands = [*shifted, weight.reshape(9 * inputs, outputs), grad]
    if prev is not None:
        in_specs.append(block)
        operands.append(prev)
    flops = 4 * owned * out_rows * out_cols * 9 * inputs * outputs
    return pl.pallas_call(
        functools.partial(second_kernel, rows=rows, carry=prev is not None),
        grid=(owned, out_rows // rows),
        in_specs=in_specs,
        out_specs=[block, pl.BlockSpec((None, outputs, 9 * inputs), lambda n, i: (n, 0, 0))],
        out_shape=[
            jax.ShapeDtypeStruct((owned, out_rows, out_cols, outputs), out_dtype),
            jax.ShapeDtypeStruct((owned, outputs, 9 * inputs), jnp.float32),
        ],
        scratch_shapes=[pltpu.VMEM((9 * inputs, outputs), jnp.float32)],
        compiler_params=pltpu.CompilerParams(
            dimension_semantics=("arbitrary", "arbitrary"), vmem_limit_bytes=60 * 1024 * 1024
        ),
        cost_estimate=pl.CostEstimate(
            flops=flops,
            transcendentals=0,
            bytes_accessed=hidden.size * 2 * 4 + owned * out_rows * out_cols * outputs * 8
            + owned * outputs * 9 * inputs * 4,
        ),
    )(*operands)


def halving_reduce_scatter(partials, axes):
    devices = lax.axis_size(axes)
    tiles = lax.axis_size(axes[-1])
    bits = devices.bit_length() - 1
    me = lax.axis_index(axes)
    core = tiles.bit_length() - 1
    high = [b for b in range(bits) if b > core]
    low = [b for b in range(core)]
    orders = [[core] + (low[:1] + high + low[1:] if index % 2 else high + low) for index in range(len(partials))]
    bufs = []
    for partial in partials:
        rows = partial.shape[0] // devices
        bufs.append(partial.reshape((2,) * bits + (rows,) + partial.shape[1:]))
    remaining = [list(range(bits - 1, -1, -1)) for _ in partials]
    for step in range(bits):
        keeps, sends = [], []
        for index, buf in enumerate(bufs):
            bit = orders[index][step]
            axis = remaining[index].index(bit)
            mine = (me >> bit) & 1
            keeps.append(lax.dynamic_index_in_dim(buf, mine, axis=axis, keepdims=False))
            sends.append(lax.dynamic_index_in_dim(buf, 1 - mine, axis=axis, keepdims=False))
            remaining[index].pop(axis)
        groups = {}
        for index in range(len(bufs)):
            groups.setdefault(orders[index][step], []).append(index)
        arrived = [None] * len(bufs)
        for bit, members in groups.items():
            pairs = [(i, i ^ (1 << bit)) for i in range(devices)]
            if len(members) == 1:
                arrived[members[0]] = lax.ppermute(sends[members[0]], axes, pairs)
            else:
                moved = lax.ppermute(jnp.stack([sends[m] for m in members]), axes, pairs)
                for position, m in enumerate(members):
                    arrived[m] = moved[position]
        bufs = [keep + got for keep, got in zip(keeps, arrived)]
    return bufs


def local(maps, first_weight, second_weight, out_grad):
    tiles = lax.axis_size("tile")
    images, height, width, inputs = maps.shape
    outputs = first_weight.shape[3]
    owned = images // tiles
    half_rows = height // 2
    chunks = 2
    part = outputs // chunks
    upper_row = shifted_2(maps[:, height - 1 : height], "tile", 1)
    grad = out_grad.reshape(owned, -1, outputs)
    conv = None
    partials = []
    halves = first_stage(maps, upper_row, first_weight, part)
    for chunk in range(chunks):
        channels = slice(chunk * part, (chunk + 1) * part)
        local_hidden = halves[chunk]
        arrived = lax.all_to_all(
            local_hidden.reshape(tiles, owned, half_rows, width // 2, part),
            "tile",
            split_axis=0,
            concat_axis=2,
            tiled=True,
        )
        if conv is not None:
            arrived, conv = lax.optimization_barrier((arrived, conv))
        hidden = arrived.reshape(owned, half_rows * tiles, width // 2, part)
        last = chunk == chunks - 1
        conv, partial = second_stage(
            hidden, second_weight[:, :, channels], grad, conv, jnp.bfloat16 if last else jnp.float32
        )
        partials.append(partial.sum(axis=0).reshape(outputs, 9 * part))
    pieces = [summed.reshape(-1, 9, part) for summed in halving_reduce_scatter(partials, ("group", "tile"))]
    weight_grad = jnp.concatenate(pieces, axis=-1).reshape(-1, 3, 3, outputs)
    return (conv, weight_grad)


def solution(mesh):
    return jax.shard_map(
        local,
        mesh=mesh,
        in_specs=(P("group", "tile", None, None), P(), P(), P(("group", "tile"), None, None, None)),
        out_specs=(P(("group", "tile"), None, None, None), P(("group", "tile"), None, None, None)),
        check_vma=False,
    )
```

```python
import functools

import jax
import jax.numpy as jnp
from jax import lax
from jax.experimental import pallas as pl
from jax.experimental.pallas import tpu as pltpu
from jax.sharding import PartitionSpec as P


def shifted_2(shard, axis, by):
    length = lax.axis_size(axis)
    pairs = [(i, i + by) for i in range(length) if 0 <= i + by < length]
    return lax.ppermute(shard, axis, pairs)


def shift_cols_right(slab):
    zero_col = jnp.zeros_like(slab[:, :, :1])
    return jnp.concatenate([zero_col, slab[:, :, :-1]], axis=2)


def shift_cols_left(slab):
    zero_col = jnp.zeros_like(slab[:, :, :1])
    return jnp.concatenate([slab[:, :, 1:], zero_col], axis=2)


def first_conv(source, upper_row, first_weight):
    images, rows, width, inputs = source.shape
    outputs = first_weight.shape[3]
    paired = source.reshape(images, rows // 2, 2, width // 2, 2 * inputs)
    even_rows = paired[:, :, 0]
    odd_rows = paired[:, :, 1]
    upper_paired = upper_row.reshape(images, 1, width // 2, 2 * inputs)
    odd_above = jnp.concatenate([upper_paired, odd_rows[:, :-1]], axis=1)
    sources = [odd_above, even_rows, odd_rows]
    total = jnp.zeros((images, rows // 2, width // 2, outputs), jnp.float32)
    for tap_row in range(3):
        wide_kernel = first_weight[tap_row, 1:3].reshape(2 * inputs, outputs)
        total = total + jnp.dot(sources[tap_row], wide_kernel, preferred_element_type=jnp.float32)
    halves = jnp.concatenate([piece[..., inputs:] for piece in sources], axis=-1)
    narrow_kernel = first_weight[:, 0].reshape(3 * inputs, outputs)
    total = total + jnp.dot(
        shift_cols_right(halves), narrow_kernel, preferred_element_type=jnp.float32
    )
    return jnp.maximum(total, 0.0).astype(jnp.bfloat16)


def first_kernel(x_ref, up_ref, w_ref, low_ref, high_ref, scratch):
    rows, width, inputs = x_ref.shape
    out_rows, out_cols = rows // 2, width // 2
    scratch[0] = up_ref[0].astype(jnp.float32)
    scratch[1:] = x_ref[...].astype(jnp.float32)
    first_col = lax.broadcasted_iota(jnp.int32, (out_rows, out_cols, inputs), 1) == 0
    pieces = []
    for tap_row in range(3):
        even = scratch[pl.ds(tap_row, out_rows, stride=2), pl.ds(0, out_cols, stride=2), :]
        odd = scratch[pl.ds(tap_row, out_rows, stride=2), pl.ds(1, out_cols, stride=2), :]
        left = jnp.where(first_col, 0.0, pltpu.roll(odd, 1, 1))
        pieces += [even, odd, left]
    patches = jnp.concatenate(
        [p.astype(jnp.bfloat16).reshape(out_rows * out_cols, inputs) for p in pieces], axis=-1
    )
    total = jnp.dot(patches, w_ref[...], preferred_element_type=jnp.float32)
    hidden = jnp.maximum(total, 0.0).astype(jnp.bfloat16).reshape(out_rows, out_cols, -1)
    half = low_ref.shape[-1]
    low_ref[...] = hidden[..., :half]
    high_ref[...] = hidden[..., half:]


def first_stage(maps, upper_row, first_weight, part):
    images, rows, width, inputs = maps.shape
    outputs = first_weight.shape[3]
    weight = first_weight[:, jnp.array([1, 2, 0])].reshape(9 * inputs, outputs)
    out_block = pl.BlockSpec((None, rows // 2, width // 2, part), lambda n: (n, 0, 0, 0))
    shape = jax.ShapeDtypeStruct((images, rows // 2, width // 2, part), jnp.bfloat16)
    return pl.pallas_call(
        first_kernel,
        grid=(images,),
        in_specs=[
            pl.BlockSpec((None, rows, width, inputs), lambda n: (n, 0, 0, 0)),
            pl.BlockSpec((None, 1, width, inputs), lambda n: (n, 0, 0, 0)),
            pl.BlockSpec((9 * inputs, outputs), lambda n: (0, 0)),
        ],
        out_specs=[out_block, out_block],
        out_shape=[shape, shape],
        scratch_shapes=[pltpu.VMEM((rows + 1, width, inputs), jnp.float32)],
        compiler_params=pltpu.CompilerParams(
            dimension_semantics=("arbitrary",), vmem_limit_bytes=60 * 1024 * 1024
        ),
        cost_estimate=pl.CostEstimate(
            flops=2 * images * (rows // 2) * (width // 2) * 9 * inputs * outputs,
            transcendentals=0,
            bytes_accessed=maps.size * 2 + images * (rows // 2) * (width // 2) * outputs * 2,
        ),
    )(maps, upper_row, weight)


def second_kernel(*refs, rows, carry):
    if carry:
        left_ref, mid_ref, right_ref, weight_ref, grad_ref, prev_ref, out_ref, wgrad_ref, acc_ref = refs
    else:
        left_ref, mid_ref, right_ref, weight_ref, grad_ref, out_ref, wgrad_ref, acc_ref = refs
    step = pl.program_id(1)
    _, width, outputs = out_ref.shape
    inputs = mid_ref.shape[-1]
    sources = (left_ref, mid_ref, right_ref)
    patches = jnp.concatenate(
        [
            sources[tap % 3][pl.ds(step * rows + tap // 3, rows)].reshape(rows * width, inputs)
            for tap in range(9)
        ],
        axis=-1,
    )
    total = jnp.dot(patches, weight_ref[...], preferred_element_type=jnp.float32)
    if carry:
        total = total + prev_ref[...].reshape(rows * width, outputs)
    out_ref[...] = total.astype(out_ref.dtype).reshape(rows, width, outputs)
    term = lax.dot_general(
        patches, grad_ref[...], (((0,), (0,)), ((), ())), preferred_element_type=jnp.float32
    )

    @pl.when(step == 0)
    def _():
        acc_ref[...] = term

    @pl.when(step > 0)
    def _():
        acc_ref[...] += term

    @pl.when(step == pl.num_programs(1) - 1)
    def _():
        wgrad_ref[...] = acc_ref[...].T


def second_stage(hidden, weight, grad, prev, out_dtype):
    owned, out_rows, out_cols, inputs = hidden.shape
    outputs = weight.shape[-1]
    rows = min(16, out_rows)
    row_padded = jnp.pad(hidden, ((0, 0), (1, 1), (0, 0), (0, 0)))
    shifted = [shift_cols_right(row_padded), row_padded, shift_cols_left(row_padded)]
    full = pl.BlockSpec((None, out_rows + 2, out_cols, inputs), lambda n, i: (n, 0, 0, 0))
    block = pl.BlockSpec((None, rows, out_cols, outputs), lambda n, i: (n, i, 0, 0))
    in_specs = [
        full,
        full,
        full,
        pl.BlockSpec((9 * inputs, outputs), lambda n, i: (0, 0)),
        pl.BlockSpec((None, rows * out_cols, outputs), lambda n, i: (n, i, 0)),
    ]
    operands = [*shifted, weight.reshape(9 * inputs, outputs), grad]
    if prev is not None:
        in_specs.append(block)
        operands.append(prev)
    flops = 4 * owned * out_rows * out_cols * 9 * inputs * outputs
    return pl.pallas_call(
        functools.partial(second_kernel, rows=rows, carry=prev is not None),
        grid=(owned, out_rows // rows),
        in_specs=in_specs,
        out_specs=[block, pl.BlockSpec((None, outputs, 9 * inputs), lambda n, i: (n, 0, 0))],
        out_shape=[
            jax.ShapeDtypeStruct((owned, out_rows, out_cols, outputs), out_dtype),
            jax.ShapeDtypeStruct((owned, outputs, 9 * inputs), jnp.float32),
        ],
        scratch_shapes=[pltpu.VMEM((9 * inputs, outputs), jnp.float32)],
        compiler_params=pltpu.CompilerParams(
            dimension_semantics=("arbitrary", "arbitrary"), vmem_limit_bytes=60 * 1024 * 1024
        ),
        cost_estimate=pl.CostEstimate(
            flops=flops,
            transcendentals=0,
            bytes_accessed=hidden.size * 2 * 4 + owned * out_rows * out_cols * outputs * 8
            + owned * outputs * 9 * inputs * 4,
        ),
    )(*operands)


def halving_reduce_scatter(partial, axes, swap=False):
    devices = lax.axis_size(axes)
    tiles = lax.axis_size(axes[-1])
    bits = devices.bit_length() - 1
    me = lax.axis_index(axes)
    core = tiles.bit_length() - 1
    high = [b for b in range(bits) if b > core]
    low = [b for b in range(core)]
    order = [core] + (low[:1] + high + low[1:] if swap else high + low)
    rows = partial.shape[0] // devices
    buf = partial.reshape((2,) * bits + (rows,) + partial.shape[1:])
    remaining = list(range(bits - 1, -1, -1))
    for bit in order:
        axis = remaining.index(bit)
        mine = (me >> bit) & 1
        keep = lax.dynamic_index_in_dim(buf, mine, axis=axis, keepdims=False)
        send = lax.dynamic_index_in_dim(buf, 1 - mine, axis=axis, keepdims=False)
        pairs = [(i, i ^ (1 << bit)) for i in range(devices)]
        buf = keep + lax.ppermute(send, axes, pairs)
        remaining.pop(axis)
    return buf


def local(maps, first_weight, second_weight, out_grad):
    tiles = lax.axis_size("tile")
    images, height, width, inputs = maps.shape
    outputs = first_weight.shape[3]
    owned = images // tiles
    half_rows = height // 2
    chunks = 2
    part = outputs // chunks
    upper_row = shifted_2(maps[:, height - 1 : height], "tile", 1)
    grad = out_grad.reshape(owned, -1, outputs)
    conv = None
    pieces = []
    halves = first_stage(maps, upper_row, first_weight, part)
    for chunk in range(chunks):
        channels = slice(chunk * part, (chunk + 1) * part)
        local_hidden = halves[chunk]
        arrived = lax.all_to_all(
            local_hidden.reshape(tiles, owned, half_rows, width // 2, part),
            "tile",
            split_axis=0,
            concat_axis=2,
            tiled=True,
        )
        if conv is not None:
            arrived, conv = lax.optimization_barrier((arrived, conv))
        hidden = arrived.reshape(owned, half_rows * tiles, width // 2, part)
        last = chunk == chunks - 1
        weight = second_weight[:, :, channels]
        if pieces:
            weight, pieces = lax.optimization_barrier((weight, pieces))
        conv, partial = second_stage(hidden, weight, grad, conv, jnp.bfloat16 if last else jnp.float32)
        summed = halving_reduce_scatter(
            partial.sum(axis=0).reshape(outputs, 9 * part), ("group", "tile"), swap=chunk % 2 == 1
        )
        pieces.append(summed.reshape(-1, 9, part))
    weight_grad = jnp.concatenate(pieces, axis=-1).reshape(-1, 3, 3, outputs)
    return (conv, weight_grad)


def solution(mesh):
    return jax.shard_map(
        local,
        mesh=mesh,
        in_specs=(P("group", "tile", None, None), P(), P(), P(("group", "tile"), None, None, None)),
        out_specs=(P(("group", "tile"), None, None, None), P(("group", "tile"), None, None, None)),
        check_vma=False,
    )
```

```python
import functools

import jax
import jax.numpy as jnp
from jax import lax
from jax.experimental import pallas as pl
from jax.experimental.pallas import tpu as pltpu
from jax.sharding import PartitionSpec as P


def shifted_2(shard, axis, by):
    length = lax.axis_size(axis)
    pairs = [(i, i + by) for i in range(length) if 0 <= i + by < length]
    return lax.ppermute(shard, axis, pairs)


def shift_cols_right(slab):
    zero_col = jnp.zeros_like(slab[:, :, :1])
    return jnp.concatenate([zero_col, slab[:, :, :-1]], axis=2)


def shift_cols_left(slab):
    zero_col = jnp.zeros_like(slab[:, :, :1])
    return jnp.concatenate([slab[:, :, 1:], zero_col], axis=2)


def first_conv(source, upper_row, first_weight):
    images, rows, width, inputs = source.shape
    outputs = first_weight.shape[3]
    paired = source.reshape(images, rows // 2, 2, width // 2, 2 * inputs)
    even_rows = paired[:, :, 0]
    odd_rows = paired[:, :, 1]
    upper_paired = upper_row.reshape(images, 1, width // 2, 2 * inputs)
    odd_above = jnp.concatenate([upper_paired, odd_rows[:, :-1]], axis=1)
    sources = [odd_above, even_rows, odd_rows]
    total = jnp.zeros((images, rows // 2, width // 2, outputs), jnp.float32)
    for tap_row in range(3):
        wide_kernel = first_weight[tap_row, 1:3].reshape(2 * inputs, outputs)
        total = total + jnp.dot(sources[tap_row], wide_kernel, preferred_element_type=jnp.float32)
    halves = jnp.concatenate([piece[..., inputs:] for piece in sources], axis=-1)
    narrow_kernel = first_weight[:, 0].reshape(3 * inputs, outputs)
    total = total + jnp.dot(
        shift_cols_right(halves), narrow_kernel, preferred_element_type=jnp.float32
    )
    return jnp.maximum(total, 0.0).astype(jnp.bfloat16)


def first_kernel(x_ref, up_ref, w_ref, low_ref, high_ref, scratch):
    rows, width, inputs = x_ref.shape
    out_rows, out_cols = rows // 2, width // 2
    scratch[0] = up_ref[0].astype(jnp.float32)
    scratch[1:] = x_ref[...].astype(jnp.float32)
    first_col = lax.broadcasted_iota(jnp.int32, (out_rows, out_cols, inputs), 1) == 0
    pieces = []
    for tap_row in range(3):
        even = scratch[pl.ds(tap_row, out_rows, stride=2), pl.ds(0, out_cols, stride=2), :]
        odd = scratch[pl.ds(tap_row, out_rows, stride=2), pl.ds(1, out_cols, stride=2), :]
        left = jnp.where(first_col, 0.0, pltpu.roll(odd, 1, 1))
        pieces += [even, odd, left]
    patches = jnp.concatenate(
        [p.astype(jnp.bfloat16).reshape(out_rows * out_cols, inputs) for p in pieces], axis=-1
    )
    total = jnp.dot(patches, w_ref[...], preferred_element_type=jnp.float32)
    hidden = jnp.maximum(total, 0.0).astype(jnp.bfloat16).reshape(out_rows, out_cols, -1)
    half = low_ref.shape[-1]
    low_ref[...] = hidden[..., :half]
    high_ref[...] = hidden[..., half:]


def first_stage(maps, upper_row, first_weight, part):
    images, rows, width, inputs = maps.shape
    outputs = first_weight.shape[3]
    weight = first_weight[:, jnp.array([1, 2, 0])].reshape(9 * inputs, outputs)
    out_block = pl.BlockSpec((None, rows // 2, width // 2, part), lambda n: (n, 0, 0, 0))
    shape = jax.ShapeDtypeStruct((images, rows // 2, width // 2, part), jnp.bfloat16)
    return pl.pallas_call(
        first_kernel,
        grid=(images,),
        in_specs=[
            pl.BlockSpec((None, rows, width, inputs), lambda n: (n, 0, 0, 0)),
            pl.BlockSpec((None, 1, width, inputs), lambda n: (n, 0, 0, 0)),
            pl.BlockSpec((9 * inputs, outputs), lambda n: (0, 0)),
        ],
        out_specs=[out_block, out_block],
        out_shape=[shape, shape],
        scratch_shapes=[pltpu.VMEM((rows + 1, width, inputs), jnp.float32)],
        compiler_params=pltpu.CompilerParams(
            dimension_semantics=("arbitrary",), vmem_limit_bytes=60 * 1024 * 1024
        ),
        cost_estimate=pl.CostEstimate(
            flops=2 * images * (rows // 2) * (width // 2) * 9 * inputs * outputs,
            transcendentals=0,
            bytes_accessed=maps.size * 2 + images * (rows // 2) * (width // 2) * outputs * 2,
        ),
    )(maps, upper_row, weight)


def second_kernel(*refs, rows, carry):
    if carry:
        left_ref, mid_ref, right_ref, weight_ref, grad_ref, prev_ref, out_ref, wgrad_ref, acc_ref = refs
    else:
        left_ref, mid_ref, right_ref, weight_ref, grad_ref, out_ref, wgrad_ref, acc_ref = refs
    step = pl.program_id(1)
    _, width, outputs = out_ref.shape
    inputs = mid_ref.shape[-1]
    sources = (left_ref, mid_ref, right_ref)
    patches = jnp.concatenate(
        [
            sources[tap % 3][pl.ds(step * rows + tap // 3, rows)].reshape(rows * width, inputs)
            for tap in range(9)
        ],
        axis=-1,
    )
    total = jnp.dot(patches, weight_ref[...], preferred_element_type=jnp.float32)
    if carry:
        total = total + prev_ref[...].reshape(rows * width, outputs)
    out_ref[...] = total.astype(out_ref.dtype).reshape(rows, width, outputs)
    term = lax.dot_general(
        patches, grad_ref[...], (((0,), (0,)), ((), ())), preferred_element_type=jnp.float32
    )

    @pl.when(step == 0)
    def _():
        acc_ref[...] = term

    @pl.when(step > 0)
    def _():
        acc_ref[...] += term

    @pl.when(step == pl.num_programs(1) - 1)
    def _():
        wgrad_ref[...] = acc_ref[...].T


def second_stage(hidden, weight, grad, prev, out_dtype):
    owned, out_rows, out_cols, inputs = hidden.shape
    outputs = weight.shape[-1]
    rows = min(32, out_rows)
    row_padded = jnp.pad(hidden, ((0, 0), (1, 1), (0, 0), (0, 0)))
    shifted = [shift_cols_right(row_padded), row_padded, shift_cols_left(row_padded)]
    full = pl.BlockSpec((None, out_rows + 2, out_cols, inputs), lambda n, i: (n, 0, 0, 0))
    block = pl.BlockSpec((None, rows, out_cols, outputs), lambda n, i: (n, i, 0, 0))
    in_specs = [
        full,
        full,
        full,
        pl.BlockSpec((9 * inputs, outputs), lambda n, i: (0, 0)),
        pl.BlockSpec((None, rows * out_cols, outputs), lambda n, i: (n, i, 0)),
    ]
    operands = [*shifted, weight.reshape(9 * inputs, outputs), grad]
    if prev is not None:
        in_specs.append(block)
        operands.append(prev)
    flops = 4 * owned * out_rows * out_cols * 9 * inputs * outputs
    return pl.pallas_call(
        functools.partial(second_kernel, rows=rows, carry=prev is not None),
        grid=(owned, out_rows // rows),
        in_specs=in_specs,
        out_specs=[block, pl.BlockSpec((None, outputs, 9 * inputs), lambda n, i: (n, 0, 0))],
        out_shape=[
            jax.ShapeDtypeStruct((owned, out_rows, out_cols, outputs), out_dtype),
            jax.ShapeDtypeStruct((owned, outputs, 9 * inputs), jnp.float32),
        ],
        scratch_shapes=[pltpu.VMEM((9 * inputs, outputs), jnp.float32)],
        compiler_params=pltpu.CompilerParams(
            dimension_semantics=("arbitrary", "arbitrary"), vmem_limit_bytes=60 * 1024 * 1024
        ),
        cost_estimate=pl.CostEstimate(
            flops=flops,
            transcendentals=0,
            bytes_accessed=hidden.size * 2 * 4 + owned * out_rows * out_cols * outputs * 8
            + owned * outputs * 9 * inputs * 4,
        ),
    )(*operands)


def halving_reduce_scatter(partial, axes, swap=False):
    devices = lax.axis_size(axes)
    tiles = lax.axis_size(axes[-1])
    bits = devices.bit_length() - 1
    me = lax.axis_index(axes)
    core = tiles.bit_length() - 1
    high = [b for b in range(bits) if b > core]
    low = [b for b in range(core)]
    order = [core] + (low[:1] + high + low[1:] if swap else high + low)
    rows = partial.shape[0] // devices
    buf = partial.reshape((2,) * bits + (rows,) + partial.shape[1:])
    remaining = list(range(bits - 1, -1, -1))
    for bit in order:
        axis = remaining.index(bit)
        mine = (me >> bit) & 1
        keep = lax.dynamic_index_in_dim(buf, mine, axis=axis, keepdims=False)
        send = lax.dynamic_index_in_dim(buf, 1 - mine, axis=axis, keepdims=False)
        pairs = [(i, i ^ (1 << bit)) for i in range(devices)]
        buf = keep + lax.ppermute(send, axes, pairs)
        remaining.pop(axis)
    return buf


def local(maps, first_weight, second_weight, out_grad):
    tiles = lax.axis_size("tile")
    images, height, width, inputs = maps.shape
    outputs = first_weight.shape[3]
    owned = images // tiles
    half_rows = height // 2
    chunks = 2
    part = outputs // chunks
    upper_row = shifted_2(maps[:, height - 1 : height], "tile", 1)
    grad = out_grad.reshape(owned, -1, outputs)
    conv = None
    pieces = []
    halves = first_stage(maps, upper_row, first_weight, part)
    for chunk in range(chunks):
        channels = slice(chunk * part, (chunk + 1) * part)
        local_hidden = halves[chunk]
        arrived = lax.all_to_all(
            local_hidden.reshape(tiles, owned, half_rows, width // 2, part),
            "tile",
            split_axis=0,
            concat_axis=2,
            tiled=True,
        )
        if conv is not None:
            arrived, conv = lax.optimization_barrier((arrived, conv))
        hidden = arrived.reshape(owned, half_rows * tiles, width // 2, part)
        last = chunk == chunks - 1
        conv, partial = second_stage(
            hidden, second_weight[:, :, channels], grad, conv, jnp.bfloat16 if last else jnp.float32
        )
        summed = halving_reduce_scatter(
            partial.sum(axis=0).reshape(outputs, 9 * part), ("group", "tile"), swap=chunk % 2 == 1
        )
        pieces.append(summed.reshape(-1, 9, part))
    weight_grad = jnp.concatenate(pieces, axis=-1).reshape(-1, 3, 3, outputs)
    return (conv, weight_grad)


def solution(mesh):
    return jax.shard_map(
        local,
        mesh=mesh,
        in_specs=(P("group", "tile", None, None), P(), P(), P(("group", "tile"), None, None, None)),
        out_specs=(P(("group", "tile"), None, None, None), P(("group", "tile"), None, None, None)),
        check_vma=False,
    )
```

```python
import functools

import jax
import jax.numpy as jnp
from jax import lax
from jax.experimental import pallas as pl
from jax.experimental.pallas import tpu as pltpu
from jax.sharding import PartitionSpec as P


def shifted_2(shard, axis, by):
    length = lax.axis_size(axis)
    pairs = [(i, i + by) for i in range(length) if 0 <= i + by < length]
    return lax.ppermute(shard, axis, pairs)


def shift_cols_right(slab):
    zero_col = jnp.zeros_like(slab[:, :, :1])
    return jnp.concatenate([zero_col, slab[:, :, :-1]], axis=2)


def shift_cols_left(slab):
    zero_col = jnp.zeros_like(slab[:, :, :1])
    return jnp.concatenate([slab[:, :, 1:], zero_col], axis=2)


def first_conv(source, upper_row, first_weight):
    images, rows, width, inputs = source.shape
    outputs = first_weight.shape[3]
    paired = source.reshape(images, rows // 2, 2, width // 2, 2 * inputs)
    even_rows = paired[:, :, 0]
    odd_rows = paired[:, :, 1]
    upper_paired = upper_row.reshape(images, 1, width // 2, 2 * inputs)
    odd_above = jnp.concatenate([upper_paired, odd_rows[:, :-1]], axis=1)
    sources = [odd_above, even_rows, odd_rows]
    total = jnp.zeros((images, rows // 2, width // 2, outputs), jnp.float32)
    for tap_row in range(3):
        wide_kernel = first_weight[tap_row, 1:3].reshape(2 * inputs, outputs)
        total = total + jnp.dot(sources[tap_row], wide_kernel, preferred_element_type=jnp.float32)
    halves = jnp.concatenate([piece[..., inputs:] for piece in sources], axis=-1)
    narrow_kernel = first_weight[:, 0].reshape(3 * inputs, outputs)
    total = total + jnp.dot(
        shift_cols_right(halves), narrow_kernel, preferred_element_type=jnp.float32
    )
    return jnp.maximum(total, 0.0).astype(jnp.bfloat16)


def first_kernel(x_ref, up_ref, w_ref, low_ref, high_ref, scratch):
    rows, width, inputs = x_ref.shape
    out_rows, out_cols = rows // 2, width // 2
    scratch[0] = up_ref[0].astype(jnp.float32)
    scratch[1:] = x_ref[...].astype(jnp.float32)
    first_col = lax.broadcasted_iota(jnp.int32, (out_rows, out_cols, inputs), 1) == 0
    pieces = []
    for tap_row in range(3):
        even = scratch[pl.ds(tap_row, out_rows, stride=2), pl.ds(0, out_cols, stride=2), :]
        odd = scratch[pl.ds(tap_row, out_rows, stride=2), pl.ds(1, out_cols, stride=2), :]
        left = jnp.where(first_col, 0.0, pltpu.roll(odd, 1, 1))
        pieces += [even, odd, left]
    patches = jnp.concatenate(
        [p.astype(jnp.bfloat16).reshape(out_rows * out_cols, inputs) for p in pieces], axis=-1
    )
    total = jnp.dot(patches, w_ref[...], preferred_element_type=jnp.float32)
    hidden = jnp.maximum(total, 0.0).astype(jnp.bfloat16).reshape(out_rows, out_cols, -1)
    half = low_ref.shape[-1]
    low_ref[...] = hidden[..., :half]
    high_ref[...] = hidden[..., half:]


def first_stage(maps, upper_row, first_weight, part):
    images, rows, width, inputs = maps.shape
    outputs = first_weight.shape[3]
    weight = first_weight[:, jnp.array([1, 2, 0])].reshape(9 * inputs, outputs)
    out_block = pl.BlockSpec((None, rows // 2, width // 2, part), lambda n: (n, 0, 0, 0))
    shape = jax.ShapeDtypeStruct((images, rows // 2, width // 2, part), jnp.bfloat16)
    return pl.pallas_call(
        first_kernel,
        grid=(images,),
        in_specs=[
            pl.BlockSpec((None, rows, width, inputs), lambda n: (n, 0, 0, 0)),
            pl.BlockSpec((None, 1, width, inputs), lambda n: (n, 0, 0, 0)),
            pl.BlockSpec((9 * inputs, outputs), lambda n: (0, 0)),
        ],
        out_specs=[out_block, out_block],
        out_shape=[shape, shape],
        scratch_shapes=[pltpu.VMEM((rows + 1, width, inputs), jnp.float32)],
        compiler_params=pltpu.CompilerParams(
            dimension_semantics=("arbitrary",), vmem_limit_bytes=60 * 1024 * 1024
        ),
        cost_estimate=pl.CostEstimate(
            flops=2 * images * (rows // 2) * (width // 2) * 9 * inputs * outputs,
            transcendentals=0,
            bytes_accessed=maps.size * 2 + images * (rows // 2) * (width // 2) * outputs * 2,
        ),
    )(maps, upper_row, weight)


def second_kernel(*refs, rows, carry):
    if carry:
        src_ref, weight_ref, grad_ref, prev_ref, out_ref, wgrad_ref, acc_ref = refs
    else:
        src_ref, weight_ref, grad_ref, out_ref, wgrad_ref, acc_ref = refs
    step = pl.program_id(1)
    _, width, outputs = out_ref.shape
    inputs = src_ref.shape[-1]
    patches = jnp.concatenate(
        [
            src_ref[tap % 3, pl.ds(step * rows + tap // 3, rows)].reshape(rows * width, inputs)
            for tap in range(9)
        ],
        axis=-1,
    )
    total = jnp.dot(patches, weight_ref[...], preferred_element_type=jnp.float32)
    if carry:
        total = total + prev_ref[...].reshape(rows * width, outputs)
    out_ref[...] = total.astype(out_ref.dtype).reshape(rows, width, outputs)
    term = lax.dot_general(
        patches, grad_ref[...], (((0,), (0,)), ((), ())), preferred_element_type=jnp.float32
    )

    @pl.when(step == 0)
    def _():
        acc_ref[...] = term

    @pl.when(step > 0)
    def _():
        acc_ref[...] += term

    @pl.when(step == pl.num_programs(1) - 1)
    def _():
        wgrad_ref[...] = acc_ref[...].T


def second_stage(hidden, weight, grad, prev, out_dtype):
    owned, out_rows, out_cols, inputs = hidden.shape
    outputs = weight.shape[-1]
    rows = min(32, out_rows)
    row_padded = jnp.pad(hidden, ((0, 0), (1, 1), (0, 0), (0, 0)))
    shifted = jnp.stack([shift_cols_right(row_padded), row_padded, shift_cols_left(row_padded)], axis=1)
    full = pl.BlockSpec((None, 3, out_rows + 2, out_cols, inputs), lambda n, i: (n, 0, 0, 0, 0))
    block = pl.BlockSpec((None, rows, out_cols, outputs), lambda n, i: (n, i, 0, 0))
    in_specs = [
        full,
        pl.BlockSpec((9 * inputs, outputs), lambda n, i: (0, 0)),
        pl.BlockSpec((None, rows * out_cols, outputs), lambda n, i: (n, i, 0)),
    ]
    operands = [shifted, weight.reshape(9 * inputs, outputs), grad]
    if prev is not None:
        in_specs.append(block)
        operands.append(prev)
    flops = 4 * owned * out_rows * out_cols * 9 * inputs * outputs
    return pl.pallas_call(
        functools.partial(second_kernel, rows=rows, carry=prev is not None),
        grid=(owned, out_rows // rows),
        in_specs=in_specs,
        out_specs=[block, pl.BlockSpec((None, outputs, 9 * inputs), lambda n, i: (n, 0, 0))],
        out_shape=[
            jax.ShapeDtypeStruct((owned, out_rows, out_cols, outputs), out_dtype),
            jax.ShapeDtypeStruct((owned, outputs, 9 * inputs), jnp.float32),
        ],
        scratch_shapes=[pltpu.VMEM((9 * inputs, outputs), jnp.float32)],
        compiler_params=pltpu.CompilerParams(
            dimension_semantics=("arbitrary", "arbitrary"), vmem_limit_bytes=60 * 1024 * 1024
        ),
        cost_estimate=pl.CostEstimate(
            flops=flops,
            transcendentals=0,
            bytes_accessed=hidden.size * 2 * 4 + owned * out_rows * out_cols * outputs * 8
            + owned * outputs * 9 * inputs * 4,
        ),
    )(*operands)


def halving_reduce_scatter(partial, axes, swap=False):
    devices = lax.axis_size(axes)
    tiles = lax.axis_size(axes[-1])
    bits = devices.bit_length() - 1
    me = lax.axis_index(axes)
    core = tiles.bit_length() - 1
    high = [b for b in range(bits) if b > core]
    low = [b for b in range(core)]
    order = [core] + (low[:1] + high + low[1:] if swap else high + low)
    rows = partial.shape[0] // devices
    buf = partial.reshape((2,) * bits + (rows,) + partial.shape[1:])
    remaining = list(range(bits - 1, -1, -1))
    for bit in order:
        axis = remaining.index(bit)
        mine = (me >> bit) & 1
        keep = lax.dynamic_index_in_dim(buf, mine, axis=axis, keepdims=False)
        send = lax.dynamic_index_in_dim(buf, 1 - mine, axis=axis, keepdims=False)
        pairs = [(i, i ^ (1 << bit)) for i in range(devices)]
        buf = keep + lax.ppermute(send, axes, pairs)
        remaining.pop(axis)
    return buf


def local(maps, first_weight, second_weight, out_grad):
    tiles = lax.axis_size("tile")
    images, height, width, inputs = maps.shape
    outputs = first_weight.shape[3]
    owned = images // tiles
    half_rows = height // 2
    chunks = 2
    part = outputs // chunks
    upper_row = shifted_2(maps[:, height - 1 : height], "tile", 1)
    grad = out_grad.reshape(owned, -1, outputs)
    conv = None
    pieces = []
    halves = first_stage(maps, upper_row, first_weight, part)
    for chunk in range(chunks):
        channels = slice(chunk * part, (chunk + 1) * part)
        local_hidden = halves[chunk]
        arrived = lax.all_to_all(
            local_hidden.reshape(tiles, owned, half_rows, width // 2, part),
            "tile",
            split_axis=0,
            concat_axis=2,
            tiled=True,
        )
        if conv is not None:
            arrived, conv = lax.optimization_barrier((arrived, conv))
        hidden = arrived.reshape(owned, half_rows * tiles, width // 2, part)
        last = chunk == chunks - 1
        conv, partial = second_stage(
            hidden, second_weight[:, :, channels], grad, conv, jnp.bfloat16 if last else jnp.float32
        )
        summed = halving_reduce_scatter(
            partial.sum(axis=0).reshape(outputs, 9 * part), ("group", "tile"), swap=chunk % 2 == 1
        )
        pieces.append(summed.reshape(-1, 9, part))
    weight_grad = jnp.concatenate(pieces, axis=-1).reshape(-1, 3, 3, outputs)
    return (conv, weight_grad)


def solution(mesh):
    return jax.shard_map(
        local,
        mesh=mesh,
        in_specs=(P("group", "tile", None, None), P(), P(), P(("group", "tile"), None, None, None)),
        out_specs=(P(("group", "tile"), None, None, None), P(("group", "tile"), None, None, None)),
        check_vma=False,
    )
```

```python
import functools

import jax
import jax.numpy as jnp
from jax import lax
from jax.experimental import pallas as pl
from jax.experimental.pallas import tpu as pltpu
from jax.sharding import PartitionSpec as P


def shifted_2(shard, axis, by):
    length = lax.axis_size(axis)
    pairs = [(i, i + by) for i in range(length) if 0 <= i + by < length]
    return lax.ppermute(shard, axis, pairs)


def shift_cols_right(slab):
    zero_col = jnp.zeros_like(slab[:, :, :1])
    return jnp.concatenate([zero_col, slab[:, :, :-1]], axis=2)


def shift_cols_left(slab):
    zero_col = jnp.zeros_like(slab[:, :, :1])
    return jnp.concatenate([slab[:, :, 1:], zero_col], axis=2)


def first_conv(source, upper_row, first_weight):
    images, rows, width, inputs = source.shape
    outputs = first_weight.shape[3]
    paired = source.reshape(images, rows // 2, 2, width // 2, 2 * inputs)
    even_rows = paired[:, :, 0]
    odd_rows = paired[:, :, 1]
    upper_paired = upper_row.reshape(images, 1, width // 2, 2 * inputs)
    odd_above = jnp.concatenate([upper_paired, odd_rows[:, :-1]], axis=1)
    sources = [odd_above, even_rows, odd_rows]
    total = jnp.zeros((images, rows // 2, width // 2, outputs), jnp.float32)
    for tap_row in range(3):
        wide_kernel = first_weight[tap_row, 1:3].reshape(2 * inputs, outputs)
        total = total + jnp.dot(sources[tap_row], wide_kernel, preferred_element_type=jnp.float32)
    halves = jnp.concatenate([piece[..., inputs:] for piece in sources], axis=-1)
    narrow_kernel = first_weight[:, 0].reshape(3 * inputs, outputs)
    total = total + jnp.dot(
        shift_cols_right(halves), narrow_kernel, preferred_element_type=jnp.float32
    )
    return jnp.maximum(total, 0.0).astype(jnp.bfloat16)


def first_kernel(x_ref, up_ref, w_ref, low_ref, high_ref, scratch):
    rows, width, inputs = x_ref.shape
    out_rows, out_cols = rows // 2, width // 2
    scratch[0] = up_ref[0].astype(jnp.float32)
    scratch[1:] = x_ref[...].astype(jnp.float32)
    first_col = lax.broadcasted_iota(jnp.int32, (out_rows, out_cols, inputs), 1) == 0
    pieces = []
    for tap_row in range(3):
        even = scratch[pl.ds(tap_row, out_rows, stride=2), pl.ds(0, out_cols, stride=2), :]
        odd = scratch[pl.ds(tap_row, out_rows, stride=2), pl.ds(1, out_cols, stride=2), :]
        left = jnp.where(first_col, 0.0, pltpu.roll(odd, 1, 1))
        pieces += [even, odd, left]
    patches = jnp.concatenate(
        [p.astype(jnp.bfloat16).reshape(out_rows * out_cols, inputs) for p in pieces], axis=-1
    )
    total = jnp.dot(patches, w_ref[...], preferred_element_type=jnp.float32)
    hidden = jnp.maximum(total, 0.0).astype(jnp.bfloat16).reshape(out_rows, out_cols, -1)
    half = low_ref.shape[-1]
    low_ref[...] = hidden[..., :half]
    high_ref[...] = hidden[..., half:]


def first_stage(maps, upper_row, first_weight, part):
    images, rows, width, inputs = maps.shape
    outputs = first_weight.shape[3]
    weight = first_weight[:, jnp.array([1, 2, 0])].reshape(9 * inputs, outputs)
    out_block = pl.BlockSpec((None, rows // 2, width // 2, part), lambda n: (n, 0, 0, 0))
    shape = jax.ShapeDtypeStruct((images, rows // 2, width // 2, part), jnp.bfloat16)
    return pl.pallas_call(
        first_kernel,
        grid=(images,),
        in_specs=[
            pl.BlockSpec((None, rows, width, inputs), lambda n: (n, 0, 0, 0)),
            pl.BlockSpec((None, 1, width, inputs), lambda n: (n, 0, 0, 0)),
            pl.BlockSpec((9 * inputs, outputs), lambda n: (0, 0)),
        ],
        out_specs=[out_block, out_block],
        out_shape=[shape, shape],
        scratch_shapes=[pltpu.VMEM((rows + 1, width, inputs), jnp.float32)],
        compiler_params=pltpu.CompilerParams(
            dimension_semantics=("arbitrary",), vmem_limit_bytes=60 * 1024 * 1024
        ),
        cost_estimate=pl.CostEstimate(
            flops=2 * images * (rows // 2) * (width // 2) * 9 * inputs * outputs,
            transcendentals=0,
            bytes_accessed=maps.size * 2 + images * (rows // 2) * (width // 2) * outputs * 2,
        ),
    )(maps, upper_row, weight)


def second_kernel(*refs, rows, carry):
    if carry:
        src_ref, weight_ref, grad_ref, prev_ref, out_ref, wgrad_ref, acc_ref = refs
    else:
        src_ref, weight_ref, grad_ref, out_ref, wgrad_ref, acc_ref = refs
    step = pl.program_id(1)
    _, width, outputs = out_ref.shape
    inputs = src_ref.shape[-1]
    patches = jnp.concatenate(
        [
            src_ref[tap % 3, pl.ds(step * rows + tap // 3, rows)].reshape(rows * width, inputs)
            for tap in range(9)
        ],
        axis=-1,
    )
    total = jnp.dot(patches, weight_ref[...], preferred_element_type=jnp.float32)
    if carry:
        total = total + prev_ref[...].reshape(rows * width, outputs)
    out_ref[...] = total.astype(out_ref.dtype).reshape(rows, width, outputs)
    term = lax.dot_general(
        patches, grad_ref[...], (((0,), (0,)), ((), ())), preferred_element_type=jnp.float32
    )

    @pl.when(step == 0)
    def _():
        acc_ref[...] = term

    @pl.when(step > 0)
    def _():
        acc_ref[...] += term

    @pl.when(step == pl.num_programs(1) - 1)
    def _():
        wgrad_ref[...] = acc_ref[...].T


def second_stage(hidden, weight, grad, prev, out_dtype):
    owned, out_rows, out_cols, inputs = hidden.shape
    outputs = weight.shape[-1]
    rows = min(32, out_rows)
    row_padded = jnp.pad(hidden, ((0, 0), (1, 1), (0, 0), (0, 0)))
    shifted = jnp.stack([shift_cols_right(row_padded), row_padded, shift_cols_left(row_padded)], axis=1)
    full = pl.BlockSpec((None, 3, out_rows + 2, out_cols, inputs), lambda n, i: (n, 0, 0, 0, 0))
    block = pl.BlockSpec((None, rows, out_cols, outputs), lambda n, i: (n, i, 0, 0))
    in_specs = [
        full,
        pl.BlockSpec((9 * inputs, outputs), lambda n, i: (0, 0)),
        pl.BlockSpec((None, rows * out_cols, outputs), lambda n, i: (n, i, 0)),
    ]
    operands = [shifted, weight.reshape(9 * inputs, outputs), grad]
    if prev is not None:
        in_specs.append(block)
        operands.append(prev)
    flops = 4 * owned * out_rows * out_cols * 9 * inputs * outputs
    return pl.pallas_call(
        functools.partial(second_kernel, rows=rows, carry=prev is not None),
        grid=(owned, out_rows // rows),
        in_specs=in_specs,
        out_specs=[block, pl.BlockSpec((None, outputs, 9 * inputs), lambda n, i: (n, 0, 0))],
        out_shape=[
            jax.ShapeDtypeStruct((owned, out_rows, out_cols, outputs), out_dtype),
            jax.ShapeDtypeStruct((owned, outputs, 9 * inputs), jnp.float32),
        ],
        scratch_shapes=[pltpu.VMEM((9 * inputs, outputs), jnp.float32)],
        compiler_params=pltpu.CompilerParams(
            dimension_semantics=("arbitrary", "arbitrary"), vmem_limit_bytes=60 * 1024 * 1024
        ),
        cost_estimate=pl.CostEstimate(
            flops=flops,
            transcendentals=0,
            bytes_accessed=hidden.size * 2 * 4 + owned * out_rows * out_cols * outputs * 8
            + owned * outputs * 9 * inputs * 4,
        ),
    )(*operands)


def halving_reduce_scatter(partial, axes, swap=False):
    devices = lax.axis_size(axes)
    tiles = lax.axis_size(axes[-1])
    bits = devices.bit_length() - 1
    me = lax.axis_index(axes)
    core = tiles.bit_length() - 1
    high = [b for b in range(bits) if b > core]
    low = [b for b in range(core)]
    order = [core] + (low[:1] + high + low[1:] if swap else high + low)
    rows = partial.shape[0] // devices
    buf = partial.reshape((2,) * bits + (rows,) + partial.shape[1:])
    remaining = list(range(bits - 1, -1, -1))
    for bit in order:
        axis = remaining.index(bit)
        mine = (me >> bit) & 1
        keep = lax.dynamic_index_in_dim(buf, mine, axis=axis, keepdims=False)
        send = lax.dynamic_index_in_dim(buf, 1 - mine, axis=axis, keepdims=False)
        pairs = [(i, i ^ (1 << bit)) for i in range(devices)]
        buf = keep + lax.ppermute(send.astype(jnp.bfloat16), axes, pairs).astype(jnp.float32)
        remaining.pop(axis)
    return buf


def local(maps, first_weight, second_weight, out_grad):
    tiles = lax.axis_size("tile")
    images, height, width, inputs = maps.shape
    outputs = first_weight.shape[3]
    owned = images // tiles
    half_rows = height // 2
    chunks = 2
    part = outputs // chunks
    upper_row = shifted_2(maps[:, height - 1 : height], "tile", 1)
    grad = out_grad.reshape(owned, -1, outputs)
    conv = None
    pieces = []
    halves = first_stage(maps, upper_row, first_weight, part)
    for chunk in range(chunks):
        channels = slice(chunk * part, (chunk + 1) * part)
        local_hidden = halves[chunk]
        arrived = lax.all_to_all(
            local_hidden.reshape(tiles, owned, half_rows, width // 2, part),
            "tile",
            split_axis=0,
            concat_axis=2,
            tiled=True,
        )
        if conv is not None:
            arrived, conv = lax.optimization_barrier((arrived, conv))
        hidden = arrived.reshape(owned, half_rows * tiles, width // 2, part)
        last = chunk == chunks - 1
        conv, partial = second_stage(
            hidden, second_weight[:, :, channels], grad, conv, jnp.bfloat16 if last else jnp.float32
        )
        summed = halving_reduce_scatter(
            partial.sum(axis=0).reshape(outputs, 9 * part), ("group", "tile"), swap=chunk % 2 == 1
        )
        pieces.append(summed.reshape(-1, 9, part))
    weight_grad = jnp.concatenate(pieces, axis=-1).reshape(-1, 3, 3, outputs)
    return (conv, weight_grad)


def solution(mesh):
    return jax.shard_map(
        local,
        mesh=mesh,
        in_specs=(P("group", "tile", None, None), P(), P(), P(("group", "tile"), None, None, None)),
        out_specs=(P(("group", "tile"), None, None, None), P(("group", "tile"), None, None, None)),
        check_vma=False,
    )
```

```python
import functools

import jax
import jax.numpy as jnp
from jax import lax
from jax.experimental import pallas as pl
from jax.experimental.pallas import tpu as pltpu
from jax.sharding import PartitionSpec as P


def shifted_2(shard, axis, by):
    length = lax.axis_size(axis)
    pairs = [(i, i + by) for i in range(length) if 0 <= i + by < length]
    return lax.ppermute(shard, axis, pairs)


def shift_cols_right(slab):
    zero_col = jnp.zeros_like(slab[:, :, :1])
    return jnp.concatenate([zero_col, slab[:, :, :-1]], axis=2)


def shift_cols_left(slab):
    zero_col = jnp.zeros_like(slab[:, :, :1])
    return jnp.concatenate([slab[:, :, 1:], zero_col], axis=2)


def first_conv(source, upper_row, first_weight):
    images, rows, width, inputs = source.shape
    outputs = first_weight.shape[3]
    paired = source.reshape(images, rows // 2, 2, width // 2, 2 * inputs)
    even_rows = paired[:, :, 0]
    odd_rows = paired[:, :, 1]
    upper_paired = upper_row.reshape(images, 1, width // 2, 2 * inputs)
    odd_above = jnp.concatenate([upper_paired, odd_rows[:, :-1]], axis=1)
    sources = [odd_above, even_rows, odd_rows]
    total = jnp.zeros((images, rows // 2, width // 2, outputs), jnp.float32)
    for tap_row in range(3):
        wide_kernel = first_weight[tap_row, 1:3].reshape(2 * inputs, outputs)
        total = total + jnp.dot(sources[tap_row], wide_kernel, preferred_element_type=jnp.float32)
    halves = jnp.concatenate([piece[..., inputs:] for piece in sources], axis=-1)
    narrow_kernel = first_weight[:, 0].reshape(3 * inputs, outputs)
    total = total + jnp.dot(
        shift_cols_right(halves), narrow_kernel, preferred_element_type=jnp.float32
    )
    return jnp.maximum(total, 0.0).astype(jnp.bfloat16)


def first_kernel(x_ref, up_ref, w_ref, low_ref, high_ref, scratch):
    rows, width, inputs = x_ref.shape
    out_rows, out_cols = rows // 2, width // 2
    scratch[0] = up_ref[0].astype(jnp.float32)
    scratch[1:] = x_ref[...].astype(jnp.float32)
    first_col = lax.broadcasted_iota(jnp.int32, (out_rows, out_cols, inputs), 1) == 0
    pieces = []
    for tap_row in range(3):
        even = scratch[pl.ds(tap_row, out_rows, stride=2), pl.ds(0, out_cols, stride=2), :]
        odd = scratch[pl.ds(tap_row, out_rows, stride=2), pl.ds(1, out_cols, stride=2), :]
        left = jnp.where(first_col, 0.0, pltpu.roll(odd, 1, 1))
        pieces += [even, odd, left]
    patches = jnp.concatenate(
        [p.astype(jnp.bfloat16).reshape(out_rows * out_cols, inputs) for p in pieces], axis=-1
    )
    total = jnp.dot(patches, w_ref[...], preferred_element_type=jnp.float32)
    hidden = jnp.maximum(total, 0.0).astype(jnp.bfloat16).reshape(out_rows, out_cols, -1)
    half = low_ref.shape[-1]
    low_ref[...] = hidden[..., :half]
    high_ref[...] = hidden[..., half:]


def first_stage(maps, upper_row, first_weight, part):
    images, rows, width, inputs = maps.shape
    outputs = first_weight.shape[3]
    weight = first_weight[:, jnp.array([1, 2, 0])].reshape(9 * inputs, outputs)
    out_block = pl.BlockSpec((None, rows // 2, width // 2, part), lambda n: (n, 0, 0, 0))
    shape = jax.ShapeDtypeStruct((images, rows // 2, width // 2, part), jnp.bfloat16)
    return pl.pallas_call(
        first_kernel,
        grid=(images,),
        in_specs=[
            pl.BlockSpec((None, rows, width, inputs), lambda n: (n, 0, 0, 0)),
            pl.BlockSpec((None, 1, width, inputs), lambda n: (n, 0, 0, 0)),
            pl.BlockSpec((9 * inputs, outputs), lambda n: (0, 0)),
        ],
        out_specs=[out_block, out_block],
        out_shape=[shape, shape],
        scratch_shapes=[pltpu.VMEM((rows + 1, width, inputs), jnp.float32)],
        compiler_params=pltpu.CompilerParams(
            dimension_semantics=("arbitrary",), vmem_limit_bytes=60 * 1024 * 1024
        ),
        cost_estimate=pl.CostEstimate(
            flops=2 * images * (rows // 2) * (width // 2) * 9 * inputs * outputs,
            transcendentals=0,
            bytes_accessed=maps.size * 2 + images * (rows // 2) * (width // 2) * outputs * 2,
        ),
    )(maps, upper_row, weight)


def second_kernel(*refs, rows, carry):
    if carry:
        src_ref, weight_ref, grad_ref, prev_ref, out_ref, wgrad_ref, acc_ref = refs
    else:
        src_ref, weight_ref, grad_ref, out_ref, wgrad_ref, acc_ref = refs
    step = pl.program_id(1)
    _, width, outputs = out_ref.shape
    inputs = src_ref.shape[-1]
    patches = jnp.concatenate(
        [
            src_ref[tap % 3, pl.ds(step * rows + tap // 3, rows)].reshape(rows * width, inputs)
            for tap in range(9)
        ],
        axis=-1,
    )
    total = jnp.dot(patches, weight_ref[...], preferred_element_type=jnp.float32)
    if carry:
        total = total + prev_ref[...].reshape(rows * width, outputs)
    out_ref[...] = total.astype(out_ref.dtype).reshape(rows, width, outputs)
    term = lax.dot_general(
        patches, grad_ref[...], (((0,), (0,)), ((), ())), preferred_element_type=jnp.float32
    )

    @pl.when(step == 0)
    def _():
        acc_ref[...] = term

    @pl.when(step > 0)
    def _():
        acc_ref[...] += term

    @pl.when(step == pl.num_programs(1) - 1)
    def _():
        wgrad_ref[...] = acc_ref[...].T


def second_stage(hidden, weight, grad, prev, out_dtype):
    owned, out_rows, out_cols, inputs = hidden.shape
    outputs = weight.shape[-1]
    rows = min(32, out_rows)
    row_padded = jnp.pad(hidden, ((0, 0), (1, 1), (0, 0), (0, 0)))
    shifted = jnp.stack([shift_cols_right(row_padded), row_padded, shift_cols_left(row_padded)], axis=1)
    full = pl.BlockSpec((None, 3, out_rows + 2, out_cols, inputs), lambda n, i: (n, 0, 0, 0, 0))
    block = pl.BlockSpec((None, rows, out_cols, outputs), lambda n, i: (n, i, 0, 0))
    in_specs = [
        full,
        pl.BlockSpec((9 * inputs, outputs), lambda n, i: (0, 0)),
        pl.BlockSpec((None, rows * out_cols, outputs), lambda n, i: (n, i, 0)),
    ]
    operands = [shifted, weight.reshape(9 * inputs, outputs), grad]
    if prev is not None:
        in_specs.append(block)
        operands.append(prev)
    flops = 4 * owned * out_rows * out_cols * 9 * inputs * outputs
    return pl.pallas_call(
        functools.partial(second_kernel, rows=rows, carry=prev is not None),
        grid=(owned, out_rows // rows),
        in_specs=in_specs,
        out_specs=[block, pl.BlockSpec((None, outputs, 9 * inputs), lambda n, i: (n, 0, 0))],
        out_shape=[
            jax.ShapeDtypeStruct((owned, out_rows, out_cols, outputs), out_dtype),
            jax.ShapeDtypeStruct((owned, outputs, 9 * inputs), jnp.float32),
        ],
        scratch_shapes=[pltpu.VMEM((9 * inputs, outputs), jnp.float32)],
        compiler_params=pltpu.CompilerParams(
            dimension_semantics=("arbitrary", "arbitrary"), vmem_limit_bytes=60 * 1024 * 1024
        ),
        cost_estimate=pl.CostEstimate(
            flops=flops,
            transcendentals=0,
            bytes_accessed=hidden.size * 2 * 4 + owned * out_rows * out_cols * outputs * 8
            + owned * outputs * 9 * inputs * 4,
        ),
    )(*operands)


def halving_reduce_scatter(partial, axes, swap=False):
    devices = lax.axis_size(axes)
    tiles = lax.axis_size(axes[-1])
    bits = devices.bit_length() - 1
    me = lax.axis_index(axes)
    core = tiles.bit_length() - 1
    high = [b for b in range(bits) if b > core]
    low = [b for b in range(core)]
    order = [core] + (low[:1] + high + low[1:] if swap else high + low)
    rows = partial.shape[0] // devices
    buf = partial.reshape((2,) * bits + (rows,) + partial.shape[1:])
    remaining = list(range(bits - 1, -1, -1))
    for position, bit in enumerate(order):
        axis = remaining.index(bit)
        mine = (me >> bit) & 1
        keep = lax.dynamic_index_in_dim(buf, mine, axis=axis, keepdims=False)
        send = lax.dynamic_index_in_dim(buf, 1 - mine, axis=axis, keepdims=False)
        pairs = [(i, i ^ (1 << bit)) for i in range(devices)]
        if position == 1:
            buf = keep + lax.ppermute(send.astype(jnp.bfloat16), axes, pairs).astype(jnp.float32)
        else:
            buf = keep + lax.ppermute(send, axes, pairs)
        remaining.pop(axis)
    return buf


def local(maps, first_weight, second_weight, out_grad):
    tiles = lax.axis_size("tile")
    images, height, width, inputs = maps.shape
    outputs = first_weight.shape[3]
    owned = images // tiles
    half_rows = height // 2
    chunks = 2
    part = outputs // chunks
    upper_row = shifted_2(maps[:, height - 1 : height], "tile", 1)
    grad = out_grad.reshape(owned, -1, outputs)
    conv = None
    pieces = []
    halves = first_stage(maps, upper_row, first_weight, part)
    for chunk in range(chunks):
        channels = slice(chunk * part, (chunk + 1) * part)
        local_hidden = halves[chunk]
        arrived = lax.all_to_all(
            local_hidden.reshape(tiles, owned, half_rows, width // 2, part),
            "tile",
            split_axis=0,
            concat_axis=2,
            tiled=True,
        )
        if conv is not None:
            arrived, conv = lax.optimization_barrier((arrived, conv))
        hidden = arrived.reshape(owned, half_rows * tiles, width // 2, part)
        last = chunk == chunks - 1
        conv, partial = second_stage(
            hidden, second_weight[:, :, channels], grad, conv, jnp.bfloat16 if last else jnp.float32
        )
        summed = halving_reduce_scatter(
            partial.sum(axis=0).reshape(outputs, 9 * part), ("group", "tile"), swap=chunk % 2 == 1
        )
        pieces.append(summed.reshape(-1, 9, part))
    weight_grad = jnp.concatenate(pieces, axis=-1).reshape(-1, 3, 3, outputs)
    return (conv, weight_grad)


def solution(mesh):
    return jax.shard_map(
        local,
        mesh=mesh,
        in_specs=(P("group", "tile", None, None), P(), P(), P(("group", "tile"), None, None, None)),
        out_specs=(P(("group", "tile"), None, None, None), P(("group", "tile"), None, None, None)),
        check_vma=False,
    )
```

```python
import functools

import jax
import jax.numpy as jnp
from jax import lax
from jax.experimental import pallas as pl
from jax.experimental.pallas import tpu as pltpu
from jax.sharding import PartitionSpec as P


def shifted_2(shard, axis, by):
    length = lax.axis_size(axis)
    pairs = [(i, i + by) for i in range(length) if 0 <= i + by < length]
    return lax.ppermute(shard, axis, pairs)


def shift_cols_right(slab):
    zero_col = jnp.zeros_like(slab[:, :, :1])
    return jnp.concatenate([zero_col, slab[:, :, :-1]], axis=2)


def shift_cols_left(slab):
    zero_col = jnp.zeros_like(slab[:, :, :1])
    return jnp.concatenate([slab[:, :, 1:], zero_col], axis=2)


def first_conv(source, upper_row, first_weight):
    images, rows, width, inputs = source.shape
    outputs = first_weight.shape[3]
    paired = source.reshape(images, rows // 2, 2, width // 2, 2 * inputs)
    even_rows = paired[:, :, 0]
    odd_rows = paired[:, :, 1]
    upper_paired = upper_row.reshape(images, 1, width // 2, 2 * inputs)
    odd_above = jnp.concatenate([upper_paired, odd_rows[:, :-1]], axis=1)
    sources = [odd_above, even_rows, odd_rows]
    total = jnp.zeros((images, rows // 2, width // 2, outputs), jnp.float32)
    for tap_row in range(3):
        wide_kernel = first_weight[tap_row, 1:3].reshape(2 * inputs, outputs)
        total = total + jnp.dot(sources[tap_row], wide_kernel, preferred_element_type=jnp.float32)
    halves = jnp.concatenate([piece[..., inputs:] for piece in sources], axis=-1)
    narrow_kernel = first_weight[:, 0].reshape(3 * inputs, outputs)
    total = total + jnp.dot(
        shift_cols_right(halves), narrow_kernel, preferred_element_type=jnp.float32
    )
    return jnp.maximum(total, 0.0).astype(jnp.bfloat16)


def first_kernel(x_ref, w_ref, low_ref, high_ref, scratch):
    rows, width, inputs = x_ref.shape
    out_rows, out_cols = rows // 2, width // 2
    scratch[0] = jnp.zeros(scratch.shape[1:], jnp.float32)
    scratch[1:] = x_ref[...].astype(jnp.float32)
    first_col = lax.broadcasted_iota(jnp.int32, (out_rows, out_cols, inputs), 1) == 0
    pieces = []
    for tap_row in range(3):
        even = scratch[pl.ds(tap_row, out_rows, stride=2), pl.ds(0, out_cols, stride=2), :]
        odd = scratch[pl.ds(tap_row, out_rows, stride=2), pl.ds(1, out_cols, stride=2), :]
        left = jnp.where(first_col, 0.0, pltpu.roll(odd, 1, 1))
        pieces += [even, odd, left]
    patches = jnp.concatenate(
        [p.astype(jnp.bfloat16).reshape(out_rows * out_cols, inputs) for p in pieces], axis=-1
    )
    total = jnp.dot(patches, w_ref[...], preferred_element_type=jnp.float32)
    hidden = jnp.maximum(total, 0.0).astype(jnp.bfloat16).reshape(out_rows, out_cols, -1)
    half = low_ref.shape[-1]
    low_ref[...] = hidden[..., :half]
    high_ref[...] = hidden[..., half:]


def first_row_kernel(x_ref, up_ref, w_ref, _low, _high, low_ref, high_ref, scratch):
    images, _, width, inputs = x_ref.shape
    out_cols = width // 2
    scratch[:, 0] = up_ref[:, 0].astype(jnp.float32)
    scratch[:, 1:] = x_ref[...].astype(jnp.float32)
    first_col = lax.broadcasted_iota(jnp.int32, (images, out_cols, inputs), 1) == 0
    pieces = []
    for tap_row in range(3):
        even = scratch[:, tap_row, pl.ds(0, out_cols, stride=2), :]
        odd = scratch[:, tap_row, pl.ds(1, out_cols, stride=2), :]
        left = jnp.where(first_col, 0.0, pltpu.roll(odd, 1, 1))
        pieces += [even, odd, left]
    patches = jnp.concatenate(
        [p.astype(jnp.bfloat16).reshape(images * out_cols, inputs) for p in pieces], axis=-1
    )
    total = jnp.dot(patches, w_ref[...], preferred_element_type=jnp.float32)
    hidden = jnp.maximum(total, 0.0).astype(jnp.bfloat16).reshape(images, 1, out_cols, -1)
    half = low_ref.shape[-1]
    low_ref[...] = hidden[..., :half]
    high_ref[...] = hidden[..., half:]


def first_stage(maps, upper_row, first_weight, part):
    images, rows, width, inputs = maps.shape
    outputs = first_weight.shape[3]
    weight = first_weight[:, jnp.array([1, 2, 0])].reshape(9 * inputs, outputs)
    shape = jax.ShapeDtypeStruct((images, rows // 2, width // 2, part), jnp.bfloat16)
    params = pltpu.CompilerParams(dimension_semantics=("arbitrary",), vmem_limit_bytes=60 * 1024 * 1024)
    weight_spec = pl.BlockSpec((9 * inputs, outputs), lambda n: (0, 0))

    def cost(out_rows):
        return pl.CostEstimate(
            flops=2 * images * out_rows * (width // 2) * 9 * inputs * outputs,
            transcendentals=0,
            bytes_accessed=images * out_rows * 2 * width * inputs * 2 + images * out_rows * (width // 2) * outputs * 2,
        )

    out_block = pl.BlockSpec((None, rows // 2, width // 2, part), lambda n: (n, 0, 0, 0))
    low, high = pl.pallas_call(
        first_kernel,
        grid=(images,),
        in_specs=[pl.BlockSpec((None, rows, width, inputs), lambda n: (n, 0, 0, 0)), weight_spec],
        out_specs=[out_block, out_block],
        out_shape=[shape, shape],
        scratch_shapes=[pltpu.VMEM((rows + 1, width, inputs), jnp.float32)],
        compiler_params=params,
        cost_estimate=cost(rows // 2),
    )(maps, weight)
    row_block = pl.BlockSpec((images, 1, width // 2, part), lambda n: (0, 0, 0, 0))
    anywhere = pl.BlockSpec(memory_space=pl.ANY)
    return pl.pallas_call(
        first_row_kernel,
        grid=(1,),
        in_specs=[
            pl.BlockSpec((images, 2, width, inputs), lambda n: (0, 0, 0, 0)),
            pl.BlockSpec((images, 1, width, inputs), lambda n: (0, 0, 0, 0)),
            weight_spec,
            anywhere,
            anywhere,
        ],
        out_specs=[row_block, row_block],
        out_shape=[shape, shape],
        scratch_shapes=[pltpu.VMEM((images, 3, width, inputs), jnp.float32)],
        input_output_aliases={3: 0, 4: 1},
        compiler_params=params,
        cost_estimate=cost(1),
    )(maps, upper_row, weight, low, high)


def second_kernel(*refs, rows, carry):
    if carry:
        src_ref, weight_ref, grad_ref, prev_ref, out_ref, wgrad_ref, acc_ref = refs
    else:
        src_ref, weight_ref, grad_ref, out_ref, wgrad_ref, acc_ref = refs
    step = pl.program_id(1)
    _, width, outputs = out_ref.shape
    inputs = src_ref.shape[-1]
    patches = jnp.concatenate(
        [
            src_ref[tap % 3, pl.ds(step * rows + tap // 3, rows)].reshape(rows * width, inputs)
            for tap in range(9)
        ],
        axis=-1,
    )
    total = jnp.dot(patches, weight_ref[...], preferred_element_type=jnp.float32)
    if carry:
        total = total + prev_ref[...].reshape(rows * width, outputs)
    out_ref[...] = total.astype(out_ref.dtype).reshape(rows, width, outputs)
    term = lax.dot_general(
        patches, grad_ref[...], (((0,), (0,)), ((), ())), preferred_element_type=jnp.float32
    )

    @pl.when(step == 0)
    def _():
        acc_ref[...] = term

    @pl.when(step > 0)
    def _():
        acc_ref[...] += term

    @pl.when(step == pl.num_programs(1) - 1)
    def _():
        wgrad_ref[...] = acc_ref[...].T


def second_stage(hidden, weight, grad, prev, out_dtype):
    owned, out_rows, out_cols, inputs = hidden.shape
    outputs = weight.shape[-1]
    rows = min(32, out_rows)
    row_padded = jnp.pad(hidden, ((0, 0), (1, 1), (0, 0), (0, 0)))
    shifted = jnp.stack([shift_cols_right(row_padded), row_padded, shift_cols_left(row_padded)], axis=1)
    full = pl.BlockSpec((None, 3, out_rows + 2, out_cols, inputs), lambda n, i: (n, 0, 0, 0, 0))
    block = pl.BlockSpec((None, rows, out_cols, outputs), lambda n, i: (n, i, 0, 0))
    in_specs = [
        full,
        pl.BlockSpec((9 * inputs, outputs), lambda n, i: (0, 0)),
        pl.BlockSpec((None, rows * out_cols, outputs), lambda n, i: (n, i, 0)),
    ]
    operands = [shifted, weight.reshape(9 * inputs, outputs), grad]
    if prev is not None:
        in_specs.append(block)
        operands.append(prev)
    flops = 4 * owned * out_rows * out_cols * 9 * inputs * outputs
    return pl.pallas_call(
        functools.partial(second_kernel, rows=rows, carry=prev is not None),
        grid=(owned, out_rows // rows),
        in_specs=in_specs,
        out_specs=[block, pl.BlockSpec((None, outputs, 9 * inputs), lambda n, i: (n, 0, 0))],
        out_shape=[
            jax.ShapeDtypeStruct((owned, out_rows, out_cols, outputs), out_dtype),
            jax.ShapeDtypeStruct((owned, outputs, 9 * inputs), jnp.float32),
        ],
        scratch_shapes=[pltpu.VMEM((9 * inputs, outputs), jnp.float32)],
        compiler_params=pltpu.CompilerParams(
            dimension_semantics=("arbitrary", "arbitrary"), vmem_limit_bytes=60 * 1024 * 1024
        ),
        cost_estimate=pl.CostEstimate(
            flops=flops,
            transcendentals=0,
            bytes_accessed=hidden.size * 2 * 4 + owned * out_rows * out_cols * outputs * 8
            + owned * outputs * 9 * inputs * 4,
        ),
    )(*operands)


def halving_reduce_scatter(partial, axes, swap=False):
    devices = lax.axis_size(axes)
    tiles = lax.axis_size(axes[-1])
    bits = devices.bit_length() - 1
    me = lax.axis_index(axes)
    core = tiles.bit_length() - 1
    high = [b for b in range(bits) if b > core]
    low = [b for b in range(core)]
    order = [core] + (low[:1] + high + low[1:] if swap else high + low)
    rows = partial.shape[0] // devices
    buf = partial.reshape((2,) * bits + (rows,) + partial.shape[1:])
    remaining = list(range(bits - 1, -1, -1))
    for bit in order:
        axis = remaining.index(bit)
        mine = (me >> bit) & 1
        keep = lax.dynamic_index_in_dim(buf, mine, axis=axis, keepdims=False)
        send = lax.dynamic_index_in_dim(buf, 1 - mine, axis=axis, keepdims=False)
        pairs = [(i, i ^ (1 << bit)) for i in range(devices)]
        buf = keep + lax.ppermute(send, axes, pairs)
        remaining.pop(axis)
    return buf


def local(maps, first_weight, second_weight, out_grad):
    tiles = lax.axis_size("tile")
    images, height, width, inputs = maps.shape
    outputs = first_weight.shape[3]
    owned = images // tiles
    half_rows = height // 2
    chunks = 2
    part = outputs // chunks
    upper_row = shifted_2(maps[:, height - 1 : height], "tile", 1)
    grad = out_grad.reshape(owned, -1, outputs)
    conv = None
    pieces = []
    halves = first_stage(maps, upper_row, first_weight, part)
    for chunk in range(chunks):
        channels = slice(chunk * part, (chunk + 1) * part)
        local_hidden = halves[chunk]
        arrived = lax.all_to_all(
            local_hidden.reshape(tiles, owned, half_rows, width // 2, part),
            "tile",
            split_axis=0,
            concat_axis=2,
            tiled=True,
        )
        if conv is not None:
            arrived, conv = lax.optimization_barrier((arrived, conv))
        hidden = arrived.reshape(owned, half_rows * tiles, width // 2, part)
        last = chunk == chunks - 1
        conv, partial = second_stage(
            hidden, second_weight[:, :, channels], grad, conv, jnp.bfloat16 if last else jnp.float32
        )
        summed = halving_reduce_scatter(
            partial.sum(axis=0).reshape(outputs, 9 * part), ("group", "tile"), swap=chunk % 2 == 1
        )
        pieces.append(summed.reshape(-1, 9, part))
    weight_grad = jnp.concatenate(pieces, axis=-1).reshape(-1, 3, 3, outputs)
    return (conv, weight_grad)


def solution(mesh):
    return jax.shard_map(
        local,
        mesh=mesh,
        in_specs=(P("group", "tile", None, None), P(), P(), P(("group", "tile"), None, None, None)),
        out_specs=(P(("group", "tile"), None, None, None), P(("group", "tile"), None, None, None)),
        check_vma=False,
    )
```

```python
import functools

import jax
import jax.numpy as jnp
from jax import lax
from jax.experimental import pallas as pl
from jax.experimental.pallas import tpu as pltpu
from jax.sharding import PartitionSpec as P


def shifted_2(shard, axis, by):
    length = lax.axis_size(axis)
    pairs = [(i, i + by) for i in range(length) if 0 <= i + by < length]
    return lax.ppermute(shard, axis, pairs)


def shift_cols_right(slab):
    zero_col = jnp.zeros_like(slab[:, :, :1])
    return jnp.concatenate([zero_col, slab[:, :, :-1]], axis=2)


def shift_cols_left(slab):
    zero_col = jnp.zeros_like(slab[:, :, :1])
    return jnp.concatenate([slab[:, :, 1:], zero_col], axis=2)


def first_conv(source, upper_row, first_weight):
    images, rows, width, inputs = source.shape
    outputs = first_weight.shape[3]
    paired = source.reshape(images, rows // 2, 2, width // 2, 2 * inputs)
    even_rows = paired[:, :, 0]
    odd_rows = paired[:, :, 1]
    upper_paired = upper_row.reshape(images, 1, width // 2, 2 * inputs)
    odd_above = jnp.concatenate([upper_paired, odd_rows[:, :-1]], axis=1)
    sources = [odd_above, even_rows, odd_rows]
    total = jnp.zeros((images, rows // 2, width // 2, outputs), jnp.float32)
    for tap_row in range(3):
        wide_kernel = first_weight[tap_row, 1:3].reshape(2 * inputs, outputs)
        total = total + jnp.dot(sources[tap_row], wide_kernel, preferred_element_type=jnp.float32)
    halves = jnp.concatenate([piece[..., inputs:] for piece in sources], axis=-1)
    narrow_kernel = first_weight[:, 0].reshape(3 * inputs, outputs)
    total = total + jnp.dot(
        shift_cols_right(halves), narrow_kernel, preferred_element_type=jnp.float32
    )
    return jnp.maximum(total, 0.0).astype(jnp.bfloat16)


def first_kernel(x_ref, w_ref, low_ref, high_ref, scratch):
    rows, width, inputs = x_ref.shape
    out_rows, out_cols = rows // 2, width // 2
    scratch[0] = jnp.zeros(scratch.shape[1:], jnp.float32)
    scratch[1:] = x_ref[...].astype(jnp.float32)
    first_col = lax.broadcasted_iota(jnp.int32, (out_rows, out_cols, inputs), 1) == 0
    pieces = []
    for tap_row in range(3):
        even = scratch[pl.ds(tap_row, out_rows, stride=2), pl.ds(0, out_cols, stride=2), :]
        odd = scratch[pl.ds(tap_row, out_rows, stride=2), pl.ds(1, out_cols, stride=2), :]
        left = jnp.where(first_col, 0.0, pltpu.roll(odd, 1, 1))
        pieces += [left, even, odd]
    patches = jnp.concatenate(
        [p.astype(jnp.bfloat16).reshape(out_rows * out_cols, inputs) for p in pieces], axis=-1
    )
    total = jnp.dot(patches, w_ref[...], preferred_element_type=jnp.float32)
    hidden = jnp.maximum(total, 0.0).astype(jnp.bfloat16).reshape(out_rows, out_cols, -1)
    half = low_ref.shape[-1]
    low_ref[...] = hidden[..., :half]
    high_ref[...] = hidden[..., half:]


def first_row_kernel(x_ref, up_ref, w_ref, _low, _high, low_ref, high_ref, scratch):
    images, _, width, inputs = x_ref.shape
    out_cols = width // 2
    scratch[:, 0] = up_ref[:, 0].astype(jnp.float32)
    scratch[:, 1:] = x_ref[...].astype(jnp.float32)
    first_col = lax.broadcasted_iota(jnp.int32, (images, out_cols, inputs), 1) == 0
    pieces = []
    for tap_row in range(3):
        even = scratch[:, tap_row, pl.ds(0, out_cols, stride=2), :]
        odd = scratch[:, tap_row, pl.ds(1, out_cols, stride=2), :]
        left = jnp.where(first_col, 0.0, pltpu.roll(odd, 1, 1))
        pieces += [left, even, odd]
    patches = jnp.concatenate(
        [p.astype(jnp.bfloat16).reshape(images * out_cols, inputs) for p in pieces], axis=-1
    )
    total = jnp.dot(patches, w_ref[...], preferred_element_type=jnp.float32)
    hidden = jnp.maximum(total, 0.0).astype(jnp.bfloat16).reshape(images, 1, out_cols, -1)
    half = low_ref.shape[-1]
    low_ref[...] = hidden[..., :half]
    high_ref[...] = hidden[..., half:]


def first_stage(maps, upper_row, first_weight, part):
    images, rows, width, inputs = maps.shape
    outputs = first_weight.shape[3]
    weight = first_weight.reshape(9 * inputs, outputs)
    shape = jax.ShapeDtypeStruct((images, rows // 2, width // 2, part), jnp.bfloat16)
    params = pltpu.CompilerParams(dimension_semantics=("arbitrary",), vmem_limit_bytes=60 * 1024 * 1024)
    weight_spec = pl.BlockSpec((9 * inputs, outputs), lambda n: (0, 0))

    def cost(out_rows):
        return pl.CostEstimate(
            flops=2 * images * out_rows * (width // 2) * 9 * inputs * outputs,
            transcendentals=0,
            bytes_accessed=images * out_rows * 2 * width * inputs * 2 + images * out_rows * (width // 2) * outputs * 2,
        )

    out_block = pl.BlockSpec((None, rows // 2, width // 2, part), lambda n: (n, 0, 0, 0))
    low, high = pl.pallas_call(
        first_kernel,
        grid=(images,),
        in_specs=[pl.BlockSpec((None, rows, width, inputs), lambda n: (n, 0, 0, 0)), weight_spec],
        out_specs=[out_block, out_block],
        out_shape=[shape, shape],
        scratch_shapes=[pltpu.VMEM((rows + 1, width, inputs), jnp.float32)],
        compiler_params=params,
        cost_estimate=cost(rows // 2),
    )(maps, weight)
    row_block = pl.BlockSpec((images, 1, width // 2, part), lambda n: (0, 0, 0, 0))
    anywhere = pl.BlockSpec(memory_space=pl.ANY)
    return pl.pallas_call(
        first_row_kernel,
        grid=(1,),
        in_specs=[
            pl.BlockSpec((images, 2, width, inputs), lambda n: (0, 0, 0, 0)),
            pl.BlockSpec((images, 1, width, inputs), lambda n: (0, 0, 0, 0)),
            weight_spec,
            anywhere,
            anywhere,
        ],
        out_specs=[row_block, row_block],
        out_shape=[shape, shape],
        scratch_shapes=[pltpu.VMEM((images, 3, width, inputs), jnp.float32)],
        input_output_aliases={3: 0, 4: 1},
        compiler_params=params,
        cost_estimate=cost(1),
    )(maps, upper_row, weight, low, high)


def second_kernel(*refs, rows, carry):
    if carry:
        src_ref, weight_ref, grad_ref, prev_ref, out_ref, wgrad_ref, acc_ref = refs
    else:
        src_ref, weight_ref, grad_ref, out_ref, wgrad_ref, acc_ref = refs
    step = pl.program_id(1)
    _, width, outputs = out_ref.shape
    inputs = src_ref.shape[-1]
    patches = jnp.concatenate(
        [
            src_ref[tap % 3, pl.ds(step * rows + tap // 3, rows)].reshape(rows * width, inputs)
            for tap in range(9)
        ],
        axis=-1,
    )
    total = jnp.dot(patches, weight_ref[...], preferred_element_type=jnp.float32)
    if carry:
        total = total + prev_ref[...].reshape(rows * width, outputs)
    out_ref[...] = total.astype(out_ref.dtype).reshape(rows, width, outputs)
    term = lax.dot_general(
        patches, grad_ref[...], (((0,), (0,)), ((), ())), preferred_element_type=jnp.float32
    )

    @pl.when(step == 0)
    def _():
        acc_ref[...] = term

    @pl.when(step > 0)
    def _():
        acc_ref[...] += term

    @pl.when(step == pl.num_programs(1) - 1)
    def _():
        wgrad_ref[...] = acc_ref[...].T


def second_stage(hidden, weight, grad, prev, out_dtype):
    owned, out_rows, out_cols, inputs = hidden.shape
    outputs = weight.shape[-1]
    rows = min(32, out_rows)
    row_padded = jnp.pad(hidden, ((0, 0), (1, 1), (0, 0), (0, 0)))
    shifted = jnp.stack([shift_cols_right(row_padded), row_padded, shift_cols_left(row_padded)], axis=1)
    full = pl.BlockSpec((None, 3, out_rows + 2, out_cols, inputs), lambda n, i: (n, 0, 0, 0, 0))
    block = pl.BlockSpec((None, rows, out_cols, outputs), lambda n, i: (n, i, 0, 0))
    in_specs = [
        full,
        pl.BlockSpec((9 * inputs, outputs), lambda n, i: (0, 0)),
        pl.BlockSpec((None, rows * out_cols, outputs), lambda n, i: (n, i, 0)),
    ]
    operands = [shifted, weight.reshape(9 * inputs, outputs), grad]
    if prev is not None:
        in_specs.append(block)
        operands.append(prev)
    flops = 4 * owned * out_rows * out_cols * 9 * inputs * outputs
    return pl.pallas_call(
        functools.partial(second_kernel, rows=rows, carry=prev is not None),
        grid=(owned, out_rows // rows),
        in_specs=in_specs,
        out_specs=[block, pl.BlockSpec((None, outputs, 9 * inputs), lambda n, i: (n, 0, 0))],
        out_shape=[
            jax.ShapeDtypeStruct((owned, out_rows, out_cols, outputs), out_dtype),
            jax.ShapeDtypeStruct((owned, outputs, 9 * inputs), jnp.float32),
        ],
        scratch_shapes=[pltpu.VMEM((9 * inputs, outputs), jnp.float32)],
        compiler_params=pltpu.CompilerParams(
            dimension_semantics=("arbitrary", "arbitrary"), vmem_limit_bytes=60 * 1024 * 1024
        ),
        cost_estimate=pl.CostEstimate(
            flops=flops,
            transcendentals=0,
            bytes_accessed=hidden.size * 2 * 4 + owned * out_rows * out_cols * outputs * 8
            + owned * outputs * 9 * inputs * 4,
        ),
    )(*operands)


def halving_reduce_scatter(partial, axes, swap=False):
    devices = lax.axis_size(axes)
    tiles = lax.axis_size(axes[-1])
    bits = devices.bit_length() - 1
    me = lax.axis_index(axes)
    core = tiles.bit_length() - 1
    high = [b for b in range(bits) if b > core]
    low = [b for b in range(core)]
    order = [core] + (low[:1] + high + low[1:] if swap else high + low)
    rows = partial.shape[0] // devices
    buf = partial.reshape((2,) * bits + (rows,) + partial.shape[1:])
    remaining = list(range(bits - 1, -1, -1))
    for bit in order:
        axis = remaining.index(bit)
        mine = (me >> bit) & 1
        keep = lax.dynamic_index_in_dim(buf, mine, axis=axis, keepdims=False)
        send = lax.dynamic_index_in_dim(buf, 1 - mine, axis=axis, keepdims=False)
        pairs = [(i, i ^ (1 << bit)) for i in range(devices)]
        buf = keep + lax.ppermute(send, axes, pairs)
        remaining.pop(axis)
    return buf


def local(maps, first_weight, second_weight, out_grad):
    tiles = lax.axis_size("tile")
    images, height, width, inputs = maps.shape
    outputs = first_weight.shape[3]
    owned = images // tiles
    half_rows = height // 2
    chunks = 2
    part = outputs // chunks
    upper_row = shifted_2(maps[:, height - 1 : height], "tile", 1)
    grad = out_grad.reshape(owned, -1, outputs)
    conv = None
    pieces = []
    halves = first_stage(maps, upper_row, first_weight, part)
    for chunk in range(chunks):
        channels = slice(chunk * part, (chunk + 1) * part)
        local_hidden = halves[chunk]
        arrived = lax.all_to_all(
            local_hidden.reshape(tiles, owned, half_rows, width // 2, part),
            "tile",
            split_axis=0,
            concat_axis=2,
            tiled=True,
        )
        if conv is not None:
            arrived, conv = lax.optimization_barrier((arrived, conv))
        hidden = arrived.reshape(owned, half_rows * tiles, width // 2, part)
        last = chunk == chunks - 1
        conv, partial = second_stage(
            hidden, second_weight[:, :, channels], grad, conv, jnp.bfloat16 if last else jnp.float32
        )
        summed = halving_reduce_scatter(
            partial.sum(axis=0).reshape(outputs, 9 * part), ("group", "tile"), swap=chunk % 2 == 1
        )
        pieces.append(summed.reshape(-1, 9, part))
    weight_grad = jnp.concatenate(pieces, axis=-1).reshape(-1, 3, 3, outputs)
    return (conv, weight_grad)


def solution(mesh):
    return jax.shard_map(
        local,
        mesh=mesh,
        in_specs=(P("group", "tile", None, None), P(), P(), P(("group", "tile"), None, None, None)),
        out_specs=(P(("group", "tile"), None, None, None), P(("group", "tile"), None, None, None)),
        check_vma=False,
    )
```

```python
import functools

import jax
import jax.numpy as jnp
from jax import lax
from jax.experimental import pallas as pl
from jax.experimental.pallas import tpu as pltpu
from jax.sharding import PartitionSpec as P


def shifted_2(shard, axis, by):
    length = lax.axis_size(axis)
    pairs = [(i, i + by) for i in range(length) if 0 <= i + by < length]
    return lax.ppermute(shard, axis, pairs)


def shift_cols_right(slab):
    zero_col = jnp.zeros_like(slab[:, :, :1])
    return jnp.concatenate([zero_col, slab[:, :, :-1]], axis=2)


def shift_cols_left(slab):
    zero_col = jnp.zeros_like(slab[:, :, :1])
    return jnp.concatenate([slab[:, :, 1:], zero_col], axis=2)


def first_conv(source, upper_row, first_weight):
    images, rows, width, inputs = source.shape
    outputs = first_weight.shape[3]
    paired = source.reshape(images, rows // 2, 2, width // 2, 2 * inputs)
    even_rows = paired[:, :, 0]
    odd_rows = paired[:, :, 1]
    upper_paired = upper_row.reshape(images, 1, width // 2, 2 * inputs)
    odd_above = jnp.concatenate([upper_paired, odd_rows[:, :-1]], axis=1)
    sources = [odd_above, even_rows, odd_rows]
    total = jnp.zeros((images, rows // 2, width // 2, outputs), jnp.float32)
    for tap_row in range(3):
        wide_kernel = first_weight[tap_row, 1:3].reshape(2 * inputs, outputs)
        total = total + jnp.dot(sources[tap_row], wide_kernel, preferred_element_type=jnp.float32)
    halves = jnp.concatenate([piece[..., inputs:] for piece in sources], axis=-1)
    narrow_kernel = first_weight[:, 0].reshape(3 * inputs, outputs)
    total = total + jnp.dot(
        shift_cols_right(halves), narrow_kernel, preferred_element_type=jnp.float32
    )
    return jnp.maximum(total, 0.0).astype(jnp.bfloat16)


def first_kernel(x_ref, w_ref, low_ref, high_ref, scratch):
    rows, width, inputs = x_ref.shape
    out_rows, out_cols = rows // 2, width // 2
    scratch[0] = jnp.zeros(scratch.shape[1:], jnp.float32)
    scratch[1:] = x_ref[...].astype(jnp.float32)
    first_col = lax.broadcasted_iota(jnp.int32, (out_rows, out_cols, inputs), 1) == 0
    pieces = []
    for tap_row in range(3):
        even = scratch[pl.ds(tap_row, out_rows, stride=2), pl.ds(0, out_cols, stride=2), :]
        odd = scratch[pl.ds(tap_row, out_rows, stride=2), pl.ds(1, out_cols, stride=2), :]
        left = jnp.where(first_col, 0.0, pltpu.roll(odd, 1, 1))
        pieces += [left, even, odd]
    patches = jnp.concatenate(
        [p.astype(jnp.bfloat16).reshape(out_rows * out_cols, inputs) for p in pieces], axis=-1
    )
    total = jnp.dot(patches, w_ref[...], preferred_element_type=jnp.float32)
    hidden = jnp.maximum(total, 0.0).astype(jnp.bfloat16).reshape(out_rows, out_cols, -1)
    half = low_ref.shape[-1]
    low_ref[...] = hidden[..., :half]
    high_ref[...] = hidden[..., half:]


def first_row_kernel(x_ref, up_ref, w_ref, _low, _high, low_ref, high_ref, scratch):
    images, _, width, inputs = x_ref.shape
    out_cols = width // 2
    scratch[:, 0] = up_ref[:, 0].astype(jnp.float32)
    scratch[:, 1:] = x_ref[...].astype(jnp.float32)
    first_col = lax.broadcasted_iota(jnp.int32, (images, out_cols, inputs), 1) == 0
    pieces = []
    for tap_row in range(3):
        even = scratch[:, tap_row, pl.ds(0, out_cols, stride=2), :]
        odd = scratch[:, tap_row, pl.ds(1, out_cols, stride=2), :]
        left = jnp.where(first_col, 0.0, pltpu.roll(odd, 1, 1))
        pieces += [left, even, odd]
    patches = jnp.concatenate(
        [p.astype(jnp.bfloat16).reshape(images * out_cols, inputs) for p in pieces], axis=-1
    )
    total = jnp.dot(patches, w_ref[...], preferred_element_type=jnp.float32)
    hidden = jnp.maximum(total, 0.0).astype(jnp.bfloat16).reshape(images, 1, out_cols, -1)
    half = low_ref.shape[-1]
    low_ref[...] = hidden[..., :half]
    high_ref[...] = hidden[..., half:]


def first_stage(maps, upper_row, first_weight, part):
    images, rows, width, inputs = maps.shape
    outputs = first_weight.shape[3]
    weight = first_weight.reshape(9 * inputs, outputs)
    shape = jax.ShapeDtypeStruct((images, rows // 2, width // 2, part), jnp.bfloat16)
    params = pltpu.CompilerParams(dimension_semantics=("arbitrary",), vmem_limit_bytes=60 * 1024 * 1024)
    weight_spec = pl.BlockSpec((9 * inputs, outputs), lambda n: (0, 0))

    def cost(out_rows):
        return pl.CostEstimate(
            flops=2 * images * out_rows * (width // 2) * 9 * inputs * outputs,
            transcendentals=0,
            bytes_accessed=images * out_rows * 2 * width * inputs * 2 + images * out_rows * (width // 2) * outputs * 2,
        )

    out_block = pl.BlockSpec((None, rows // 2, width // 2, part), lambda n: (n, 0, 0, 0))
    low, high = pl.pallas_call(
        first_kernel,
        grid=(images,),
        in_specs=[pl.BlockSpec((None, rows, width, inputs), lambda n: (n, 0, 0, 0)), weight_spec],
        out_specs=[out_block, out_block],
        out_shape=[shape, shape],
        scratch_shapes=[pltpu.VMEM((rows + 1, width, inputs), jnp.float32)],
        compiler_params=params,
        cost_estimate=cost(rows // 2),
    )(maps, weight)
    row_block = pl.BlockSpec((images, 1, width // 2, part), lambda n: (0, 0, 0, 0))
    anywhere = pl.BlockSpec(memory_space=pl.ANY)
    return pl.pallas_call(
        first_row_kernel,
        grid=(1,),
        in_specs=[
            pl.BlockSpec((images, 2, width, inputs), lambda n: (0, 0, 0, 0)),
            pl.BlockSpec((images, 1, width, inputs), lambda n: (0, 0, 0, 0)),
            weight_spec,
            anywhere,
            anywhere,
        ],
        out_specs=[row_block, row_block],
        out_shape=[shape, shape],
        scratch_shapes=[pltpu.VMEM((images, 3, width, inputs), jnp.float32)],
        input_output_aliases={3: 0, 4: 1},
        compiler_params=params,
        cost_estimate=cost(1),
    )(maps, upper_row, weight, low, high)


def second_kernel(*refs, rows, carry):
    if carry:
        src_ref, weight_ref, grad_ref, prev_ref, out_ref, wgrad_ref, acc_ref = refs
    else:
        src_ref, weight_ref, grad_ref, out_ref, wgrad_ref, acc_ref = refs
    step = pl.program_id(1)
    _, width, outputs = out_ref.shape
    inputs = src_ref.shape[-1]
    patches = jnp.concatenate(
        [
            src_ref[tap % 3, pl.ds(step * rows + tap // 3, rows)].reshape(rows * width, inputs)
            for tap in range(9)
        ],
        axis=-1,
    )
    total = jnp.dot(patches, weight_ref[...], preferred_element_type=jnp.float32)
    if carry:
        total = total + prev_ref[...].reshape(rows * width, outputs)
    out_ref[...] = total.astype(out_ref.dtype).reshape(rows, width, outputs)
    term = lax.dot_general(
        patches, grad_ref[...], (((0,), (0,)), ((), ())), preferred_element_type=jnp.float32
    )

    @pl.when(step == 0)
    def _():
        acc_ref[...] = term

    @pl.when(step > 0)
    def _():
        acc_ref[...] += term

    @pl.when(step == pl.num_programs(1) - 1)
    def _():
        wgrad_ref[...] = acc_ref[...].T


def second_stage(hidden, weight, grad, prev, out_dtype):
    owned, out_rows, out_cols, inputs = hidden.shape
    outputs = weight.shape[-1]
    rows = min(32, out_rows)
    row_padded = jnp.pad(hidden, ((0, 0), (1, 1), (0, 0), (0, 0)))
    shifted = jnp.stack([shift_cols_right(row_padded), row_padded, shift_cols_left(row_padded)], axis=1)
    full = pl.BlockSpec((None, 3, out_rows + 2, out_cols, inputs), lambda n, i: (n, 0, 0, 0, 0))
    block = pl.BlockSpec((None, rows, out_cols, outputs), lambda n, i: (n, i, 0, 0))
    in_specs = [
        full,
        pl.BlockSpec((9 * inputs, outputs), lambda n, i: (0, 0)),
        pl.BlockSpec((None, rows * out_cols, outputs), lambda n, i: (n, i, 0)),
    ]
    operands = [shifted, weight.reshape(9 * inputs, outputs), grad]
    if prev is not None:
        in_specs.append(block)
        operands.append(prev)
    flops = 4 * owned * out_rows * out_cols * 9 * inputs * outputs
    return pl.pallas_call(
        functools.partial(second_kernel, rows=rows, carry=prev is not None),
        grid=(owned, out_rows // rows),
        in_specs=in_specs,
        out_specs=[block, pl.BlockSpec((None, outputs, 9 * inputs), lambda n, i: (n, 0, 0))],
        out_shape=[
            jax.ShapeDtypeStruct((owned, out_rows, out_cols, outputs), out_dtype),
            jax.ShapeDtypeStruct((owned, outputs, 9 * inputs), jnp.float32),
        ],
        scratch_shapes=[pltpu.VMEM((9 * inputs, outputs), jnp.float32)],
        compiler_params=pltpu.CompilerParams(
            dimension_semantics=("arbitrary", "arbitrary"), vmem_limit_bytes=60 * 1024 * 1024
        ),
        cost_estimate=pl.CostEstimate(
            flops=flops,
            transcendentals=0,
            bytes_accessed=hidden.size * 2 * 4 + owned * out_rows * out_cols * outputs * 8
            + owned * outputs * 9 * inputs * 4,
        ),
    )(*operands)


def halving_reduce_scatter(partial, axes, swap=False):
    devices = lax.axis_size(axes)
    tiles = lax.axis_size(axes[-1])
    bits = devices.bit_length() - 1
    me = lax.axis_index(axes)
    core = tiles.bit_length() - 1
    high = [b for b in range(bits) if b > core]
    low = [b for b in range(core)]
    order = [core] + (low[:2] + high + low[2:] if swap else high + low)
    rows = partial.shape[0] // devices
    buf = partial.reshape((2,) * bits + (rows,) + partial.shape[1:])
    remaining = list(range(bits - 1, -1, -1))
    for bit in order:
        axis = remaining.index(bit)
        mine = (me >> bit) & 1
        keep = lax.dynamic_index_in_dim(buf, mine, axis=axis, keepdims=False)
        send = lax.dynamic_index_in_dim(buf, 1 - mine, axis=axis, keepdims=False)
        pairs = [(i, i ^ (1 << bit)) for i in range(devices)]
        buf = keep + lax.ppermute(send, axes, pairs)
        remaining.pop(axis)
    return buf


def local(maps, first_weight, second_weight, out_grad):
    tiles = lax.axis_size("tile")
    images, height, width, inputs = maps.shape
    outputs = first_weight.shape[3]
    owned = images // tiles
    half_rows = height // 2
    chunks = 2
    part = outputs // chunks
    upper_row = shifted_2(maps[:, height - 1 : height], "tile", 1)
    grad = out_grad.reshape(owned, -1, outputs)
    conv = None
    pieces = []
    halves = first_stage(maps, upper_row, first_weight, part)
    for chunk in range(chunks):
        channels = slice(chunk * part, (chunk + 1) * part)
        local_hidden = halves[chunk]
        arrived = lax.all_to_all(
            local_hidden.reshape(tiles, owned, half_rows, width // 2, part),
            "tile",
            split_axis=0,
            concat_axis=2,
            tiled=True,
        )
        if conv is not None:
            arrived, conv = lax.optimization_barrier((arrived, conv))
        hidden = arrived.reshape(owned, half_rows * tiles, width // 2, part)
        last = chunk == chunks - 1
        conv, partial = second_stage(
            hidden, second_weight[:, :, channels], grad, conv, jnp.bfloat16 if last else jnp.float32
        )
        summed = halving_reduce_scatter(
            partial.sum(axis=0).reshape(outputs, 9 * part), ("group", "tile"), swap=chunk % 2 == 1
        )
        pieces.append(summed.reshape(-1, 9, part))
    weight_grad = jnp.concatenate(pieces, axis=-1).reshape(-1, 3, 3, outputs)
    return (conv, weight_grad)


def solution(mesh):
    return jax.shard_map(
        local,
        mesh=mesh,
        in_specs=(P("group", "tile", None, None), P(), P(), P(("group", "tile"), None, None, None)),
        out_specs=(P(("group", "tile"), None, None, None), P(("group", "tile"), None, None, None)),
        check_vma=False,
    )
```

```python
import functools

import jax
import jax.numpy as jnp
from jax import lax
from jax.experimental import pallas as pl
from jax.experimental.pallas import tpu as pltpu
from jax.sharding import PartitionSpec as P


def shifted_2(shard, axis, by):
    length = lax.axis_size(axis)
    pairs = [(i, i + by) for i in range(length) if 0 <= i + by < length]
    return lax.ppermute(shard, axis, pairs)


def shift_cols_right(slab):
    zero_col = jnp.zeros_like(slab[:, :, :1])
    return jnp.concatenate([zero_col, slab[:, :, :-1]], axis=2)


def shift_cols_left(slab):
    zero_col = jnp.zeros_like(slab[:, :, :1])
    return jnp.concatenate([slab[:, :, 1:], zero_col], axis=2)


def first_conv(source, upper_row, first_weight):
    images, rows, width, inputs = source.shape
    outputs = first_weight.shape[3]
    paired = source.reshape(images, rows // 2, 2, width // 2, 2 * inputs)
    even_rows = paired[:, :, 0]
    odd_rows = paired[:, :, 1]
    upper_paired = upper_row.reshape(images, 1, width // 2, 2 * inputs)
    odd_above = jnp.concatenate([upper_paired, odd_rows[:, :-1]], axis=1)
    sources = [odd_above, even_rows, odd_rows]
    total = jnp.zeros((images, rows // 2, width // 2, outputs), jnp.float32)
    for tap_row in range(3):
        wide_kernel = first_weight[tap_row, 1:3].reshape(2 * inputs, outputs)
        total = total + jnp.dot(sources[tap_row], wide_kernel, preferred_element_type=jnp.float32)
    halves = jnp.concatenate([piece[..., inputs:] for piece in sources], axis=-1)
    narrow_kernel = first_weight[:, 0].reshape(3 * inputs, outputs)
    total = total + jnp.dot(
        shift_cols_right(halves), narrow_kernel, preferred_element_type=jnp.float32
    )
    return jnp.maximum(total, 0.0).astype(jnp.bfloat16)


def first_kernel(x_ref, w_ref, low_ref, high_ref, scratch):
    images, rows, width, inputs = x_ref.shape
    out_rows, out_cols = rows // 2, width // 2
    scratch[:, 0] = jnp.zeros((images,) + scratch.shape[2:], jnp.float32)
    scratch[:, 1:] = x_ref[...].astype(jnp.float32)
    first_col = lax.broadcasted_iota(jnp.int32, (images, out_rows, out_cols, inputs), 2) == 0
    pieces = []
    for tap_row in range(3):
        even = scratch[:, pl.ds(tap_row, out_rows, stride=2), pl.ds(0, out_cols, stride=2), :]
        odd = scratch[:, pl.ds(tap_row, out_rows, stride=2), pl.ds(1, out_cols, stride=2), :]
        left = jnp.where(first_col, 0.0, pltpu.roll(odd, 1, 2))
        pieces += [left, even, odd]
    patches = jnp.concatenate(
        [p.astype(jnp.bfloat16).reshape(images * out_rows * out_cols, inputs) for p in pieces], axis=-1
    )
    total = jnp.dot(patches, w_ref[...], preferred_element_type=jnp.float32)
    hidden = jnp.maximum(total, 0.0).astype(jnp.bfloat16).reshape(images, out_rows, out_cols, -1)
    half = low_ref.shape[-1]
    low_ref[...] = hidden[..., :half]
    high_ref[...] = hidden[..., half:]


def first_row_kernel(x_ref, up_ref, w_ref, _low, _high, low_ref, high_ref, scratch):
    images, _, width, inputs = x_ref.shape
    out_cols = width // 2
    scratch[:, 0] = up_ref[:, 0].astype(jnp.float32)
    scratch[:, 1:] = x_ref[...].astype(jnp.float32)
    first_col = lax.broadcasted_iota(jnp.int32, (images, out_cols, inputs), 1) == 0
    pieces = []
    for tap_row in range(3):
        even = scratch[:, tap_row, pl.ds(0, out_cols, stride=2), :]
        odd = scratch[:, tap_row, pl.ds(1, out_cols, stride=2), :]
        left = jnp.where(first_col, 0.0, pltpu.roll(odd, 1, 1))
        pieces += [left, even, odd]
    patches = jnp.concatenate(
        [p.astype(jnp.bfloat16).reshape(images * out_cols, inputs) for p in pieces], axis=-1
    )
    total = jnp.dot(patches, w_ref[...], preferred_element_type=jnp.float32)
    hidden = jnp.maximum(total, 0.0).astype(jnp.bfloat16).reshape(images, 1, out_cols, -1)
    half = low_ref.shape[-1]
    low_ref[...] = hidden[..., :half]
    high_ref[...] = hidden[..., half:]


def first_stage(maps, upper_row, first_weight, part):
    images, rows, width, inputs = maps.shape
    outputs = first_weight.shape[3]
    weight = first_weight.reshape(9 * inputs, outputs)
    shape = jax.ShapeDtypeStruct((images, rows // 2, width // 2, part), jnp.bfloat16)
    params = pltpu.CompilerParams(dimension_semantics=("arbitrary",), vmem_limit_bytes=60 * 1024 * 1024)
    weight_spec = pl.BlockSpec((9 * inputs, outputs), lambda n: (0, 0))

    def cost(out_rows):
        return pl.CostEstimate(
            flops=2 * images * out_rows * (width // 2) * 9 * inputs * outputs,
            transcendentals=0,
            bytes_accessed=images * out_rows * 2 * width * inputs * 2 + images * out_rows * (width // 2) * outputs * 2,
        )

    per = 2 if images % 2 == 0 else 1
    out_block = pl.BlockSpec((per, rows // 2, width // 2, part), lambda n: (n, 0, 0, 0))
    low, high = pl.pallas_call(
        first_kernel,
        grid=(images // per,),
        in_specs=[pl.BlockSpec((per, rows, width, inputs), lambda n: (n, 0, 0, 0)), weight_spec],
        out_specs=[out_block, out_block],
        out_shape=[shape, shape],
        scratch_shapes=[pltpu.VMEM((per, rows + 1, width, inputs), jnp.float32)],
        compiler_params=params,
        cost_estimate=cost(rows // 2),
    )(maps, weight)
    row_block = pl.BlockSpec((images, 1, width // 2, part), lambda n: (0, 0, 0, 0))
    anywhere = pl.BlockSpec(memory_space=pl.ANY)
    return pl.pallas_call(
        first_row_kernel,
        grid=(1,),
        in_specs=[
            pl.BlockSpec((images, 2, width, inputs), lambda n: (0, 0, 0, 0)),
            pl.BlockSpec((images, 1, width, inputs), lambda n: (0, 0, 0, 0)),
            weight_spec,
            anywhere,
            anywhere,
        ],
        out_specs=[row_block, row_block],
        out_shape=[shape, shape],
        scratch_shapes=[pltpu.VMEM((images, 3, width, inputs), jnp.float32)],
        input_output_aliases={3: 0, 4: 1},
        compiler_params=params,
        cost_estimate=cost(1),
    )(maps, upper_row, weight, low, high)


def second_kernel(*refs, rows, carry):
    if carry:
        src_ref, weight_ref, grad_ref, prev_ref, out_ref, wgrad_ref, acc_ref = refs
    else:
        src_ref, weight_ref, grad_ref, out_ref, wgrad_ref, acc_ref = refs
    step = pl.program_id(1)
    _, width, outputs = out_ref.shape
    inputs = src_ref.shape[-1]
    patches = jnp.concatenate(
        [
            src_ref[tap % 3, pl.ds(step * rows + tap // 3, rows)].reshape(rows * width, inputs)
            for tap in range(9)
        ],
        axis=-1,
    )
    total = jnp.dot(patches, weight_ref[...], preferred_element_type=jnp.float32)
    if carry:
        total = total + prev_ref[...].reshape(rows * width, outputs)
    out_ref[...] = total.astype(out_ref.dtype).reshape(rows, width, outputs)
    term = lax.dot_general(
        patches, grad_ref[...], (((0,), (0,)), ((), ())), preferred_element_type=jnp.float32
    )

    @pl.when(step == 0)
    def _():
        acc_ref[...] = term

    @pl.when(step > 0)
    def _():
        acc_ref[...] += term

    @pl.when(step == pl.num_programs(1) - 1)
    def _():
        wgrad_ref[...] = acc_ref[...].T


def second_stage(hidden, weight, grad, prev, out_dtype):
    owned, out_rows, out_cols, inputs = hidden.shape
    outputs = weight.shape[-1]
    rows = min(32, out_rows)
    row_padded = jnp.pad(hidden, ((0, 0), (1, 1), (0, 0), (0, 0)))
    shifted = jnp.stack([shift_cols_right(row_padded), row_padded, shift_cols_left(row_padded)], axis=1)
    full = pl.BlockSpec((None, 3, out_rows + 2, out_cols, inputs), lambda n, i: (n, 0, 0, 0, 0))
    block = pl.BlockSpec((None, rows, out_cols, outputs), lambda n, i: (n, i, 0, 0))
    in_specs = [
        full,
        pl.BlockSpec((9 * inputs, outputs), lambda n, i: (0, 0)),
        pl.BlockSpec((None, rows * out_cols, outputs), lambda n, i: (n, i, 0)),
    ]
    operands = [shifted, weight.reshape(9 * inputs, outputs), grad]
    if prev is not None:
        in_specs.append(block)
        operands.append(prev)
    flops = 4 * owned * out_rows * out_cols * 9 * inputs * outputs
    return pl.pallas_call(
        functools.partial(second_kernel, rows=rows, carry=prev is not None),
        grid=(owned, out_rows // rows),
        in_specs=in_specs,
        out_specs=[block, pl.BlockSpec((None, outputs, 9 * inputs), lambda n, i: (n, 0, 0))],
        out_shape=[
            jax.ShapeDtypeStruct((owned, out_rows, out_cols, outputs), out_dtype),
            jax.ShapeDtypeStruct((owned, outputs, 9 * inputs), jnp.float32),
        ],
        scratch_shapes=[pltpu.VMEM((9 * inputs, outputs), jnp.float32)],
        compiler_params=pltpu.CompilerParams(
            dimension_semantics=("arbitrary", "arbitrary"), vmem_limit_bytes=60 * 1024 * 1024
        ),
        cost_estimate=pl.CostEstimate(
            flops=flops,
            transcendentals=0,
            bytes_accessed=hidden.size * 2 * 4 + owned * out_rows * out_cols * outputs * 8
            + owned * outputs * 9 * inputs * 4,
        ),
    )(*operands)


def halving_reduce_scatter(partial, axes, swap=False):
    devices = lax.axis_size(axes)
    tiles = lax.axis_size(axes[-1])
    bits = devices.bit_length() - 1
    me = lax.axis_index(axes)
    core = tiles.bit_length() - 1
    high = [b for b in range(bits) if b > core]
    low = [b for b in range(core)]
    order = [core] + (low[:1] + high + low[1:] if swap else high + low)
    rows = partial.shape[0] // devices
    buf = partial.reshape((2,) * bits + (rows,) + partial.shape[1:])
    remaining = list(range(bits - 1, -1, -1))
    for bit in order:
        axis = remaining.index(bit)
        mine = (me >> bit) & 1
        keep = lax.dynamic_index_in_dim(buf, mine, axis=axis, keepdims=False)
        send = lax.dynamic_index_in_dim(buf, 1 - mine, axis=axis, keepdims=False)
        pairs = [(i, i ^ (1 << bit)) for i in range(devices)]
        buf = keep + lax.ppermute(send, axes, pairs)
        remaining.pop(axis)
    return buf


def local(maps, first_weight, second_weight, out_grad):
    tiles = lax.axis_size("tile")
    images, height, width, inputs = maps.shape
    outputs = first_weight.shape[3]
    owned = images // tiles
    half_rows = height // 2
    chunks = 2
    part = outputs // chunks
    upper_row = shifted_2(maps[:, height - 1 : height], "tile", 1)
    grad = out_grad.reshape(owned, -1, outputs)
    conv = None
    pieces = []
    halves = first_stage(maps, upper_row, first_weight, part)
    for chunk in range(chunks):
        channels = slice(chunk * part, (chunk + 1) * part)
        local_hidden = halves[chunk]
        arrived = lax.all_to_all(
            local_hidden.reshape(tiles, owned, half_rows, width // 2, part),
            "tile",
            split_axis=0,
            concat_axis=2,
            tiled=True,
        )
        if conv is not None:
            arrived, conv = lax.optimization_barrier((arrived, conv))
        hidden = arrived.reshape(owned, half_rows * tiles, width // 2, part)
        last = chunk == chunks - 1
        conv, partial = second_stage(
            hidden, second_weight[:, :, channels], grad, conv, jnp.bfloat16 if last else jnp.float32
        )
        summed = halving_reduce_scatter(
            partial.sum(axis=0).reshape(outputs, 9 * part), ("group", "tile"), swap=chunk % 2 == 1
        )
        pieces.append(summed.reshape(-1, 9, part))
    weight_grad = jnp.concatenate(pieces, axis=-1).reshape(-1, 3, 3, outputs)
    return (conv, weight_grad)


def solution(mesh):
    return jax.shard_map(
        local,
        mesh=mesh,
        in_specs=(P("group", "tile", None, None), P(), P(), P(("group", "tile"), None, None, None)),
        out_specs=(P(("group", "tile"), None, None, None), P(("group", "tile"), None, None, None)),
        check_vma=False,
    )
```

```python
import functools

import jax
import jax.numpy as jnp
from jax import lax
from jax.experimental import pallas as pl
from jax.experimental.pallas import tpu as pltpu
from jax.sharding import PartitionSpec as P


def shifted_2(shard, axis, by):
    length = lax.axis_size(axis)
    pairs = [(i, i + by) for i in range(length) if 0 <= i + by < length]
    return lax.ppermute(shard, axis, pairs)


def shift_cols_right(slab):
    zero_col = jnp.zeros_like(slab[:, :, :1])
    return jnp.concatenate([zero_col, slab[:, :, :-1]], axis=2)


def shift_cols_left(slab):
    zero_col = jnp.zeros_like(slab[:, :, :1])
    return jnp.concatenate([slab[:, :, 1:], zero_col], axis=2)


def first_conv(source, upper_row, first_weight):
    images, rows, width, inputs = source.shape
    outputs = first_weight.shape[3]
    paired = source.reshape(images, rows // 2, 2, width // 2, 2 * inputs)
    even_rows = paired[:, :, 0]
    odd_rows = paired[:, :, 1]
    upper_paired = upper_row.reshape(images, 1, width // 2, 2 * inputs)
    odd_above = jnp.concatenate([upper_paired, odd_rows[:, :-1]], axis=1)
    sources = [odd_above, even_rows, odd_rows]
    total = jnp.zeros((images, rows // 2, width // 2, outputs), jnp.float32)
    for tap_row in range(3):
        wide_kernel = first_weight[tap_row, 1:3].reshape(2 * inputs, outputs)
        total = total + jnp.dot(sources[tap_row], wide_kernel, preferred_element_type=jnp.float32)
    halves = jnp.concatenate([piece[..., inputs:] for piece in sources], axis=-1)
    narrow_kernel = first_weight[:, 0].reshape(3 * inputs, outputs)
    total = total + jnp.dot(
        shift_cols_right(halves), narrow_kernel, preferred_element_type=jnp.float32
    )
    return jnp.maximum(total, 0.0).astype(jnp.bfloat16)


def first_kernel(x_ref, w_ref, low_ref, high_ref, scratch):
    images, rows, width, inputs = x_ref.shape
    out_rows, out_cols = rows // 2, width // 2
    scratch[:, 0] = jnp.zeros((images,) + scratch.shape[2:], jnp.float32)
    scratch[:, 1:] = x_ref[...].astype(jnp.float32)
    first_col = lax.broadcasted_iota(jnp.int32, (images, out_rows, out_cols, inputs), 2) == 0
    pieces = []
    for tap_row in range(3):
        even = scratch[:, pl.ds(tap_row, out_rows, stride=2), pl.ds(0, out_cols, stride=2), :]
        odd = scratch[:, pl.ds(tap_row, out_rows, stride=2), pl.ds(1, out_cols, stride=2), :]
        left = jnp.where(first_col, 0.0, pltpu.roll(odd, 1, 2))
        pieces += [left, even, odd]
    patches = jnp.concatenate(
        [p.astype(jnp.bfloat16).reshape(images * out_rows * out_cols, inputs) for p in pieces], axis=-1
    )
    total = jnp.dot(patches, w_ref[...], preferred_element_type=jnp.float32)
    hidden = jnp.maximum(total, 0.0).astype(jnp.bfloat16).reshape(images, out_rows, out_cols, -1)
    half = low_ref.shape[-1]
    low_ref[...] = hidden[..., :half]
    high_ref[...] = hidden[..., half:]


def first_row_kernel(x_ref, up_ref, w_ref, _low, _high, low_ref, high_ref, scratch):
    images, _, width, inputs = x_ref.shape
    out_cols = width // 2
    scratch[:, 0] = up_ref[:, 0].astype(jnp.float32)
    scratch[:, 1:] = x_ref[...].astype(jnp.float32)
    first_col = lax.broadcasted_iota(jnp.int32, (images, out_cols, inputs), 1) == 0
    pieces = []
    for tap_row in range(3):
        even = scratch[:, tap_row, pl.ds(0, out_cols, stride=2), :]
        odd = scratch[:, tap_row, pl.ds(1, out_cols, stride=2), :]
        left = jnp.where(first_col, 0.0, pltpu.roll(odd, 1, 1))
        pieces += [left, even, odd]
    patches = jnp.concatenate(
        [p.astype(jnp.bfloat16).reshape(images * out_cols, inputs) for p in pieces], axis=-1
    )
    total = jnp.dot(patches, w_ref[...], preferred_element_type=jnp.float32)
    hidden = jnp.maximum(total, 0.0).astype(jnp.bfloat16).reshape(images, 1, out_cols, -1)
    half = low_ref.shape[-1]
    low_ref[...] = hidden[..., :half]
    high_ref[...] = hidden[..., half:]


def first_stage(maps, upper_row, first_weight, part):
    images, rows, width, inputs = maps.shape
    outputs = first_weight.shape[3]
    weight = first_weight.reshape(9 * inputs, outputs)
    shape = jax.ShapeDtypeStruct((images, rows // 2, width // 2, part), jnp.bfloat16)
    params = pltpu.CompilerParams(dimension_semantics=("arbitrary",), vmem_limit_bytes=60 * 1024 * 1024)
    weight_spec = pl.BlockSpec((9 * inputs, outputs), lambda n: (0, 0))

    def cost(out_rows):
        return pl.CostEstimate(
            flops=2 * images * out_rows * (width // 2) * 9 * inputs * outputs,
            transcendentals=0,
            bytes_accessed=images * out_rows * 2 * width * inputs * 2 + images * out_rows * (width // 2) * outputs * 2,
        )

    per = 4 if images % 4 == 0 else 1
    out_block = pl.BlockSpec((per, rows // 2, width // 2, part), lambda n: (n, 0, 0, 0))
    low, high = pl.pallas_call(
        first_kernel,
        grid=(images // per,),
        in_specs=[pl.BlockSpec((per, rows, width, inputs), lambda n: (n, 0, 0, 0)), weight_spec],
        out_specs=[out_block, out_block],
        out_shape=[shape, shape],
        scratch_shapes=[pltpu.VMEM((per, rows + 1, width, inputs), jnp.float32)],
        compiler_params=params,
        cost_estimate=cost(rows // 2),
    )(maps, weight)
    row_block = pl.BlockSpec((images, 1, width // 2, part), lambda n: (0, 0, 0, 0))
    anywhere = pl.BlockSpec(memory_space=pl.ANY)
    return pl.pallas_call(
        first_row_kernel,
        grid=(1,),
        in_specs=[
            pl.BlockSpec((images, 2, width, inputs), lambda n: (0, 0, 0, 0)),
            pl.BlockSpec((images, 1, width, inputs), lambda n: (0, 0, 0, 0)),
            weight_spec,
            anywhere,
            anywhere,
        ],
        out_specs=[row_block, row_block],
        out_shape=[shape, shape],
        scratch_shapes=[pltpu.VMEM((images, 3, width, inputs), jnp.float32)],
        input_output_aliases={3: 0, 4: 1},
        compiler_params=params,
        cost_estimate=cost(1),
    )(maps, upper_row, weight, low, high)


def second_kernel(*refs, rows, carry):
    if carry:
        src_ref, weight_ref, grad_ref, prev_ref, out_ref, wgrad_ref, acc_ref = refs
    else:
        src_ref, weight_ref, grad_ref, out_ref, wgrad_ref, acc_ref = refs
    step = pl.program_id(1)
    _, width, outputs = out_ref.shape
    inputs = src_ref.shape[-1]
    patches = jnp.concatenate(
        [
            src_ref[tap % 3, pl.ds(step * rows + tap // 3, rows)].reshape(rows * width, inputs)
            for tap in range(9)
        ],
        axis=-1,
    )
    total = jnp.dot(patches, weight_ref[...], preferred_element_type=jnp.float32)
    if carry:
        total = total + prev_ref[...].reshape(rows * width, outputs)
    out_ref[...] = total.astype(out_ref.dtype).reshape(rows, width, outputs)
    term = lax.dot_general(
        patches, grad_ref[...], (((0,), (0,)), ((), ())), preferred_element_type=jnp.float32
    )

    @pl.when(step == 0)
    def _():
        acc_ref[...] = term

    @pl.when(step > 0)
    def _():
        acc_ref[...] += term

    @pl.when(step == pl.num_programs(1) - 1)
    def _():
        wgrad_ref[...] = acc_ref[...].T


def second_stage(hidden, weight, grad, prev, out_dtype):
    owned, out_rows, out_cols, inputs = hidden.shape
    outputs = weight.shape[-1]
    rows = min(32, out_rows)
    row_padded = jnp.pad(hidden, ((0, 0), (1, 1), (0, 0), (0, 0)))
    shifted = jnp.stack([shift_cols_right(row_padded), row_padded, shift_cols_left(row_padded)], axis=1)
    full = pl.BlockSpec((None, 3, out_rows + 2, out_cols, inputs), lambda n, i: (n, 0, 0, 0, 0))
    block = pl.BlockSpec((None, rows, out_cols, outputs), lambda n, i: (n, i, 0, 0))
    in_specs = [
        full,
        pl.BlockSpec((9 * inputs, outputs), lambda n, i: (0, 0)),
        pl.BlockSpec((None, rows * out_cols, outputs), lambda n, i: (n, i, 0)),
    ]
    operands = [shifted, weight.reshape(9 * inputs, outputs), grad]
    if prev is not None:
        in_specs.append(block)
        operands.append(prev)
    flops = 4 * owned * out_rows * out_cols * 9 * inputs * outputs
    return pl.pallas_call(
        functools.partial(second_kernel, rows=rows, carry=prev is not None),
        grid=(owned, out_rows // rows),
        in_specs=in_specs,
        out_specs=[block, pl.BlockSpec((None, outputs, 9 * inputs), lambda n, i: (n, 0, 0))],
        out_shape=[
            jax.ShapeDtypeStruct((owned, out_rows, out_cols, outputs), out_dtype),
            jax.ShapeDtypeStruct((owned, outputs, 9 * inputs), jnp.float32),
        ],
        scratch_shapes=[pltpu.VMEM((9 * inputs, outputs), jnp.float32)],
        compiler_params=pltpu.CompilerParams(
            dimension_semantics=("arbitrary", "arbitrary"), vmem_limit_bytes=60 * 1024 * 1024
        ),
        cost_estimate=pl.CostEstimate(
            flops=flops,
            transcendentals=0,
            bytes_accessed=hidden.size * 2 * 4 + owned * out_rows * out_cols * outputs * 8
            + owned * outputs * 9 * inputs * 4,
        ),
    )(*operands)


def halving_reduce_scatter(partial, axes, swap=False):
    devices = lax.axis_size(axes)
    tiles = lax.axis_size(axes[-1])
    bits = devices.bit_length() - 1
    me = lax.axis_index(axes)
    core = tiles.bit_length() - 1
    high = [b for b in range(bits) if b > core]
    low = [b for b in range(core)]
    order = [core] + (low[:1] + high + low[1:] if swap else high + low)
    rows = partial.shape[0] // devices
    buf = partial.reshape((2,) * bits + (rows,) + partial.shape[1:])
    remaining = list(range(bits - 1, -1, -1))
    for bit in order:
        axis = remaining.index(bit)
        mine = (me >> bit) & 1
        keep = lax.dynamic_index_in_dim(buf, mine, axis=axis, keepdims=False)
        send = lax.dynamic_index_in_dim(buf, 1 - mine, axis=axis, keepdims=False)
        pairs = [(i, i ^ (1 << bit)) for i in range(devices)]
        buf = keep + lax.ppermute(send, axes, pairs)
        remaining.pop(axis)
    return buf


def local(maps, first_weight, second_weight, out_grad):
    tiles = lax.axis_size("tile")
    images, height, width, inputs = maps.shape
    outputs = first_weight.shape[3]
    owned = images // tiles
    half_rows = height // 2
    chunks = 2
    part = outputs // chunks
    upper_row = shifted_2(maps[:, height - 1 : height], "tile", 1)
    grad = out_grad.reshape(owned, -1, outputs)
    conv = None
    pieces = []
    halves = first_stage(maps, upper_row, first_weight, part)
    for chunk in range(chunks):
        channels = slice(chunk * part, (chunk + 1) * part)
        local_hidden = halves[chunk]
        arrived = lax.all_to_all(
            local_hidden.reshape(tiles, owned, half_rows, width // 2, part),
            "tile",
            split_axis=0,
            concat_axis=2,
            tiled=True,
        )
        if conv is not None:
            arrived, conv = lax.optimization_barrier((arrived, conv))
        hidden = arrived.reshape(owned, half_rows * tiles, width // 2, part)
        last = chunk == chunks - 1
        conv, partial = second_stage(
            hidden, second_weight[:, :, channels], grad, conv, jnp.bfloat16 if last else jnp.float32
        )
        summed = halving_reduce_scatter(
            partial.sum(axis=0).reshape(outputs, 9 * part), ("group", "tile"), swap=chunk % 2 == 1
        )
        pieces.append(summed.reshape(-1, 9, part))
    weight_grad = jnp.concatenate(pieces, axis=-1).reshape(-1, 3, 3, outputs)
    return (conv, weight_grad)


def solution(mesh):
    return jax.shard_map(
        local,
        mesh=mesh,
        in_specs=(P("group", "tile", None, None), P(), P(), P(("group", "tile"), None, None, None)),
        out_specs=(P(("group", "tile"), None, None, None), P(("group", "tile"), None, None, None)),
        check_vma=False,
    )
```

```python
import functools

import jax
import jax.numpy as jnp
from jax import lax
from jax.experimental import pallas as pl
from jax.experimental.pallas import tpu as pltpu
from jax.sharding import PartitionSpec as P


def shifted_2(shard, axis, by):
    length = lax.axis_size(axis)
    pairs = [(i, i + by) for i in range(length) if 0 <= i + by < length]
    return lax.ppermute(shard, axis, pairs)


def shift_cols_right(slab):
    zero_col = jnp.zeros_like(slab[:, :, :1])
    return jnp.concatenate([zero_col, slab[:, :, :-1]], axis=2)


def shift_cols_left(slab):
    zero_col = jnp.zeros_like(slab[:, :, :1])
    return jnp.concatenate([slab[:, :, 1:], zero_col], axis=2)


def first_conv(source, upper_row, first_weight):
    images, rows, width, inputs = source.shape
    outputs = first_weight.shape[3]
    paired = source.reshape(images, rows // 2, 2, width // 2, 2 * inputs)
    even_rows = paired[:, :, 0]
    odd_rows = paired[:, :, 1]
    upper_paired = upper_row.reshape(images, 1, width // 2, 2 * inputs)
    odd_above = jnp.concatenate([upper_paired, odd_rows[:, :-1]], axis=1)
    sources = [odd_above, even_rows, odd_rows]
    total = jnp.zeros((images, rows // 2, width // 2, outputs), jnp.float32)
    for tap_row in range(3):
        wide_kernel = first_weight[tap_row, 1:3].reshape(2 * inputs, outputs)
        total = total + jnp.dot(sources[tap_row], wide_kernel, preferred_element_type=jnp.float32)
    halves = jnp.concatenate([piece[..., inputs:] for piece in sources], axis=-1)
    narrow_kernel = first_weight[:, 0].reshape(3 * inputs, outputs)
    total = total + jnp.dot(
        shift_cols_right(halves), narrow_kernel, preferred_element_type=jnp.float32
    )
    return jnp.maximum(total, 0.0).astype(jnp.bfloat16)


def first_kernel(x_ref, w_ref, low_ref, high_ref, scratch):
    images, rows, width, inputs = x_ref.shape
    out_rows, out_cols = rows // 2, width // 2
    scratch[:, 0] = jnp.zeros((images,) + scratch.shape[2:], jnp.float32)
    scratch[:, 1:] = x_ref[...].astype(jnp.float32)
    first_col = lax.broadcasted_iota(jnp.int32, (images, out_rows, out_cols, inputs), 2) == 0
    pieces = []
    for tap_row in range(3):
        even = scratch[:, pl.ds(tap_row, out_rows, stride=2), pl.ds(0, out_cols, stride=2), :]
        odd = scratch[:, pl.ds(tap_row, out_rows, stride=2), pl.ds(1, out_cols, stride=2), :]
        left = jnp.where(first_col, 0.0, pltpu.roll(odd, 1, 2))
        pieces += [left, even, odd]
    patches = jnp.concatenate(
        [p.astype(jnp.bfloat16).reshape(images * out_rows * out_cols, inputs) for p in pieces], axis=-1
    )
    total = jnp.dot(patches, w_ref[...], preferred_element_type=jnp.float32)
    hidden = jnp.maximum(total, 0.0).astype(jnp.bfloat16).reshape(images, out_rows, out_cols, -1)
    half = low_ref.shape[-1]
    low_ref[...] = hidden[..., :half]
    high_ref[...] = hidden[..., half:]


def first_row_kernel(x_ref, up_ref, w_ref, _low, _high, low_ref, high_ref, scratch):
    images, _, width, inputs = x_ref.shape
    out_cols = width // 2
    scratch[:, 0] = up_ref[:, 0].astype(jnp.float32)
    scratch[:, 1:] = x_ref[...].astype(jnp.float32)
    first_col = lax.broadcasted_iota(jnp.int32, (images, out_cols, inputs), 1) == 0
    pieces = []
    for tap_row in range(3):
        even = scratch[:, tap_row, pl.ds(0, out_cols, stride=2), :]
        odd = scratch[:, tap_row, pl.ds(1, out_cols, stride=2), :]
        left = jnp.where(first_col, 0.0, pltpu.roll(odd, 1, 1))
        pieces += [left, even, odd]
    patches = jnp.concatenate(
        [p.astype(jnp.bfloat16).reshape(images * out_cols, inputs) for p in pieces], axis=-1
    )
    total = jnp.dot(patches, w_ref[...], preferred_element_type=jnp.float32)
    hidden = jnp.maximum(total, 0.0).astype(jnp.bfloat16).reshape(images, 1, out_cols, -1)
    half = low_ref.shape[-1]
    low_ref[...] = hidden[..., :half]
    high_ref[...] = hidden[..., half:]


def first_stage(maps, upper_row, first_weight, part):
    images, rows, width, inputs = maps.shape
    outputs = first_weight.shape[3]
    weight = first_weight.reshape(9 * inputs, outputs)
    shape = jax.ShapeDtypeStruct((images, rows // 2, width // 2, part), jnp.bfloat16)
    params = pltpu.CompilerParams(dimension_semantics=("arbitrary",), vmem_limit_bytes=60 * 1024 * 1024)
    weight_spec = pl.BlockSpec((9 * inputs, outputs), lambda n: (0, 0))

    def cost(out_rows):
        return pl.CostEstimate(
            flops=2 * images * out_rows * (width // 2) * 9 * inputs * outputs,
            transcendentals=0,
            bytes_accessed=images * out_rows * 2 * width * inputs * 2 + images * out_rows * (width // 2) * outputs * 2,
        )

    per = 4 if images % 4 == 0 else 1
    out_block = pl.BlockSpec((per, rows // 2, width // 2, part), lambda n: (n, 0, 0, 0))
    low, high = pl.pallas_call(
        first_kernel,
        grid=(images // per,),
        in_specs=[pl.BlockSpec((per, rows, width, inputs), lambda n: (n, 0, 0, 0)), weight_spec],
        out_specs=[out_block, out_block],
        out_shape=[shape, shape],
        scratch_shapes=[pltpu.VMEM((per, rows + 1, width, inputs), jnp.float32)],
        compiler_params=params,
        cost_estimate=cost(rows // 2),
    )(maps, weight)
    row_block = pl.BlockSpec((images, 1, width // 2, part), lambda n: (0, 0, 0, 0))
    anywhere = pl.BlockSpec(memory_space=pl.ANY)
    return pl.pallas_call(
        first_row_kernel,
        grid=(1,),
        in_specs=[
            pl.BlockSpec((images, 2, width, inputs), lambda n: (0, 0, 0, 0)),
            pl.BlockSpec((images, 1, width, inputs), lambda n: (0, 0, 0, 0)),
            weight_spec,
            anywhere,
            anywhere,
        ],
        out_specs=[row_block, row_block],
        out_shape=[shape, shape],
        scratch_shapes=[pltpu.VMEM((images, 3, width, inputs), jnp.float32)],
        input_output_aliases={3: 0, 4: 1},
        compiler_params=params,
        cost_estimate=cost(1),
    )(maps, upper_row, weight, low, high)


def second_kernel(*refs, rows, carry):
    if carry:
        src_ref, weight_ref, grad_ref, prev_ref, out_ref, wgrad_ref, acc_ref = refs
    else:
        src_ref, weight_ref, grad_ref, out_ref, wgrad_ref, acc_ref = refs
    step = pl.program_id(1)
    _, width, outputs = out_ref.shape
    inputs = src_ref.shape[-1]
    patches = jnp.concatenate(
        [
            src_ref[tap % 3, pl.ds(step * rows + tap // 3, rows)].reshape(rows * width, inputs)
            for tap in range(9)
        ],
        axis=-1,
    )
    total = jnp.dot(patches, weight_ref[...], preferred_element_type=jnp.float32)
    if carry:
        total = total + prev_ref[...].reshape(rows * width, outputs)
    out_ref[...] = total.astype(out_ref.dtype).reshape(rows, width, outputs)
    term = lax.dot_general(
        patches, grad_ref[...], (((0,), (0,)), ((), ())), preferred_element_type=jnp.float32
    )

    @pl.when(step == 0)
    def _():
        acc_ref[...] = term

    @pl.when(step > 0)
    def _():
        acc_ref[...] += term

    @pl.when(step == pl.num_programs(1) - 1)
    def _():
        wgrad_ref[...] = acc_ref[...].T


def second_stage(hidden, weight, grad, prev, out_dtype):
    owned, out_rows, out_cols, inputs = hidden.shape
    outputs = weight.shape[-1]
    rows = min(64, out_rows)
    row_padded = jnp.pad(hidden, ((0, 0), (1, 1), (0, 0), (0, 0)))
    shifted = jnp.stack([shift_cols_right(row_padded), row_padded, shift_cols_left(row_padded)], axis=1)
    full = pl.BlockSpec((None, 3, out_rows + 2, out_cols, inputs), lambda n, i: (n, 0, 0, 0, 0))
    block = pl.BlockSpec((None, rows, out_cols, outputs), lambda n, i: (n, i, 0, 0))
    in_specs = [
        full,
        pl.BlockSpec((9 * inputs, outputs), lambda n, i: (0, 0)),
        pl.BlockSpec((None, rows * out_cols, outputs), lambda n, i: (n, i, 0)),
    ]
    operands = [shifted, weight.reshape(9 * inputs, outputs), grad]
    if prev is not None:
        in_specs.append(block)
        operands.append(prev)
    flops = 4 * owned * out_rows * out_cols * 9 * inputs * outputs
    return pl.pallas_call(
        functools.partial(second_kernel, rows=rows, carry=prev is not None),
        grid=(owned, out_rows // rows),
        in_specs=in_specs,
        out_specs=[block, pl.BlockSpec((None, outputs, 9 * inputs), lambda n, i: (n, 0, 0))],
        out_shape=[
            jax.ShapeDtypeStruct((owned, out_rows, out_cols, outputs), out_dtype),
            jax.ShapeDtypeStruct((owned, outputs, 9 * inputs), jnp.float32),
        ],
        scratch_shapes=[pltpu.VMEM((9 * inputs, outputs), jnp.float32)],
        compiler_params=pltpu.CompilerParams(
            dimension_semantics=("arbitrary", "arbitrary"), vmem_limit_bytes=60 * 1024 * 1024
        ),
        cost_estimate=pl.CostEstimate(
            flops=flops,
            transcendentals=0,
            bytes_accessed=hidden.size * 2 * 4 + owned * out_rows * out_cols * outputs * 8
            + owned * outputs * 9 * inputs * 4,
        ),
    )(*operands)


def halving_reduce_scatter(partial, axes, swap=False):
    devices = lax.axis_size(axes)
    tiles = lax.axis_size(axes[-1])
    bits = devices.bit_length() - 1
    me = lax.axis_index(axes)
    core = tiles.bit_length() - 1
    high = [b for b in range(bits) if b > core]
    low = [b for b in range(core)]
    order = [core] + (low[:1] + high + low[1:] if swap else high + low)
    rows = partial.shape[0] // devices
    buf = partial.reshape((2,) * bits + (rows,) + partial.shape[1:])
    remaining = list(range(bits - 1, -1, -1))
    for bit in order:
        axis = remaining.index(bit)
        mine = (me >> bit) & 1
        keep = lax.dynamic_index_in_dim(buf, mine, axis=axis, keepdims=False)
        send = lax.dynamic_index_in_dim(buf, 1 - mine, axis=axis, keepdims=False)
        pairs = [(i, i ^ (1 << bit)) for i in range(devices)]
        buf = keep + lax.ppermute(send, axes, pairs)
        remaining.pop(axis)
    return buf


def local(maps, first_weight, second_weight, out_grad):
    tiles = lax.axis_size("tile")
    images, height, width, inputs = maps.shape
    outputs = first_weight.shape[3]
    owned = images // tiles
    half_rows = height // 2
    chunks = 2
    part = outputs // chunks
    upper_row = shifted_2(maps[:, height - 1 : height], "tile", 1)
    grad = out_grad.reshape(owned, -1, outputs)
    conv = None
    pieces = []
    halves = first_stage(maps, upper_row, first_weight, part)
    for chunk in range(chunks):
        channels = slice(chunk * part, (chunk + 1) * part)
        local_hidden = halves[chunk]
        arrived = lax.all_to_all(
            local_hidden.reshape(tiles, owned, half_rows, width // 2, part),
            "tile",
            split_axis=0,
            concat_axis=2,
            tiled=True,
        )
        if conv is not None:
            arrived, conv = lax.optimization_barrier((arrived, conv))
        hidden = arrived.reshape(owned, half_rows * tiles, width // 2, part)
        last = chunk == chunks - 1
        conv, partial = second_stage(
            hidden, second_weight[:, :, channels], grad, conv, jnp.bfloat16 if last else jnp.float32
        )
        summed = halving_reduce_scatter(
            partial.sum(axis=0).reshape(outputs, 9 * part), ("group", "tile"), swap=chunk % 2 == 1
        )
        pieces.append(summed.reshape(-1, 9, part))
    weight_grad = jnp.concatenate(pieces, axis=-1).reshape(-1, 3, 3, outputs)
    return (conv, weight_grad)


def solution(mesh):
    return jax.shard_map(
        local,
        mesh=mesh,
        in_specs=(P("group", "tile", None, None), P(), P(), P(("group", "tile"), None, None, None)),
        out_specs=(P(("group", "tile"), None, None, None), P(("group", "tile"), None, None, None)),
        check_vma=False,
    )
```

```python
import functools

import jax
import jax.numpy as jnp
from jax import lax
from jax.experimental import pallas as pl
from jax.experimental.pallas import tpu as pltpu
from jax.sharding import PartitionSpec as P


def shifted_2(shard, axis, by):
    length = lax.axis_size(axis)
    pairs = [(i, i + by) for i in range(length) if 0 <= i + by < length]
    return lax.ppermute(shard, axis, pairs)


def shift_cols_right(slab):
    zero_col = jnp.zeros_like(slab[:, :, :1])
    return jnp.concatenate([zero_col, slab[:, :, :-1]], axis=2)


def shift_cols_left(slab):
    zero_col = jnp.zeros_like(slab[:, :, :1])
    return jnp.concatenate([slab[:, :, 1:], zero_col], axis=2)


def first_conv(source, upper_row, first_weight):
    images, rows, width, inputs = source.shape
    outputs = first_weight.shape[3]
    paired = source.reshape(images, rows // 2, 2, width // 2, 2 * inputs)
    even_rows = paired[:, :, 0]
    odd_rows = paired[:, :, 1]
    upper_paired = upper_row.reshape(images, 1, width // 2, 2 * inputs)
    odd_above = jnp.concatenate([upper_paired, odd_rows[:, :-1]], axis=1)
    sources = [odd_above, even_rows, odd_rows]
    total = jnp.zeros((images, rows // 2, width // 2, outputs), jnp.float32)
    for tap_row in range(3):
        wide_kernel = first_weight[tap_row, 1:3].reshape(2 * inputs, outputs)
        total = total + jnp.dot(sources[tap_row], wide_kernel, preferred_element_type=jnp.float32)
    halves = jnp.concatenate([piece[..., inputs:] for piece in sources], axis=-1)
    narrow_kernel = first_weight[:, 0].reshape(3 * inputs, outputs)
    total = total + jnp.dot(
        shift_cols_right(halves), narrow_kernel, preferred_element_type=jnp.float32
    )
    return jnp.maximum(total, 0.0).astype(jnp.bfloat16)


def first_kernel(x_ref, w_ref, low_ref, high_ref, scratch):
    images, rows, width, inputs = x_ref.shape
    out_rows, out_cols = rows // 2, width // 2
    scratch[:, 0] = jnp.zeros((images,) + scratch.shape[2:], jnp.float32)
    scratch[:, 1:] = x_ref[...].astype(jnp.float32)
    first_col = lax.broadcasted_iota(jnp.int32, (images, out_rows, out_cols, inputs), 2) == 0
    pieces = []
    for tap_row in range(3):
        even = scratch[:, pl.ds(tap_row, out_rows, stride=2), pl.ds(0, out_cols, stride=2), :]
        odd = scratch[:, pl.ds(tap_row, out_rows, stride=2), pl.ds(1, out_cols, stride=2), :]
        left = jnp.where(first_col, 0.0, pltpu.roll(odd, 1, 2))
        pieces += [left, even, odd]
    patches = jnp.concatenate(
        [p.astype(jnp.bfloat16).reshape(images * out_rows * out_cols, inputs) for p in pieces], axis=-1
    )
    total = jnp.dot(patches, w_ref[...], preferred_element_type=jnp.float32)
    hidden = jnp.maximum(total, 0.0).astype(jnp.bfloat16).reshape(images, out_rows, out_cols, -1)
    half = low_ref.shape[-1]
    low_ref[...] = hidden[..., :half]
    high_ref[...] = hidden[..., half:]


def first_row_kernel(x_ref, up_ref, w_ref, _low, _high, low_ref, high_ref, scratch):
    images, _, width, inputs = x_ref.shape
    out_cols = width // 2
    scratch[:, 0] = up_ref[:, 0].astype(jnp.float32)
    scratch[:, 1:] = x_ref[...].astype(jnp.float32)
    first_col = lax.broadcasted_iota(jnp.int32, (images, out_cols, inputs), 1) == 0
    pieces = []
    for tap_row in range(3):
        even = scratch[:, tap_row, pl.ds(0, out_cols, stride=2), :]
        odd = scratch[:, tap_row, pl.ds(1, out_cols, stride=2), :]
        left = jnp.where(first_col, 0.0, pltpu.roll(odd, 1, 1))
        pieces += [left, even, odd]
    patches = jnp.concatenate(
        [p.astype(jnp.bfloat16).reshape(images * out_cols, inputs) for p in pieces], axis=-1
    )
    total = jnp.dot(patches, w_ref[...], preferred_element_type=jnp.float32)
    hidden = jnp.maximum(total, 0.0).astype(jnp.bfloat16).reshape(images, 1, out_cols, -1)
    half = low_ref.shape[-1]
    low_ref[...] = hidden[..., :half]
    high_ref[...] = hidden[..., half:]


def first_stage(maps, upper_row, first_weight, part):
    images, rows, width, inputs = maps.shape
    outputs = first_weight.shape[3]
    weight = first_weight.reshape(9 * inputs, outputs)
    shape = jax.ShapeDtypeStruct((images, rows // 2, width // 2, part), jnp.bfloat16)
    params = pltpu.CompilerParams(dimension_semantics=("arbitrary",), vmem_limit_bytes=60 * 1024 * 1024)
    weight_spec = pl.BlockSpec((9 * inputs, outputs), lambda n: (0, 0))

    def cost(out_rows):
        return pl.CostEstimate(
            flops=2 * images * out_rows * (width // 2) * 9 * inputs * outputs,
            transcendentals=0,
            bytes_accessed=images * out_rows * 2 * width * inputs * 2 + images * out_rows * (width // 2) * outputs * 2,
        )

    per = 4 if images % 4 == 0 else 1
    out_block = pl.BlockSpec((per, rows // 2, width // 2, part), lambda n: (n, 0, 0, 0))
    low, high = pl.pallas_call(
        first_kernel,
        grid=(images // per,),
        in_specs=[pl.BlockSpec((per, rows, width, inputs), lambda n: (n, 0, 0, 0)), weight_spec],
        out_specs=[out_block, out_block],
        out_shape=[shape, shape],
        scratch_shapes=[pltpu.VMEM((per, rows + 1, width, inputs), jnp.float32)],
        compiler_params=params,
        cost_estimate=cost(rows // 2),
    )(maps, weight)
    row_block = pl.BlockSpec((images, 1, width // 2, part), lambda n: (0, 0, 0, 0))
    anywhere = pl.BlockSpec(memory_space=pl.ANY)
    return pl.pallas_call(
        first_row_kernel,
        grid=(1,),
        in_specs=[
            pl.BlockSpec((images, 2, width, inputs), lambda n: (0, 0, 0, 0)),
            pl.BlockSpec((images, 1, width, inputs), lambda n: (0, 0, 0, 0)),
            weight_spec,
            anywhere,
            anywhere,
        ],
        out_specs=[row_block, row_block],
        out_shape=[shape, shape],
        scratch_shapes=[pltpu.VMEM((images, 3, width, inputs), jnp.float32)],
        input_output_aliases={3: 0, 4: 1},
        compiler_params=params,
        cost_estimate=cost(1),
    )(maps, upper_row, weight, low, high)


def second_kernel(*refs, rows, carry):
    if carry:
        src_ref, weight_ref, grad_ref, prev_ref, out_ref, wgrad_ref, acc_ref = refs
    else:
        src_ref, weight_ref, grad_ref, out_ref, wgrad_ref, acc_ref = refs
    step = pl.program_id(1)
    _, width, outputs = out_ref.shape
    inputs = src_ref.shape[-1]
    patches = jnp.concatenate(
        [
            src_ref[tap % 3, pl.ds(step * rows + tap // 3, rows)].reshape(rows * width, inputs)
            for tap in range(9)
        ],
        axis=-1,
    )
    total = jnp.dot(patches, weight_ref[...], preferred_element_type=jnp.float32)
    if carry:
        total = total + prev_ref[...].reshape(rows * width, outputs)
    out_ref[...] = total.astype(out_ref.dtype).reshape(rows, width, outputs)
    term = lax.dot_general(
        patches, grad_ref[...], (((0,), (0,)), ((), ())), preferred_element_type=jnp.float32
    )

    @pl.when(step == 0)
    def _():
        acc_ref[...] = term

    @pl.when(step > 0)
    def _():
        acc_ref[...] += term

    @pl.when(step == pl.num_programs(1) - 1)
    def _():
        wgrad_ref[...] = acc_ref[...].T


def second_stage(hidden, weight, grad, prev, out_dtype):
    owned, out_rows, out_cols, inputs = hidden.shape
    outputs = weight.shape[-1]
    rows = min(32, out_rows)
    row_padded = jnp.pad(hidden, ((0, 0), (1, 1), (0, 0), (0, 0)))
    zero = jnp.zeros((), hidden.dtype)
    none = (0, 0, 0)
    right = lax.pad(row_padded, zero, [none, none, (1, -1, 0), none])
    left = lax.pad(row_padded, zero, [none, none, (-1, 1, 0), none])
    shifted = jnp.stack([right, row_padded, left], axis=1)
    full = pl.BlockSpec((None, 3, out_rows + 2, out_cols, inputs), lambda n, i: (n, 0, 0, 0, 0))
    block = pl.BlockSpec((None, rows, out_cols, outputs), lambda n, i: (n, i, 0, 0))
    in_specs = [
        full,
        pl.BlockSpec((9 * inputs, outputs), lambda n, i: (0, 0)),
        pl.BlockSpec((None, rows * out_cols, outputs), lambda n, i: (n, i, 0)),
    ]
    operands = [shifted, weight.reshape(9 * inputs, outputs), grad]
    if prev is not None:
        in_specs.append(block)
        operands.append(prev)
    flops = 4 * owned * out_rows * out_cols * 9 * inputs * outputs
    return pl.pallas_call(
        functools.partial(second_kernel, rows=rows, carry=prev is not None),
        grid=(owned, out_rows // rows),
        in_specs=in_specs,
        out_specs=[block, pl.BlockSpec((None, outputs, 9 * inputs), lambda n, i: (n, 0, 0))],
        out_shape=[
            jax.ShapeDtypeStruct((owned, out_rows, out_cols, outputs), out_dtype),
            jax.ShapeDtypeStruct((owned, outputs, 9 * inputs), jnp.float32),
        ],
        scratch_shapes=[pltpu.VMEM((9 * inputs, outputs), jnp.float32)],
        compiler_params=pltpu.CompilerParams(
            dimension_semantics=("arbitrary", "arbitrary"), vmem_limit_bytes=60 * 1024 * 1024
        ),
        cost_estimate=pl.CostEstimate(
            flops=flops,
            transcendentals=0,
            bytes_accessed=hidden.size * 2 * 4 + owned * out_rows * out_cols * outputs * 8
            + owned * outputs * 9 * inputs * 4,
        ),
    )(*operands)


def halving_reduce_scatter(partial, axes, swap=False):
    devices = lax.axis_size(axes)
    tiles = lax.axis_size(axes[-1])
    bits = devices.bit_length() - 1
    me = lax.axis_index(axes)
    core = tiles.bit_length() - 1
    high = [b for b in range(bits) if b > core]
    low = [b for b in range(core)]
    order = [core] + (low[:1] + high + low[1:] if swap else high + low)
    rows = partial.shape[0] // devices
    buf = partial.reshape((2,) * bits + (rows,) + partial.shape[1:])
    remaining = list(range(bits - 1, -1, -1))
    for bit in order:
        axis = remaining.index(bit)
        mine = (me >> bit) & 1
        keep = lax.dynamic_index_in_dim(buf, mine, axis=axis, keepdims=False)
        send = lax.dynamic_index_in_dim(buf, 1 - mine, axis=axis, keepdims=False)
        pairs = [(i, i ^ (1 << bit)) for i in range(devices)]
        buf = keep + lax.ppermute(send, axes, pairs)
        remaining.pop(axis)
    return buf


def local(maps, first_weight, second_weight, out_grad):
    tiles = lax.axis_size("tile")
    images, height, width, inputs = maps.shape
    outputs = first_weight.shape[3]
    owned = images // tiles
    half_rows = height // 2
    chunks = 2
    part = outputs // chunks
    upper_row = shifted_2(maps[:, height - 1 : height], "tile", 1)
    grad = out_grad.reshape(owned, -1, outputs)
    conv = None
    pieces = []
    halves = first_stage(maps, upper_row, first_weight, part)
    for chunk in range(chunks):
        channels = slice(chunk * part, (chunk + 1) * part)
        local_hidden = halves[chunk]
        arrived = lax.all_to_all(
            local_hidden.reshape(tiles, owned, half_rows, width // 2, part),
            "tile",
            split_axis=0,
            concat_axis=2,
            tiled=True,
        )
        if conv is not None:
            arrived, conv = lax.optimization_barrier((arrived, conv))
        hidden = arrived.reshape(owned, half_rows * tiles, width // 2, part)
        last = chunk == chunks - 1
        conv, partial = second_stage(
            hidden, second_weight[:, :, channels], grad, conv, jnp.bfloat16 if last else jnp.float32
        )
        summed = halving_reduce_scatter(
            partial.sum(axis=0).reshape(outputs, 9 * part), ("group", "tile"), swap=chunk % 2 == 1
        )
        pieces.append(summed.reshape(-1, 9, part))
    weight_grad = jnp.concatenate(pieces, axis=-1).reshape(-1, 3, 3, outputs)
    return (conv, weight_grad)


def solution(mesh):
    return jax.shard_map(
        local,
        mesh=mesh,
        in_specs=(P("group", "tile", None, None), P(), P(), P(("group", "tile"), None, None, None)),
        out_specs=(P(("group", "tile"), None, None, None), P(("group", "tile"), None, None, None)),
        check_vma=False,
    )
```
